512 devices in a mesh: rcv: 64 (over x, z_lo, y), src: 8 (over z_hi, core).
Axes of the slice: x: 4, y: 4, z: 16 (z_hi: 4, z_lo: 4; z = z_hi * 4 + z_lo), core: 2. Of those that a mesh axis runs over, the one named last changes fastest.
Arguments:
- records: float32 [16384, 4096], P(('rcv', 'src')), may hold values from -6 to 6
- window_start: int32 [512], P(('rcv', 'src')), may hold values from 0 to 160
- channel_segment: int32 [16384], replicated, may hold values from 0 to 255, as said below
- segment_row: int32 [256], replicated, may hold values from 0 to 255, as said below
Outputs:
- stacks: float32 [256, 64, 256], P('rcv', 'src')
The draws below stay inside these ranges and needn't reach their ends.
Inputs may be any that keep to these rules, and one draw needn't show every extreme that they name: `window_start`: window positions index the group's 256 channels with the tile's own 32 channels left out. A permutation: segment s is stacked into row segment_row[s], held by rcv index segment_row[s] // 4. `channel_segment`: the 32 channels of each tile (aligned blocks) lie in segments of exactly 16 rcv indices, exactly 2 channels for each; one rcv index receives 2 channels from every tile.
All inputs are finite; a program needn't handle non-finite values.
Results may differ from the reference program's by a relative error of at most 0.0058.
Values may be sent and summed in bfloat16 or wider, within the bound.
No kernel may reach another device: no remote copies, remote signals or barrier semaphores. Data moves between devices by JAX's collectives and lax.ppermute only.
A program may use at most 64 MiB of HBM per device.

```python
import math
import jax
import jax.numpy as jnp
from jax import lax

NFFT = 1024
LAGS = 256
NBLK = 4
CH_DEV = 32
CAP = 2
SEG_PER = 4
GRP = 256
NWIN = 64
TILES = 512
CHANNELS = 16384
NSEG = 256
SAMPLES = 4096
N_RCV = 64
N_SRC = 8


def routing_draw(key):
    base_key = jax.random.fold_in(key, 7)
    perm_key, bias_key, favored_key, noise_key, order_key, slot_key = jax.random.split(base_key, 6)
    segment_row = jax.random.permutation(perm_key, NSEG).astype(jnp.int32)
    row_segment = jnp.argsort(segment_row).astype(jnp.int32)
    owner_ids = jnp.arange(N_RCV, dtype=jnp.int32)
    biases = jax.random.randint(bias_key, (N_RCV,), 0, 98304)
    favored = jax.random.randint(favored_key, (), 0, N_RCV)
    biases = jnp.where(owner_ids == favored, 262144, biases)
    noises = jax.random.randint(noise_key, (TILES, N_RCV), 0, 65536)
    scores = (noises + biases[None, :]) * N_RCV + owner_ids[None, :]
    chosen = lax.top_k(scores, CH_DEV // CAP)[1].astype(jnp.int32)
    owners = jnp.repeat(chosen, CAP, axis=1)
    order_scores = jax.random.randint(order_key, (TILES, CH_DEV), 0, 1048576) * CH_DEV + jnp.arange(CH_DEV, dtype=jnp.int32)[None, :]
    owners = jnp.take_along_axis(owners, jnp.argsort(order_scores, axis=1), axis=1)
    slots = jax.random.randint(slot_key, (TILES, CH_DEV), 0, SEG_PER)
    channel_segment = row_segment[(owners * SEG_PER + slots).reshape(-1)]
    return (segment_row, channel_segment.astype(jnp.int32))


def draw_channel_segment(key, part):
    return routing_draw(key)[1]


def draw_segment_row(key, part):
    return routing_draw(key)[0]


def with_ends(entries, key, low, top_value):
    longest = entries.shape.index(max(entries.shape))
    spots = []
    for shift in (0, 1):
        where = [jax.random.randint(jax.random.fold_in(key, axis), (), 0, length) for axis, length in enumerate(entries.shape)]
        where[longest] = (where[longest] + shift) % entries.shape[longest]
        spots.append(tuple(where))
    return entries.at[spots[0]].set(low).at[spots[1]].set(top_value)


def block_levels(key, dims, cuts, low, high):
    factor_of, own = 1.0, jax.random.fold_in(key, 6)
    for dim, shards_of in cuts:
        heights = jnp.exp(jax.random.uniform(jax.random.fold_in(own, dim), (shards_of,), jnp.float32, low / len(cuts), high / len(cuts)))
        factor_of = factor_of * jnp.repeat(heights, dims[dim] // shards_of).reshape([-1 if axis == dim else 1 for axis in range(len(dims))])
    return factor_of


def bell_draw(own_key, extent, spread, limit, cuts=(), kind=jnp.bfloat16):
    array = jax.random.normal(own_key, extent, jnp.float32) * spread
    if len(cuts) > 0:
        array = block_levels(own_key, extent, cuts, -0.22, 0.18) * array
    return jnp.clip(array, min=-limit, max=limit).astype(kind)


def setup_inputs(seed: int = 0) -> dict:
    key_list = jax.random.split(jax.random.key(seed), 5)
    return {
        "records": bell_draw(key_list[0], (CHANNELS, SAMPLES), 1.0, 6.0, ((0, 512),), jnp.float32),
        "window_start": with_ends(jax.random.randint(key_list[1], (TILES,), 0, GRP - CH_DEV - NWIN + 1), jax.random.fold_in(key_list[1], 1), 0, GRP - CH_DEV - NWIN).astype(jnp.int32),
        "channel_segment": draw_channel_segment(jax.random.fold_in(key_list[4], 71), 0),
        "segment_row": draw_segment_row(jax.random.fold_in(key_list[4], 71), 0),
    }


def dft_table(length):
    sample_index = jnp.arange(length, dtype=jnp.int32)
    frequency = jnp.arange(length // 2, dtype=jnp.int32)
    angles = (sample_index[:, None] * frequency[None, :] % length).astype(jnp.float32) * (2.0 * math.pi / length)
    return jnp.concatenate([jnp.cos(angles), -jnp.sin(angles)], axis=1)

def lag_table(length, lag_count):
    frequency = jnp.arange(length // 2, dtype=jnp.int32)
    shifts = jnp.arange(lag_count, dtype=jnp.int32) - lag_count // 2
    angles = (frequency[:, None] * shifts[None, :] % length).astype(jnp.float32) * (2.0 * math.pi / length)
    return jnp.concatenate([jnp.cos(angles), -jnp.sin(angles)], axis=0).astype(jnp.bfloat16)

def whiten(spectrum):
    half_size = spectrum.shape[-1] // 2
    powers = spectrum[..., :half_size] ** 2 + spectrum[..., half_size:] ** 2
    mean_power = lax.optimization_barrier(jnp.mean(powers, axis=-1, keepdims=True))
    magnitude = jnp.sqrt(powers + 0.1 * mean_power + 1e-06)
    return spectrum / jnp.concatenate([magnitude, magnitude], axis=-1)

def correlate(own_tile, sources, lag_rows, block_count):
    half_size = own_tile.shape[-1] // 2
    left_part = own_tile.astype(jnp.float32)
    right_part = sources.astype(jnp.float32)
    left_re, left_im = (left_part[..., :half_size], left_part[..., half_size:])
    right_re, right_im = (right_part[..., :half_size], right_part[..., half_size:])
    real_part = jnp.einsum('ibf,jbf->ijf', left_re, right_re) + jnp.einsum('ibf,jbf->ijf', left_im, right_im)
    imag_part = jnp.einsum('ibf,jbf->ijf', left_re, right_im) - jnp.einsum('ibf,jbf->ijf', left_im, right_re)
    cross_spec = jnp.concatenate([real_part, imag_part], axis=-1).astype(jnp.bfloat16)
    flat_rows = cross_spec.reshape(-1, cross_spec.shape[-1])
    correlation = jnp.dot(flat_rows, lag_rows, preferred_element_type=jnp.float32) / math.sqrt(block_count * half_size)
    return correlation.astype(jnp.bfloat16).reshape(own_tile.shape[0], sources.shape[0], lag_rows.shape[1])

def reference(records, window_start, channel_segment, segment_row):
    blocks = records.reshape(CHANNELS * NBLK, NFFT)
    spectrum = jnp.dot(blocks, dft_table(NFFT), precision=lax.Precision.HIGHEST, preferred_element_type=jnp.float32)
    white = whiten(spectrum).astype(jnp.bfloat16).reshape(CHANNELS, NBLK, NFFT)
    lag_rows = lag_table(NFFT, LAGS)
    stack_rows = segment_row[channel_segment]

    def tile_step(stacks, tile_index):
        group_first = tile_index // N_SRC * GRP
        position = tile_index % N_SRC
        own_tile = lax.dynamic_slice_in_dim(white, tile_index * CH_DEV, CH_DEV)
        window_idx = window_start[tile_index] + jnp.arange(NWIN, dtype=jnp.int32)
        source_idx = jnp.where(window_idx < position * CH_DEV, window_idx, window_idx + CH_DEV) + group_first
        sources = jnp.take(white, source_idx, axis=0)
        correlation = correlate(own_tile, sources, lag_rows, NBLK).astype(jnp.float32)
        tile_rows = lax.dynamic_slice_in_dim(stack_rows, tile_index * CH_DEV, CH_DEV)
        return (stacks.at[tile_rows].add(correlation), None)
    stacks = lax.scan(tile_step, jnp.zeros((NSEG, NWIN, LAGS), jnp.float32), jnp.arange(TILES, dtype=jnp.int32))[0]
    counts = jnp.zeros((NSEG,), jnp.float32).at[stack_rows].add(1.0)
    return stacks / jnp.sqrt(jnp.maximum(counts, 1.0))[:, None, None]
```

```python
import math

import jax
import jax.numpy as jnp
from jax import lax
from jax.sharding import PartitionSpec as P

NFFT = 1024
LAGS = 256
SEG_PER = 4


def dft_table(length):
    sample_index = jnp.arange(length, dtype=jnp.int32)
    frequency = jnp.arange(length // 2, dtype=jnp.int32)
    angles = (sample_index[:, None] * frequency[None, :] % length).astype(jnp.float32) * (
        2.0 * math.pi / length
    )
    return jnp.concatenate([jnp.cos(angles), -jnp.sin(angles)], axis=1)


def lag_table(length, lag_count):
    frequency = jnp.arange(length // 2, dtype=jnp.int32)
    shifts = jnp.arange(lag_count, dtype=jnp.int32) - lag_count // 2
    angles = (frequency[:, None] * shifts[None, :] % length).astype(jnp.float32) * (
        2.0 * math.pi / length
    )
    return jnp.concatenate([jnp.cos(angles), -jnp.sin(angles)], axis=0).astype(jnp.bfloat16)


def whiten(spectrum):
    half_size = spectrum.shape[-1] // 2
    powers = spectrum[..., :half_size] ** 2 + spectrum[..., half_size:] ** 2
    mean_power = jnp.mean(powers, axis=-1, keepdims=True)
    magnitude = jnp.sqrt(powers + 0.1 * mean_power + 1e-06)
    return spectrum / jnp.concatenate([magnitude, magnitude], axis=-1)


def cross_spectra(left, sources):
    half_size = left.shape[-1] // 2
    lf = left.astype(jnp.float32)[:, :, None]
    sf = sources.astype(jnp.float32)[:, None]
    l_re, l_im = lf[..., :half_size], lf[..., half_size:]
    s_re, s_im = sf[..., :half_size], sf[..., half_size:]
    real_part = jnp.sum(l_re * s_re + l_im * s_im, axis=3)
    imag_part = jnp.sum(l_re * s_im - l_im * s_re, axis=3)
    return jnp.concatenate([real_part, imag_part], axis=-1).astype(jnp.bfloat16)


def row_counts(channel_segment, segment_row, owner):
    held_rows = owner * SEG_PER + jnp.arange(SEG_PER, dtype=jnp.int32)
    matches = segment_row[None, :] == held_rows[:, None]
    segment_ids = jnp.arange(segment_row.shape[0], dtype=jnp.int32)
    held_segments = jnp.sum(jnp.where(matches, segment_ids[None, :], 0), axis=1)
    members = channel_segment[None, :] == held_segments[:, None]
    return jnp.sum(members.astype(jnp.float32), axis=1)


def on_device(records, window_start, channel_segment, segment_row):
    tile_size = records.shape[0]
    block_count = records.shape[1] // NFFT
    src_count = lax.axis_size("src")
    group_index = lax.axis_index("rcv")
    position = lax.axis_index("src")
    segment_total = segment_row.shape[0]

    blocks = records.reshape(tile_size * block_count, NFFT)
    spectrum = jnp.dot(
        blocks, dft_table(NFFT), precision=lax.Precision.HIGHEST, preferred_element_type=jnp.float32
    )
    white = whiten(spectrum).astype(jnp.bfloat16).reshape(tile_size, block_count, NFFT)
    group = lax.all_gather(white, "src", axis=0, tiled=True)
    starts = lax.all_gather(window_start, "src", axis=0, tiled=True)
    group_size = group.shape[0]
    window_total = group_size // 4
    k_per = window_total // src_count

    k_idx = position * k_per + jnp.arange(k_per, dtype=jnp.int32)
    window_idx = starts[:, None] + k_idx[None, :]
    tile_first = (jnp.arange(src_count, dtype=jnp.int32) * tile_size)[:, None]
    source_idx = jnp.where(window_idx < tile_first, window_idx, window_idx + tile_size)
    sources = jnp.take(group, source_idx.reshape(-1), axis=0).reshape(
        src_count, k_per, block_count, NFFT
    )
    left = group.reshape(src_count, tile_size, block_count, NFFT)
    cross = cross_spectra(left, sources)
    flat_rows = cross.reshape(group_size * k_per, NFFT)
    correlation = jnp.dot(
        flat_rows, lag_table(NFFT, LAGS), preferred_element_type=jnp.float32
    ) / math.sqrt(block_count * NFFT // 2)
    correlation = correlation.astype(jnp.bfloat16).reshape(group_size, k_per * LAGS)

    group_segments = lax.dynamic_slice_in_dim(channel_segment, group_index * group_size, group_size)
    seg_match = group_segments[:, None] == jnp.arange(segment_total, dtype=jnp.int32)[None, :]
    group_rows = jnp.sum(jnp.where(seg_match, segment_row[None, :], 0), axis=1)
    onehot = (
        jnp.arange(segment_total, dtype=jnp.int32)[:, None] == group_rows[None, :]
    ).astype(jnp.bfloat16)
    partial = jnp.dot(onehot, correlation, preferred_element_type=jnp.float32).reshape(
        segment_total, k_per, LAGS
    )
    summed = lax.psum_scatter(partial, "rcv", scatter_dimension=0, tiled=True)
    counts = row_counts(channel_segment, segment_row, group_index)
    return summed / jnp.sqrt(jnp.maximum(counts, 1.0))[:, None, None]


def solution(mesh):
    in_specs = (P(("rcv", "src"), None), P(("rcv", "src")), P(), P())
    out_specs = P("rcv", "src", None)
    return jax.shard_map(
        on_device, mesh=mesh, in_specs=in_specs, out_specs=out_specs, check_vma=False
    )
```

```python
import math

import jax
import jax.numpy as jnp
from jax import lax
from jax.sharding import Mesh, PartitionSpec as P

NFFT = 1024
LAGS = 256
SEG_PER = 4


def dft_table(length):
    sample_index = jnp.arange(length, dtype=jnp.int32)
    frequency = jnp.arange(length // 2, dtype=jnp.int32)
    angles = (sample_index[:, None] * frequency[None, :] % length).astype(jnp.float32) * (
        2.0 * math.pi / length
    )
    return jnp.concatenate([jnp.cos(angles), -jnp.sin(angles)], axis=1)


def lag_table(length, lag_count):
    frequency = jnp.arange(length // 2, dtype=jnp.int32)
    shifts = jnp.arange(lag_count, dtype=jnp.int32) - lag_count // 2
    angles = (frequency[:, None] * shifts[None, :] % length).astype(jnp.float32) * (
        2.0 * math.pi / length
    )
    return jnp.concatenate([jnp.cos(angles), -jnp.sin(angles)], axis=0).astype(jnp.bfloat16)


def whiten(spectrum):
    half_size = spectrum.shape[-1] // 2
    powers = spectrum[..., :half_size] ** 2 + spectrum[..., half_size:] ** 2
    mean_power = jnp.mean(powers, axis=-1, keepdims=True)
    magnitude = jnp.sqrt(powers + 0.1 * mean_power + 1e-06)
    return spectrum / jnp.concatenate([magnitude, magnitude], axis=-1)


def cross_spectra(left, sources):
    half_size = left.shape[-1] // 2
    lf = left.astype(jnp.float32)[:, :, None]
    sf = sources.astype(jnp.float32)[:, None]
    l_re, l_im = lf[..., :half_size], lf[..., half_size:]
    s_re, s_im = sf[..., :half_size], sf[..., half_size:]
    real_part = jnp.sum(l_re * s_re + l_im * s_im, axis=3)
    imag_part = jnp.sum(l_re * s_im - l_im * s_re, axis=3)
    return jnp.concatenate([real_part, imag_part], axis=-1).astype(jnp.bfloat16)


def row_counts(channel_segment, segment_row, owner):
    held_rows = owner * SEG_PER + jnp.arange(SEG_PER, dtype=jnp.int32)
    matches = segment_row[None, :] == held_rows[:, None]
    segment_ids = jnp.arange(segment_row.shape[0], dtype=jnp.int32)
    held_segments = jnp.sum(jnp.where(matches, segment_ids[None, :], 0), axis=1)
    members = channel_segment[None, :] == held_segments[:, None]
    return jnp.sum(members.astype(jnp.float32), axis=1)


def on_device(records, window_start, channel_segment, segment_row):
    tile_size = records.shape[0]
    block_count = records.shape[1] // NFFT
    sizes = {name: lax.axis_size(name) for name in ("x", "zl", "y", "zh", "core")}
    src_count = sizes["zh"] * sizes["core"]
    x_i, zl_i, y_i = lax.axis_index("x"), lax.axis_index("zl"), lax.axis_index("y")
    zh_i, core_i = lax.axis_index("zh"), lax.axis_index("core")
    group_index = (x_i * sizes["zl"] + zl_i) * sizes["y"] + y_i
    position = zh_i * sizes["core"] + core_i
    segment_total = segment_row.shape[0]

    blocks = records.reshape(tile_size * block_count, NFFT)
    spectrum = jnp.dot(
        blocks, dft_table(NFFT), precision=lax.Precision.HIGHEST, preferred_element_type=jnp.float32
    )
    white = whiten(spectrum).astype(jnp.bfloat16).reshape(tile_size, block_count, NFFT)
    start_row = jnp.zeros((1, block_count, NFFT), jnp.bfloat16).at[0, 0, 0].set(
        window_start[0].astype(jnp.bfloat16)
    )
    extended = jnp.concatenate([white, start_row], axis=0)
    gathered = lax.all_gather(extended, "zh", axis=0)
    gathered = lax.all_gather(gathered, "core", axis=0)
    gathered = gathered.reshape(src_count, tile_size + 1, block_count, NFFT)
    left = gathered[:, :tile_size]
    starts = gathered[:, tile_size, 0, 0].astype(jnp.int32)
    group_size = src_count * tile_size
    window_total = group_size // 4
    k_per = window_total // src_count

    slot = jnp.arange(src_count, dtype=jnp.int32)
    slot_position = (slot % sizes["zh"]) * sizes["core"] + slot // sizes["zh"]
    k_idx = position * k_per + jnp.arange(k_per, dtype=jnp.int32)
    window_idx = starts[:, None] + k_idx[None, :]
    tile_first = (slot_position * tile_size)[:, None]
    source_idx = jnp.where(window_idx < tile_first, window_idx, window_idx + tile_size)
    source_pos = source_idx // tile_size
    source_slot = (source_pos % sizes["core"]) * sizes["zh"] + source_pos // sizes["core"]
    source_row = source_slot * (tile_size + 1) + source_idx % tile_size
    sources = jnp.take(
        gathered.reshape(src_count * (tile_size + 1), block_count, NFFT),
        source_row.reshape(-1),
        axis=0,
    ).reshape(src_count, k_per, block_count, NFFT)
    cross = cross_spectra(left, sources)
    flat_rows = cross.reshape(group_size * k_per, NFFT)
    correlation = jnp.dot(
        flat_rows, lag_table(NFFT, LAGS), preferred_element_type=jnp.float32
    ) / math.sqrt(block_count * NFFT // 2)
    correlation = correlation.astype(jnp.bfloat16).reshape(group_size, k_per * LAGS)

    channel_ids = (slot_position[:, None] * tile_size + jnp.arange(tile_size, dtype=jnp.int32)[None, :]).reshape(-1)
    group_segments = jnp.take(channel_segment, group_index * group_size + channel_ids)
    seg_match = group_segments[:, None] == jnp.arange(segment_total, dtype=jnp.int32)[None, :]
    group_rows = jnp.sum(jnp.where(seg_match, segment_row[None, :], 0), axis=1)
    owner = group_rows // SEG_PER
    owner_x = owner // (sizes["zl"] * sizes["y"])
    owner_zl = (owner // sizes["y"]) % sizes["zl"]
    owner_y = owner % sizes["y"]
    staged_rows = (
        (owner_y * sizes["x"] + owner_x) * sizes["zl"] + owner_zl
    ) * SEG_PER + group_rows % SEG_PER
    onehot = (
        jnp.arange(segment_total, dtype=jnp.int32)[:, None] == staged_rows[None, :]
    ).astype(jnp.bfloat16)
    partial = jnp.dot(onehot, correlation, preferred_element_type=jnp.float32).reshape(
        segment_total, k_per, LAGS
    )
    partial = lax.psum_scatter(partial, "y", scatter_dimension=0, tiled=True)
    partial = lax.psum_scatter(partial, "x", scatter_dimension=0, tiled=True)
    summed = lax.psum_scatter(partial, "zl", scatter_dimension=0, tiled=True)
    counts = row_counts(channel_segment, segment_row, group_index)
    return summed / jnp.sqrt(jnp.maximum(counts, 1.0))[:, None, None]


def solution(mesh):
    names = ("x", "zl", "y", "zh", "core")
    rcv_count, src_count = mesh.devices.shape
    zh_count = src_count // 2
    side = round(rcv_count ** (1 / 3))
    fine = Mesh(mesh.devices.reshape(side, side, rcv_count // side // side, zh_count, 2), names)
    rcv, src = ("x", "zl", "y"), ("zh", "core")
    in_specs = (P(rcv + src, None), P(rcv + src), P(), P())
    out_specs = P(rcv, src, None)
    return jax.shard_map(
        on_device, mesh=fine, in_specs=in_specs, out_specs=out_specs, check_vma=False
    )
```

```python
import math

import jax
import jax.numpy as jnp
from jax import lax
from jax.sharding import Mesh, PartitionSpec as P

NFFT = 1024
LAGS = 256
SEG_PER = 4


def dft_table(length):
    sample_index = jnp.arange(length, dtype=jnp.int32)
    frequency = jnp.arange(length // 2, dtype=jnp.int32)
    angles = (sample_index[:, None] * frequency[None, :] % length).astype(jnp.float32) * (
        2.0 * math.pi / length
    )
    return jnp.concatenate([jnp.cos(angles), -jnp.sin(angles)], axis=1)


def lag_table(length, lag_count):
    frequency = jnp.arange(length // 2, dtype=jnp.int32)
    shifts = jnp.arange(lag_count, dtype=jnp.int32) - lag_count // 2
    angles = (frequency[:, None] * shifts[None, :] % length).astype(jnp.float32) * (
        2.0 * math.pi / length
    )
    return jnp.concatenate([jnp.cos(angles), -jnp.sin(angles)], axis=0).astype(jnp.bfloat16)


def whiten(spectrum):
    half_size = spectrum.shape[-1] // 2
    powers = spectrum[..., :half_size] ** 2 + spectrum[..., half_size:] ** 2
    mean_power = jnp.mean(powers, axis=-1, keepdims=True)
    magnitude = jnp.sqrt(powers + 0.1 * mean_power + 1e-06)
    return spectrum / jnp.concatenate([magnitude, magnitude], axis=-1)


def cross_spectra(left, sources):
    half_size = left.shape[-1] // 2
    lf = left.astype(jnp.float32)[:, :, None]
    sf = sources.astype(jnp.float32)[:, None]
    l_re, l_im = lf[..., :half_size], lf[..., half_size:]
    s_re, s_im = sf[..., :half_size], sf[..., half_size:]
    real_part = jnp.sum(l_re * s_re + l_im * s_im, axis=3)
    imag_part = jnp.sum(l_re * s_im - l_im * s_re, axis=3)
    return jnp.concatenate([real_part, imag_part], axis=-1).astype(jnp.bfloat16)


def row_counts(channel_segment, segment_row, owner):
    held_rows = owner * SEG_PER + jnp.arange(SEG_PER, dtype=jnp.int32)
    matches = segment_row[None, :] == held_rows[:, None]
    segment_ids = jnp.arange(segment_row.shape[0], dtype=jnp.int32)
    held_segments = jnp.sum(jnp.where(matches, segment_ids[None, :], 0), axis=1)
    members = channel_segment[None, :] == held_segments[:, None]
    return jnp.sum(members.astype(jnp.float32), axis=1)


def shift_perm(count, shift):
    return [(i, (i + shift) % count) for i in range(count)]


def gather_relative(value, axis, count):
    parts = [value] + [lax.ppermute(value, axis, shift_perm(count, s)) for s in range(1, count)]
    return jnp.stack(parts)


def scatter_sum(value, axis, count):
    me = lax.axis_index(axis)
    blocks = value.reshape((count, value.shape[0] // count) + value.shape[1:])
    total = lax.dynamic_index_in_dim(blocks, me, axis=0, keepdims=False)
    for s in range(1, count):
        piece = lax.dynamic_index_in_dim(blocks, (me + s) % count, axis=0, keepdims=False)
        total = total + lax.ppermute(piece, axis, shift_perm(count, s))
    return total


def on_device(records, window_start, channel_segment, segment_row):
    tile_size = records.shape[0]
    block_count = records.shape[1] // NFFT
    sizes = {name: lax.axis_size(name) for name in ("x", "zl", "y", "zh", "core")}
    src_count = sizes["zh"] * sizes["core"]
    x_i, zl_i, y_i = lax.axis_index("x"), lax.axis_index("zl"), lax.axis_index("y")
    zh_i, core_i = lax.axis_index("zh"), lax.axis_index("core")
    group_index = (x_i * sizes["zl"] + zl_i) * sizes["y"] + y_i
    position = zh_i * sizes["core"] + core_i
    segment_total = segment_row.shape[0]

    blocks = records.reshape(tile_size * block_count, NFFT)
    spectrum = jnp.dot(
        blocks, dft_table(NFFT), precision=lax.Precision.HIGHEST, preferred_element_type=jnp.float32
    )
    white = whiten(spectrum).astype(jnp.bfloat16).reshape(tile_size, block_count, NFFT)
    start_row = jnp.zeros((1, block_count, NFFT), jnp.bfloat16).at[0, 0, 0].set(
        window_start[0].astype(jnp.bfloat16)
    )
    extended = jnp.concatenate([white, start_row], axis=0)
    gathered = gather_relative(extended, "zh", sizes["zh"])
    partner = lax.ppermute(gathered, "core", shift_perm(sizes["core"], 1))
    gathered = jnp.stack([gathered, partner]).reshape(src_count, tile_size + 1, block_count, NFFT)
    left = gathered[:, :tile_size]
    starts = gathered[:, tile_size, 0, 0].astype(jnp.int32)
    group_size = src_count * tile_size
    window_total = group_size // 4
    k_per = window_total // src_count

    slot = jnp.arange(src_count, dtype=jnp.int32)
    slot_zh = (zh_i - slot % sizes["zh"]) % sizes["zh"]
    slot_core = (core_i + slot // sizes["zh"]) % sizes["core"]
    slot_position = slot_zh * sizes["core"] + slot_core
    k_idx = position * k_per + jnp.arange(k_per, dtype=jnp.int32)
    window_idx = starts[:, None] + k_idx[None, :]
    tile_first = (slot_position * tile_size)[:, None]
    source_idx = jnp.where(window_idx < tile_first, window_idx, window_idx + tile_size)
    source_pos = source_idx // tile_size
    source_slot = ((source_pos % sizes["core"] - core_i) % sizes["core"]) * sizes["zh"] + (
        zh_i - source_pos // sizes["core"]
    ) % sizes["zh"]
    source_row = source_slot * (tile_size + 1) + source_idx % tile_size
    sources = jnp.take(
        gathered.reshape(src_count * (tile_size + 1), block_count, NFFT),
        source_row.reshape(-1),
        axis=0,
    ).reshape(src_count, k_per, block_count, NFFT)
    cross = cross_spectra(left, sources)
    flat_rows = cross.reshape(group_size * k_per, NFFT)
    correlation = jnp.dot(
        flat_rows, lag_table(NFFT, LAGS), preferred_element_type=jnp.float32
    ) / math.sqrt(block_count * NFFT // 2)
    correlation = correlation.astype(jnp.bfloat16).reshape(group_size, k_per * LAGS)

    channel_ids = (slot_position[:, None] * tile_size + jnp.arange(tile_size, dtype=jnp.int32)[None, :]).reshape(-1)
    group_segments = jnp.take(channel_segment, group_index * group_size + channel_ids)
    seg_match = group_segments[:, None] == jnp.arange(segment_total, dtype=jnp.int32)[None, :]
    group_rows = jnp.sum(jnp.where(seg_match, segment_row[None, :], 0), axis=1)
    owner = group_rows // SEG_PER
    owner_x = owner // (sizes["zl"] * sizes["y"])
    owner_zl = (owner // sizes["y"]) % sizes["zl"]
    owner_y = owner % sizes["y"]
    staged_rows = (
        (owner_y * sizes["x"] + owner_x) * sizes["zl"] + owner_zl
    ) * SEG_PER + group_rows % SEG_PER
    onehot = (
        jnp.arange(segment_total, dtype=jnp.int32)[:, None] == staged_rows[None, :]
    ).astype(jnp.bfloat16)
    partial = jnp.dot(onehot, correlation, preferred_element_type=jnp.float32).reshape(
        segment_total, k_per, LAGS
    )
    partial = scatter_sum(partial, "y", sizes["y"])
    partial = scatter_sum(partial, "x", sizes["x"])
    summed = scatter_sum(partial, "zl", sizes["zl"])
    counts = row_counts(channel_segment, segment_row, group_index)
    return summed / jnp.sqrt(jnp.maximum(counts, 1.0))[:, None, None]


def solution(mesh):
    names = ("x", "zl", "y", "zh", "core")
    rcv_count, src_count = mesh.devices.shape
    zh_count = src_count // 2
    side = round(rcv_count ** (1 / 3))
    fine = Mesh(mesh.devices.reshape(side, side, rcv_count // side // side, zh_count, 2), names)
    rcv, src = ("x", "zl", "y"), ("zh", "core")
    in_specs = (P(rcv + src, None), P(rcv + src), P(), P())
    out_specs = P(rcv, src, None)
    return jax.shard_map(
        on_device, mesh=fine, in_specs=in_specs, out_specs=out_specs, check_vma=False
    )
```

```python
import math

import jax
import jax.numpy as jnp
from jax import lax
from jax.sharding import Mesh, PartitionSpec as P

NFFT = 1024
LAGS = 256
SEG_PER = 4


def dft_table(length):
    sample_index = jnp.arange(length, dtype=jnp.int32)
    frequency = jnp.arange(length // 2, dtype=jnp.int32)
    angles = (sample_index[:, None] * frequency[None, :] % length).astype(jnp.float32) * (
        2.0 * math.pi / length
    )
    return jnp.concatenate([jnp.cos(angles), -jnp.sin(angles)], axis=1)


def lag_table(length, lag_count):
    frequency = jnp.arange(length // 2, dtype=jnp.int32)
    shifts = jnp.arange(lag_count, dtype=jnp.int32) - lag_count // 2
    angles = (frequency[:, None] * shifts[None, :] % length).astype(jnp.float32) * (
        2.0 * math.pi / length
    )
    return jnp.concatenate([jnp.cos(angles), -jnp.sin(angles)], axis=0).astype(jnp.bfloat16)


def whiten(spectrum):
    half_size = spectrum.shape[-1] // 2
    powers = spectrum[..., :half_size] ** 2 + spectrum[..., half_size:] ** 2
    mean_power = jnp.mean(powers, axis=-1, keepdims=True)
    magnitude = jnp.sqrt(powers + 0.1 * mean_power + 1e-06)
    return spectrum / jnp.concatenate([magnitude, magnitude], axis=-1)


def cross_spectra(left, sources):
    half_size = left.shape[-1] // 2
    lf = left.astype(jnp.float32)[:, :, None]
    sf = sources.astype(jnp.float32)[:, None]
    l_re, l_im = lf[..., :half_size], lf[..., half_size:]
    s_re, s_im = sf[..., :half_size], sf[..., half_size:]
    real_part = jnp.sum(l_re * s_re + l_im * s_im, axis=3)
    imag_part = jnp.sum(l_re * s_im - l_im * s_re, axis=3)
    return jnp.concatenate([real_part, imag_part], axis=-1).astype(jnp.bfloat16)


def row_counts(channel_segment, segment_row, owner):
    held_rows = owner * SEG_PER + jnp.arange(SEG_PER, dtype=jnp.int32)
    matches = segment_row[None, :] == held_rows[:, None]
    segment_ids = jnp.arange(segment_row.shape[0], dtype=jnp.int32)
    held_segments = jnp.sum(jnp.where(matches, segment_ids[None, :], 0), axis=1)
    members = channel_segment[None, :] == held_segments[:, None]
    return jnp.sum(members.astype(jnp.float32), axis=1)


def shift_perm(count, shift):
    return [(i, (i + shift) % count) for i in range(count)]


def gather_relative(value, axis, count):
    if count != 4:
        parts = [value] + [lax.ppermute(value, axis, shift_perm(count, s)) for s in range(1, count)]
        return jnp.stack(parts)
    half = value.shape[-1] // 2
    from_left = lax.ppermute(value, axis, shift_perm(count, 1))
    from_right = lax.ppermute(value, axis, shift_perm(count, -1))
    far_head = lax.ppermute(from_left[..., :half], axis, shift_perm(count, 1))
    far_tail = lax.ppermute(from_right[..., half:], axis, shift_perm(count, -1))
    far = jnp.concatenate([far_head, far_tail], axis=-1)
    return jnp.stack([value, from_left, far, from_right])


def scatter_sum(value, axis, count):
    me = lax.axis_index(axis)
    blocks = value.reshape((count, value.shape[0] // count) + value.shape[1:])

    def block(offset):
        return lax.dynamic_index_in_dim(blocks, (me + offset) % count, axis=0, keepdims=False)

    if count != 4:
        total = block(0)
        for s in range(1, count):
            total = total + lax.ppermute(block(s), axis, shift_perm(count, s))
        return total
    half = blocks.shape[-1] // 2
    right, left, far, own = block(1), block(-1), block(2), block(0)
    to_right = jnp.concatenate([right[..., half:], far[..., :half]], axis=-1)
    to_left = jnp.concatenate([left[..., :half], far[..., half:]], axis=-1)
    got_left = lax.ppermute(to_right, axis, shift_perm(count, 1))
    got_right = lax.ppermute(to_left, axis, shift_perm(count, -1))
    fwd_right = right[..., :half] + got_left[..., half:]
    fwd_left = left[..., half:] + got_right[..., half:]
    got2_left = lax.ppermute(fwd_right, axis, shift_perm(count, 1))
    got2_right = lax.ppermute(fwd_left, axis, shift_perm(count, -1))
    head = own[..., :half] + got_right[..., :half] + got2_left
    tail = own[..., half:] + got_left[..., :half] + got2_right
    return jnp.concatenate([head, tail], axis=-1)


def on_device(records, window_start, channel_segment, segment_row):
    tile_size = records.shape[0]
    block_count = records.shape[1] // NFFT
    sizes = {name: lax.axis_size(name) for name in ("x", "zl", "y", "zh", "core")}
    src_count = sizes["zh"] * sizes["core"]
    x_i, zl_i, y_i = lax.axis_index("x"), lax.axis_index("zl"), lax.axis_index("y")
    zh_i, core_i = lax.axis_index("zh"), lax.axis_index("core")
    group_index = (x_i * sizes["zl"] + zl_i) * sizes["y"] + y_i
    position = zh_i * sizes["core"] + core_i
    segment_total = segment_row.shape[0]

    blocks = records.reshape(tile_size * block_count, NFFT)
    spectrum = jnp.dot(
        blocks, dft_table(NFFT), precision=lax.Precision.HIGHEST, preferred_element_type=jnp.float32
    )
    white = whiten(spectrum).astype(jnp.bfloat16).reshape(tile_size, block_count, NFFT)
    start_row = jnp.zeros((1, block_count, NFFT), jnp.bfloat16).at[0, 0, 0].set(
        window_start[0].astype(jnp.bfloat16)
    )
    extended = jnp.concatenate([white, start_row], axis=0)
    gathered = gather_relative(extended, "zh", sizes["zh"])
    partner = lax.ppermute(gathered, "core", shift_perm(sizes["core"], 1))
    gathered = jnp.stack([gathered, partner]).reshape(src_count, tile_size + 1, block_count, NFFT)
    left = gathered[:, :tile_size]
    starts = gathered[:, tile_size, 0, 0].astype(jnp.int32)
    group_size = src_count * tile_size
    window_total = group_size // 4
    k_per = window_total // src_count

    slot = jnp.arange(src_count, dtype=jnp.int32)
    slot_zh = (zh_i - slot % sizes["zh"]) % sizes["zh"]
    slot_core = (core_i + slot // sizes["zh"]) % sizes["core"]
    slot_position = slot_zh * sizes["core"] + slot_core
    k_idx = position * k_per + jnp.arange(k_per, dtype=jnp.int32)
    window_idx = starts[:, None] + k_idx[None, :]
    tile_first = (slot_position * tile_size)[:, None]
    source_idx = jnp.where(window_idx < tile_first, window_idx, window_idx + tile_size)
    source_pos = source_idx // tile_size
    source_slot = ((source_pos % sizes["core"] - core_i) % sizes["core"]) * sizes["zh"] + (
        zh_i - source_pos // sizes["core"]
    ) % sizes["zh"]
    source_row = source_slot * (tile_size + 1) + source_idx % tile_size
    sources = jnp.take(
        gathered.reshape(src_count * (tile_size + 1), block_count, NFFT),
        source_row.reshape(-1),
        axis=0,
    ).reshape(src_count, k_per, block_count, NFFT)
    cross = cross_spectra(left, sources)
    flat_rows = cross.reshape(group_size * k_per, NFFT)
    correlation = jnp.dot(
        flat_rows, lag_table(NFFT, LAGS), preferred_element_type=jnp.float32
    ) / math.sqrt(block_count * NFFT // 2)
    correlation = correlation.astype(jnp.bfloat16).reshape(group_size, k_per * LAGS)

    channel_ids = (slot_position[:, None] * tile_size + jnp.arange(tile_size, dtype=jnp.int32)[None, :]).reshape(-1)
    group_segments = jnp.take(channel_segment, group_index * group_size + channel_ids)
    seg_match = group_segments[:, None] == jnp.arange(segment_total, dtype=jnp.int32)[None, :]
    group_rows = jnp.sum(jnp.where(seg_match, segment_row[None, :], 0), axis=1)
    owner = group_rows // SEG_PER
    owner_x = owner // (sizes["zl"] * sizes["y"])
    owner_zl = (owner // sizes["y"]) % sizes["zl"]
    owner_y = owner % sizes["y"]
    staged_rows = (
        (owner_y * sizes["x"] + owner_x) * sizes["zl"] + owner_zl
    ) * SEG_PER + group_rows % SEG_PER
    onehot = (
        jnp.arange(segment_total, dtype=jnp.int32)[:, None] == staged_rows[None, :]
    ).astype(jnp.bfloat16)
    partial = jnp.dot(onehot, correlation, preferred_element_type=jnp.float32).reshape(
        segment_total, k_per, LAGS
    )
    partial = scatter_sum(partial, "y", sizes["y"])
    partial = scatter_sum(partial, "x", sizes["x"])
    summed = scatter_sum(partial, "zl", sizes["zl"])
    counts = row_counts(channel_segment, segment_row, group_index)
    return summed / jnp.sqrt(jnp.maximum(counts, 1.0))[:, None, None]


def solution(mesh):
    names = ("x", "zl", "y", "zh", "core")
    rcv_count, src_count = mesh.devices.shape
    zh_count = src_count // 2
    side = round(rcv_count ** (1 / 3))
    fine = Mesh(mesh.devices.reshape(side, side, rcv_count // side // side, zh_count, 2), names)
    rcv, src = ("x", "zl", "y"), ("zh", "core")
    in_specs = (P(rcv + src, None), P(rcv + src), P(), P())
    out_specs = P(rcv, src, None)
    return jax.shard_map(
        on_device, mesh=fine, in_specs=in_specs, out_specs=out_specs, check_vma=False
    )
```

```python
import math

import jax
import jax.numpy as jnp
from jax import lax
from jax.sharding import Mesh, PartitionSpec as P

NFFT = 1024
LAGS = 256
SEG_PER = 4


def dft_table(length):
    fine_count = 32
    coarse_count = length // fine_count
    frequency = jnp.arange(length // 2, dtype=jnp.int32)
    scale = 2.0 * math.pi / length

    def angle_table(steps, stride):
        index = (jnp.arange(steps, dtype=jnp.int32)[:, None] * stride * frequency[None, :]) % length
        angles = index.astype(jnp.float32) * scale
        return jnp.cos(angles), jnp.sin(angles)

    coarse_cos, coarse_sin = angle_table(coarse_count, fine_count)
    fine_cos, fine_sin = angle_table(fine_count, 1)
    cos_part = coarse_cos[:, None] * fine_cos[None] - coarse_sin[:, None] * fine_sin[None]
    sin_part = coarse_sin[:, None] * fine_cos[None] + coarse_cos[:, None] * fine_sin[None]
    return jnp.concatenate([cos_part, -sin_part], axis=-1).reshape(length, length)


def lag_table(length, lag_count):
    frequency = jnp.arange(length // 2, dtype=jnp.int32)
    shifts = jnp.arange(lag_count, dtype=jnp.int32) - lag_count // 2
    angles = (frequency[:, None] * shifts[None, :] % length).astype(jnp.float32) * (
        2.0 * math.pi / length
    )
    return jnp.concatenate([jnp.cos(angles), -jnp.sin(angles)], axis=0).astype(jnp.bfloat16)


def whiten(spectrum):
    half_size = spectrum.shape[-1] // 2
    powers = spectrum[..., :half_size] ** 2 + spectrum[..., half_size:] ** 2
    mean_power = jnp.mean(powers, axis=-1, keepdims=True)
    magnitude = jnp.sqrt(powers + 0.1 * mean_power + 1e-06)
    return spectrum / jnp.concatenate([magnitude, magnitude], axis=-1)


def cross_spectra(left, sources):
    half_size = left.shape[-1] // 2
    lf = left.astype(jnp.float32)[:, :, None]
    sf = sources.astype(jnp.float32)[:, None]
    l_re, l_im = lf[..., :half_size], lf[..., half_size:]
    s_re, s_im = sf[..., :half_size], sf[..., half_size:]
    real_part = jnp.sum(l_re * s_re + l_im * s_im, axis=3)
    imag_part = jnp.sum(l_re * s_im - l_im * s_re, axis=3)
    return jnp.concatenate([real_part, imag_part], axis=-1).astype(jnp.bfloat16)


def row_counts(channel_segment, segment_row, owner):
    held_rows = owner * SEG_PER + jnp.arange(SEG_PER, dtype=jnp.int32)
    matches = segment_row[None, :] == held_rows[:, None]
    segment_ids = jnp.arange(segment_row.shape[0], dtype=jnp.int32)
    held_segments = jnp.sum(jnp.where(matches, segment_ids[None, :], 0), axis=1)
    members = channel_segment[None, :] == held_segments[:, None]
    return jnp.sum(members.astype(jnp.float32), axis=1)


def shift_perm(count, shift):
    return [(i, (i + shift) % count) for i in range(count)]


def gather_relative(value, axis, count):
    if count != 4:
        parts = [value] + [lax.ppermute(value, axis, shift_perm(count, s)) for s in range(1, count)]
        return jnp.stack(parts)
    half = value.shape[-1] // 2
    from_left = lax.ppermute(value, axis, shift_perm(count, 1))
    from_right = lax.ppermute(value, axis, shift_perm(count, -1))
    far_head = lax.ppermute(from_left[..., :half], axis, shift_perm(count, 1))
    far_tail = lax.ppermute(from_right[..., half:], axis, shift_perm(count, -1))
    far = jnp.concatenate([far_head, far_tail], axis=-1)
    return jnp.stack([value, from_left, far, from_right])


def scatter_sum(value, axis, count):
    me = lax.axis_index(axis)
    blocks = value.reshape((count, value.shape[0] // count) + value.shape[1:])

    def block(offset):
        return lax.dynamic_index_in_dim(blocks, (me + offset) % count, axis=0, keepdims=False)

    if count != 4:
        total = block(0)
        for s in range(1, count):
            total = total + lax.ppermute(block(s), axis, shift_perm(count, s))
        return total
    half = blocks.shape[-1] // 2
    right, left, far, own = block(1), block(-1), block(2), block(0)
    to_right = jnp.concatenate([right[..., half:], far[..., :half]], axis=-1)
    to_left = jnp.concatenate([left[..., :half], far[..., half:]], axis=-1)
    got_left = lax.ppermute(to_right, axis, shift_perm(count, 1))
    got_right = lax.ppermute(to_left, axis, shift_perm(count, -1))
    fwd_right = right[..., :half] + got_left[..., half:]
    fwd_left = left[..., half:] + got_right[..., half:]
    got2_left = lax.ppermute(fwd_right, axis, shift_perm(count, 1))
    got2_right = lax.ppermute(fwd_left, axis, shift_perm(count, -1))
    head = own[..., :half] + got_right[..., :half] + got2_left
    tail = own[..., half:] + got_left[..., :half] + got2_right
    return jnp.concatenate([head, tail], axis=-1)


def scatter_sum_direct(value, axis, count):
    me = lax.axis_index(axis)
    blocks = value.reshape((count, value.shape[0] // count) + value.shape[1:])
    total = lax.dynamic_index_in_dim(blocks, me, axis=0, keepdims=False)
    for s in range(1, count):
        piece = lax.dynamic_index_in_dim(blocks, (me + s) % count, axis=0, keepdims=False)
        sent = lax.ppermute(piece.astype(jnp.bfloat16), axis, shift_perm(count, s))
        total = total + sent.astype(jnp.float32)
    return total


def on_device(records, window_start, channel_segment, segment_row):
    tile_size = records.shape[0]
    block_count = records.shape[1] // NFFT
    sizes = {name: lax.axis_size(name) for name in ("x", "zl", "y", "zh", "core")}
    src_count = sizes["zh"] * sizes["core"]
    x_i, zl_i, y_i = lax.axis_index("x"), lax.axis_index("zl"), lax.axis_index("y")
    zh_i, core_i = lax.axis_index("zh"), lax.axis_index("core")
    group_index = (x_i * sizes["zl"] + zl_i) * sizes["y"] + y_i
    position = zh_i * sizes["core"] + core_i
    segment_total = segment_row.shape[0]

    blocks = records.reshape(tile_size * block_count, NFFT)
    spectrum = jnp.dot(
        blocks, dft_table(NFFT), precision=lax.Precision.HIGHEST, preferred_element_type=jnp.float32
    )
    white = whiten(spectrum).astype(jnp.bfloat16).reshape(tile_size, block_count, NFFT)
    start_row = jnp.zeros((1, block_count, NFFT), jnp.bfloat16).at[0, 0, 0].set(
        window_start[0].astype(jnp.bfloat16)
    )
    extended = jnp.concatenate([white, start_row], axis=0)
    gathered = gather_relative(extended, "zh", sizes["zh"])
    partner = lax.ppermute(gathered, "core", shift_perm(sizes["core"], 1))
    gathered = jnp.stack([gathered, partner]).reshape(src_count, tile_size + 1, block_count, NFFT)
    left = gathered[:, :tile_size]
    starts = gathered[:, tile_size, 0, 0].astype(jnp.int32)
    group_size = src_count * tile_size
    window_total = group_size // 4
    k_per = window_total // src_count

    slot = jnp.arange(src_count, dtype=jnp.int32)
    slot_zh = (zh_i - slot % sizes["zh"]) % sizes["zh"]
    slot_core = (core_i + slot // sizes["zh"]) % sizes["core"]
    slot_position = slot_zh * sizes["core"] + slot_core
    k_idx = position * k_per + jnp.arange(k_per, dtype=jnp.int32)
    window_idx = starts[:, None] + k_idx[None, :]
    tile_first = (slot_position * tile_size)[:, None]
    source_idx = jnp.where(window_idx < tile_first, window_idx, window_idx + tile_size)
    source_pos = source_idx // tile_size
    source_slot = ((source_pos % sizes["core"] - core_i) % sizes["core"]) * sizes["zh"] + (
        zh_i - source_pos // sizes["core"]
    ) % sizes["zh"]
    source_row = source_slot * (tile_size + 1) + source_idx % tile_size
    sources = jnp.take(
        gathered.reshape(src_count * (tile_size + 1), block_count, NFFT),
        source_row.reshape(-1),
        axis=0,
    ).reshape(src_count, k_per, block_count, NFFT)
    cross = cross_spectra(left, sources)
    flat_rows = cross.reshape(group_size * k_per, NFFT)
    correlation = jnp.dot(
        flat_rows, lag_table(NFFT, LAGS), preferred_element_type=jnp.float32
    ) / math.sqrt(block_count * NFFT // 2)
    correlation = correlation.astype(jnp.bfloat16).reshape(group_size, k_per * LAGS)

    channel_ids = (slot_position[:, None] * tile_size + jnp.arange(tile_size, dtype=jnp.int32)[None, :]).reshape(-1)
    group_segments = jnp.take(channel_segment, group_index * group_size + channel_ids)
    seg_match = group_segments[:, None] == jnp.arange(segment_total, dtype=jnp.int32)[None, :]
    group_rows = jnp.sum(jnp.where(seg_match, segment_row[None, :], 0), axis=1)
    owner = group_rows // SEG_PER
    owner_x = owner // (sizes["zl"] * sizes["y"])
    owner_zl = (owner // sizes["y"]) % sizes["zl"]
    owner_y = owner % sizes["y"]
    staged_rows = (
        (owner_y * sizes["x"] + owner_x) * sizes["zl"] + owner_zl
    ) * SEG_PER + group_rows % SEG_PER
    onehot = (
        jnp.arange(segment_total, dtype=jnp.int32)[:, None] == staged_rows[None, :]
    ).astype(jnp.bfloat16)
    partial = jnp.dot(onehot, correlation, preferred_element_type=jnp.float32).reshape(
        segment_total, k_per, LAGS
    )
    partial = scatter_sum_direct(partial, "y", sizes["y"])
    plane = sizes["x"] * sizes["zl"]
    pieces = partial.reshape((plane, partial.shape[0] // plane) + partial.shape[1:])
    arrived = lax.all_to_all(pieces, ("x", "zl"), split_axis=0, concat_axis=0, tiled=True)
    summed = jnp.sum(arrived, axis=0)
    counts = row_counts(channel_segment, segment_row, group_index)
    return summed / jnp.sqrt(jnp.maximum(counts, 1.0))[:, None, None]


def solution(mesh):
    names = ("x", "zl", "y", "zh", "core")
    rcv_count, src_count = mesh.devices.shape
    zh_count = src_count // 2
    side = round(rcv_count ** (1 / 3))
    fine = Mesh(mesh.devices.reshape(side, side, rcv_count // side // side, zh_count, 2), names)
    rcv, src = ("x", "zl", "y"), ("zh", "core")
    in_specs = (P(rcv + src, None), P(rcv + src), P(), P())
    out_specs = P(rcv, src, None)
    return jax.shard_map(
        on_device, mesh=fine, in_specs=in_specs, out_specs=out_specs, check_vma=False
    )
```

```python
import math

import jax
import jax.numpy as jnp
from jax import lax
from jax.sharding import Mesh, PartitionSpec as P

NFFT = 1024
LAGS = 256
SEG_PER = 4


def dft_table(length):
    fine_count = 32
    coarse_count = length // fine_count
    frequency = jnp.arange(length // 2, dtype=jnp.int32)
    scale = 2.0 * math.pi / length

    def angle_table(steps, stride):
        index = (jnp.arange(steps, dtype=jnp.int32)[:, None] * stride * frequency[None, :]) % length
        angles = index.astype(jnp.float32) * scale
        return jnp.cos(angles), jnp.sin(angles)

    coarse_cos, coarse_sin = angle_table(coarse_count, fine_count)
    fine_cos, fine_sin = angle_table(fine_count, 1)
    cos_part = coarse_cos[:, None] * fine_cos[None] - coarse_sin[:, None] * fine_sin[None]
    sin_part = coarse_sin[:, None] * fine_cos[None] + coarse_cos[:, None] * fine_sin[None]
    return jnp.concatenate([cos_part, -sin_part], axis=-1).reshape(length, length)


def lag_table(length, lag_count):
    frequency = jnp.arange(length // 2, dtype=jnp.int32)
    shifts = jnp.arange(lag_count, dtype=jnp.int32) - lag_count // 2
    angles = (frequency[:, None] * shifts[None, :] % length).astype(jnp.float32) * (
        2.0 * math.pi / length
    )
    return jnp.concatenate([jnp.cos(angles), -jnp.sin(angles)], axis=0).astype(jnp.bfloat16)


def whiten(spectrum):
    half_size = spectrum.shape[-1] // 2
    powers = spectrum[..., :half_size] ** 2 + spectrum[..., half_size:] ** 2
    mean_power = jnp.mean(powers, axis=-1, keepdims=True)
    magnitude = jnp.sqrt(powers + 0.1 * mean_power + 1e-06)
    return spectrum / jnp.concatenate([magnitude, magnitude], axis=-1)


def cross_spectra(left, sources):
    half_size = left.shape[-1] // 2
    lf = left.astype(jnp.float32)[:, :, None]
    sf = sources.astype(jnp.float32)[:, None]
    l_re, l_im = lf[..., :half_size], lf[..., half_size:]
    s_re, s_im = sf[..., :half_size], sf[..., half_size:]
    real_part = jnp.sum(l_re * s_re + l_im * s_im, axis=3)
    imag_part = jnp.sum(l_re * s_im - l_im * s_re, axis=3)
    return jnp.concatenate([real_part, imag_part], axis=-1).astype(jnp.bfloat16)


def row_counts(channel_segment, segment_row, owner):
    held_rows = owner * SEG_PER + jnp.arange(SEG_PER, dtype=jnp.int32)
    matches = segment_row[None, :] == held_rows[:, None]
    segment_ids = jnp.arange(segment_row.shape[0], dtype=jnp.int32)
    held_segments = jnp.sum(jnp.where(matches, segment_ids[None, :], 0), axis=1)
    members = channel_segment[None, :] == held_segments[:, None]
    return jnp.sum(members.astype(jnp.float32), axis=1)


def shift_perm(count, shift):
    return [(i, (i + shift) % count) for i in range(count)]


def gather_relative(value, axis, count):
    if count != 4:
        parts = [value] + [lax.ppermute(value, axis, shift_perm(count, s)) for s in range(1, count)]
        return jnp.stack(parts)
    half = value.shape[-1] // 2
    from_left = lax.ppermute(value, axis, shift_perm(count, 1))
    from_right = lax.ppermute(value, axis, shift_perm(count, -1))
    far_head = lax.ppermute(from_left[..., :half], axis, shift_perm(count, 1))
    far_tail = lax.ppermute(from_right[..., half:], axis, shift_perm(count, -1))
    far = jnp.concatenate([far_head, far_tail], axis=-1)
    return jnp.stack([value, from_left, far, from_right])


def scatter_sum(value, axis, count):
    me = lax.axis_index(axis)
    blocks = value.reshape((count, value.shape[0] // count) + value.shape[1:])

    def block(offset):
        return lax.dynamic_index_in_dim(blocks, (me + offset) % count, axis=0, keepdims=False)

    if count != 4:
        total = block(0)
        for s in range(1, count):
            total = total + lax.ppermute(block(s), axis, shift_perm(count, s))
        return total
    half = blocks.shape[-1] // 2
    right, left, far, own = block(1), block(-1), block(2), block(0)
    to_right = jnp.concatenate([right[..., half:], far[..., :half]], axis=-1)
    to_left = jnp.concatenate([left[..., :half], far[..., half:]], axis=-1)
    got_left = lax.ppermute(to_right, axis, shift_perm(count, 1))
    got_right = lax.ppermute(to_left, axis, shift_perm(count, -1))
    fwd_right = right[..., :half] + got_left[..., half:]
    fwd_left = left[..., half:] + got_right[..., half:]
    got2_left = lax.ppermute(fwd_right, axis, shift_perm(count, 1))
    got2_right = lax.ppermute(fwd_left, axis, shift_perm(count, -1))
    head = own[..., :half] + got_right[..., :half] + got2_left
    tail = own[..., half:] + got_left[..., :half] + got2_right
    return jnp.concatenate([head, tail], axis=-1)


def scatter_sum_direct(value, axis, count):
    me = lax.axis_index(axis)
    blocks = value.reshape((count, value.shape[0] // count) + value.shape[1:])
    total = lax.dynamic_index_in_dim(blocks, me, axis=0, keepdims=False)
    for s in range(1, count):
        piece = lax.dynamic_index_in_dim(blocks, (me + s) % count, axis=0, keepdims=False)
        sent = lax.ppermute(piece.astype(jnp.bfloat16), axis, shift_perm(count, s))
        total = total + sent.astype(jnp.float32)
    return total


def on_device(records, window_start, channel_segment, segment_row):
    tile_size = records.shape[0]
    block_count = records.shape[1] // NFFT
    sizes = {name: lax.axis_size(name) for name in ("x", "zl", "y", "zh", "core")}
    src_count = sizes["zh"] * sizes["core"]
    x_i, zl_i, y_i = lax.axis_index("x"), lax.axis_index("zl"), lax.axis_index("y")
    zh_i, core_i = lax.axis_index("zh"), lax.axis_index("core")
    group_index = (x_i * sizes["zl"] + zl_i) * sizes["y"] + y_i
    position = zh_i * sizes["core"] + core_i
    segment_total = segment_row.shape[0]

    blocks = records.reshape(tile_size * block_count, NFFT)
    spectrum = jnp.dot(
        blocks, dft_table(NFFT), precision=lax.Precision.HIGHEST, preferred_element_type=jnp.float32
    )
    white = whiten(spectrum).astype(jnp.bfloat16).reshape(tile_size, block_count, NFFT)
    start_row = jnp.zeros((1, block_count, NFFT), jnp.bfloat16).at[0, 0, 0].set(
        window_start[0].astype(jnp.bfloat16)
    )
    extended = jnp.concatenate([white, start_row], axis=0)
    gathered = gather_relative(extended, "zh", sizes["zh"])
    partner = lax.ppermute(gathered, "core", shift_perm(sizes["core"], 1))
    gathered = jnp.stack([gathered, partner]).reshape(src_count, tile_size + 1, block_count, NFFT)
    left = gathered[:, :tile_size]
    starts = gathered[:, tile_size, 0, 0].astype(jnp.int32)
    group_size = src_count * tile_size
    window_total = group_size // 4
    k_per = window_total // src_count

    slot = jnp.arange(src_count, dtype=jnp.int32)
    slot_zh = (zh_i - slot % sizes["zh"]) % sizes["zh"]
    slot_core = (core_i + slot // sizes["zh"]) % sizes["core"]
    slot_position = slot_zh * sizes["core"] + slot_core
    k_idx = position * k_per + jnp.arange(k_per, dtype=jnp.int32)
    window_idx = starts[:, None] + k_idx[None, :]
    tile_first = (slot_position * tile_size)[:, None]
    source_idx = jnp.where(window_idx < tile_first, window_idx, window_idx + tile_size)
    source_pos = source_idx // tile_size
    source_slot = ((source_pos % sizes["core"] - core_i) % sizes["core"]) * sizes["zh"] + (
        zh_i - source_pos // sizes["core"]
    ) % sizes["zh"]
    source_row = source_slot * (tile_size + 1) + source_idx % tile_size
    sources = jnp.take(
        gathered.reshape(src_count * (tile_size + 1), block_count, NFFT),
        source_row.reshape(-1),
        axis=0,
    ).reshape(src_count, k_per, block_count, NFFT)
    cross = cross_spectra(left, sources)
    flat_rows = cross.reshape(group_size * k_per, NFFT)
    correlation = jnp.dot(
        flat_rows, lag_table(NFFT, LAGS), preferred_element_type=jnp.float32
    ) / math.sqrt(block_count * NFFT // 2)
    correlation = correlation.astype(jnp.bfloat16).reshape(group_size, k_per * LAGS)

    channel_ids = (slot_position[:, None] * tile_size + jnp.arange(tile_size, dtype=jnp.int32)[None, :]).reshape(-1)
    group_segments = jnp.take(channel_segment, group_index * group_size + channel_ids)
    seg_match = group_segments[:, None] == jnp.arange(segment_total, dtype=jnp.int32)[None, :]
    group_rows = jnp.sum(jnp.where(seg_match, segment_row[None, :], 0), axis=1)
    staged_rows = group_rows
    onehot = (
        jnp.arange(segment_total, dtype=jnp.int32)[:, None] == staged_rows[None, :]
    ).astype(jnp.bfloat16)
    partial = jnp.dot(onehot, correlation, preferred_element_type=jnp.float32).reshape(
        segment_total, k_per, LAGS
    )
    owners = sizes["x"] * sizes["zl"] * sizes["y"]
    pieces = partial.astype(jnp.bfloat16).reshape((owners, partial.shape[0] // owners) + partial.shape[1:])
    arrived = lax.all_to_all(pieces, ("x", "zl", "y"), split_axis=0, concat_axis=0, tiled=True)
    summed = jnp.sum(arrived.astype(jnp.float32), axis=0)
    counts = row_counts(channel_segment, segment_row, group_index)
    return summed / jnp.sqrt(jnp.maximum(counts, 1.0))[:, None, None]


def solution(mesh):
    names = ("x", "zl", "y", "zh", "core")
    rcv_count, src_count = mesh.devices.shape
    zh_count = src_count // 2
    side = round(rcv_count ** (1 / 3))
    fine = Mesh(mesh.devices.reshape(side, side, rcv_count // side // side, zh_count, 2), names)
    rcv, src = ("x", "zl", "y"), ("zh", "core")
    in_specs = (P(rcv + src, None), P(rcv + src), P(), P())
    out_specs = P(rcv, src, None)
    return jax.shard_map(
        on_device, mesh=fine, in_specs=in_specs, out_specs=out_specs, check_vma=False
    )
```

```python
import math

import jax
import jax.numpy as jnp
from jax import lax
from jax.sharding import Mesh, PartitionSpec as P

NFFT = 1024
LAGS = 256
SEG_PER = 4


def dft_table(length):
    fine_count = 32
    coarse_count = length // fine_count
    frequency = jnp.arange(length // 2, dtype=jnp.int32)
    scale = 2.0 * math.pi / length

    def angle_table(steps, stride):
        index = (jnp.arange(steps, dtype=jnp.int32)[:, None] * stride * frequency[None, :]) % length
        angles = index.astype(jnp.float32) * scale
        return jnp.cos(angles), jnp.sin(angles)

    coarse_cos, coarse_sin = angle_table(coarse_count, fine_count)
    fine_cos, fine_sin = angle_table(fine_count, 1)
    cos_part = coarse_cos[:, None] * fine_cos[None] - coarse_sin[:, None] * fine_sin[None]
    sin_part = coarse_sin[:, None] * fine_cos[None] + coarse_cos[:, None] * fine_sin[None]
    return jnp.concatenate([cos_part, -sin_part], axis=-1).reshape(length, length)


def lag_table(length, lag_count):
    frequency = jnp.arange(length // 2, dtype=jnp.int32)
    shifts = jnp.arange(lag_count, dtype=jnp.int32) - lag_count // 2
    angles = (frequency[:, None] * shifts[None, :] % length).astype(jnp.float32) * (
        2.0 * math.pi / length
    )
    return jnp.concatenate([jnp.cos(angles), -jnp.sin(angles)], axis=0).astype(jnp.bfloat16)


def whiten(spectrum):
    half_size = spectrum.shape[-1] // 2
    powers = spectrum[..., :half_size] ** 2 + spectrum[..., half_size:] ** 2
    mean_power = jnp.mean(powers, axis=-1, keepdims=True)
    magnitude = jnp.sqrt(powers + 0.1 * mean_power + 1e-06)
    return spectrum / jnp.concatenate([magnitude, magnitude], axis=-1)


def cross_spectra(left, sources):
    half_size = left.shape[-1] // 2
    lf = left.astype(jnp.float32)[:, :, None]
    sf = sources.astype(jnp.float32)[:, None]
    l_re, l_im = lf[..., :half_size], lf[..., half_size:]
    s_re, s_im = sf[..., :half_size], sf[..., half_size:]
    real_part = jnp.sum(l_re * s_re + l_im * s_im, axis=3)
    imag_part = jnp.sum(l_re * s_im - l_im * s_re, axis=3)
    return jnp.concatenate([real_part, imag_part], axis=-1)


def row_counts(channel_segment, segment_row, owner):
    held_rows = owner * SEG_PER + jnp.arange(SEG_PER, dtype=jnp.int32)
    matches = segment_row[None, :] == held_rows[:, None]
    segment_ids = jnp.arange(segment_row.shape[0], dtype=jnp.int32)
    held_segments = jnp.sum(jnp.where(matches, segment_ids[None, :], 0), axis=1)
    members = channel_segment[None, :] == held_segments[:, None]
    return jnp.sum(members.astype(jnp.float32), axis=1)


def shift_perm(count, shift):
    return [(i, (i + shift) % count) for i in range(count)]


def gather_relative(value, axis, count):
    if count != 4:
        parts = [value] + [lax.ppermute(value, axis, shift_perm(count, s)) for s in range(1, count)]
        return jnp.stack(parts)
    half = value.shape[-1] // 2
    from_left = lax.ppermute(value, axis, shift_perm(count, 1))
    from_right = lax.ppermute(value, axis, shift_perm(count, -1))
    far_head = lax.ppermute(from_left[..., :half], axis, shift_perm(count, 1))
    far_tail = lax.ppermute(from_right[..., half:], axis, shift_perm(count, -1))
    far = jnp.concatenate([far_head, far_tail], axis=-1)
    return jnp.stack([value, from_left, far, from_right])


def scatter_sum(value, axis, count):
    me = lax.axis_index(axis)
    blocks = value.reshape((count, value.shape[0] // count) + value.shape[1:])

    def block(offset):
        return lax.dynamic_index_in_dim(blocks, (me + offset) % count, axis=0, keepdims=False)

    if count != 4:
        total = block(0)
        for s in range(1, count):
            total = total + lax.ppermute(block(s), axis, shift_perm(count, s))
        return total
    half = blocks.shape[-1] // 2
    right, left, far, own = block(1), block(-1), block(2), block(0)
    to_right = jnp.concatenate([right[..., half:], far[..., :half]], axis=-1)
    to_left = jnp.concatenate([left[..., :half], far[..., half:]], axis=-1)
    got_left = lax.ppermute(to_right, axis, shift_perm(count, 1))
    got_right = lax.ppermute(to_left, axis, shift_perm(count, -1))
    fwd_right = right[..., :half] + got_left[..., half:]
    fwd_left = left[..., half:] + got_right[..., half:]
    got2_left = lax.ppermute(fwd_right, axis, shift_perm(count, 1))
    got2_right = lax.ppermute(fwd_left, axis, shift_perm(count, -1))
    head = own[..., :half] + got_right[..., :half] + got2_left
    tail = own[..., half:] + got_left[..., :half] + got2_right
    return jnp.concatenate([head, tail], axis=-1)


def scatter_sum_direct(value, axis, count):
    me = lax.axis_index(axis)
    blocks = value.reshape((count, value.shape[0] // count) + value.shape[1:])
    total = lax.dynamic_index_in_dim(blocks, me, axis=0, keepdims=False)
    for s in range(1, count):
        piece = lax.dynamic_index_in_dim(blocks, (me + s) % count, axis=0, keepdims=False)
        sent = lax.ppermute(piece.astype(jnp.bfloat16), axis, shift_perm(count, s))
        total = total + sent.astype(jnp.float32)
    return total


def on_device(records, window_start, channel_segment, segment_row):
    tile_size = records.shape[0]
    block_count = records.shape[1] // NFFT
    sizes = {name: lax.axis_size(name) for name in ("x", "zl", "y", "zh", "core")}
    src_count = sizes["zh"] * sizes["core"]
    x_i, zl_i, y_i = lax.axis_index("x"), lax.axis_index("zl"), lax.axis_index("y")
    zh_i, core_i = lax.axis_index("zh"), lax.axis_index("core")
    group_index = (x_i * sizes["zl"] + zl_i) * sizes["y"] + y_i
    position = zh_i * sizes["core"] + core_i
    segment_total = segment_row.shape[0]

    blocks = records.reshape(tile_size * block_count, NFFT)
    spectrum = jnp.dot(
        blocks, dft_table(NFFT), precision=lax.Precision.HIGHEST, preferred_element_type=jnp.float32
    )
    white = whiten(spectrum).astype(jnp.bfloat16).reshape(tile_size, block_count, NFFT)
    start_row = jnp.zeros((1, block_count, NFFT), jnp.bfloat16).at[0, 0, 0].set(
        window_start[0].astype(jnp.bfloat16)
    )
    extended = jnp.concatenate([white, start_row], axis=0)
    chunk = block_count // 2
    group_size = src_count * tile_size
    window_total = group_size // 4
    k_per = window_total // src_count
    slot = jnp.arange(src_count, dtype=jnp.int32)
    slot_zh = (zh_i - slot % sizes["zh"]) % sizes["zh"]
    slot_core = (core_i + slot // sizes["zh"]) % sizes["core"]
    slot_position = slot_zh * sizes["core"] + slot_core
    k_idx = position * k_per + jnp.arange(k_per, dtype=jnp.int32)
    cross = None
    source_row = None
    for first in range(0, block_count, chunk):
        piece = extended[:, first:first + chunk]
        gathered = gather_relative(piece, "zh", sizes["zh"])
        partner = lax.ppermute(gathered, "core", shift_perm(sizes["core"], 1))
        gathered = jnp.stack([gathered, partner]).reshape(src_count, tile_size + 1, chunk, NFFT)
        if source_row is None:
            starts = gathered[:, tile_size, 0, 0].astype(jnp.int32)
            window_idx = starts[:, None] + k_idx[None, :]
            tile_first = (slot_position * tile_size)[:, None]
            source_idx = jnp.where(window_idx < tile_first, window_idx, window_idx + tile_size)
            source_pos = source_idx // tile_size
            source_slot = ((source_pos % sizes["core"] - core_i) % sizes["core"]) * sizes["zh"] + (
                zh_i - source_pos // sizes["core"]
            ) % sizes["zh"]
            source_row = source_slot * (tile_size + 1) + source_idx % tile_size
        sources = jnp.take(
            gathered.reshape(src_count * (tile_size + 1), chunk, NFFT),
            source_row.reshape(-1),
            axis=0,
        ).reshape(src_count, k_per, chunk, NFFT)
        part = cross_spectra(gathered[:, :tile_size], sources)
        cross = part if cross is None else cross + part
    cross = cross.astype(jnp.bfloat16)
    flat_rows = cross.reshape(group_size * k_per, NFFT)
    correlation = jnp.dot(
        flat_rows, lag_table(NFFT, LAGS), preferred_element_type=jnp.float32
    ) / math.sqrt(block_count * NFFT // 2)
    correlation = correlation.astype(jnp.bfloat16).reshape(group_size, k_per * LAGS)

    channel_ids = (slot_position[:, None] * tile_size + jnp.arange(tile_size, dtype=jnp.int32)[None, :]).reshape(-1)
    group_segments = jnp.take(channel_segment, group_index * group_size + channel_ids)
    seg_match = group_segments[:, None] == jnp.arange(segment_total, dtype=jnp.int32)[None, :]
    group_rows = jnp.sum(jnp.where(seg_match, segment_row[None, :], 0), axis=1)
    staged_rows = group_rows
    onehot = (
        jnp.arange(segment_total, dtype=jnp.int32)[:, None] == staged_rows[None, :]
    ).astype(jnp.bfloat16)
    partial = jnp.dot(onehot, correlation, preferred_element_type=jnp.float32).reshape(
        segment_total, k_per, LAGS
    )
    owners = sizes["x"] * sizes["zl"] * sizes["y"]
    pieces = partial.astype(jnp.bfloat16).reshape((owners, partial.shape[0] // owners) + partial.shape[1:])
    arrived = lax.all_to_all(pieces, ("x", "zl", "y"), split_axis=0, concat_axis=0, tiled=True)
    summed = jnp.sum(arrived.astype(jnp.float32), axis=0)
    counts = row_counts(channel_segment, segment_row, group_index)
    return summed / jnp.sqrt(jnp.maximum(counts, 1.0))[:, None, None]


def solution(mesh):
    names = ("x", "zl", "y", "zh", "core")
    rcv_count, src_count = mesh.devices.shape
    zh_count = src_count // 2
    side = round(rcv_count ** (1 / 3))
    fine = Mesh(mesh.devices.reshape(side, side, rcv_count // side // side, zh_count, 2), names)
    rcv, src = ("x", "zl", "y"), ("zh", "core")
    in_specs = (P(rcv + src, None), P(rcv + src), P(), P())
    out_specs = P(rcv, src, None)
    return jax.shard_map(
        on_device, mesh=fine, in_specs=in_specs, out_specs=out_specs, check_vma=False
    )
```

```python
import math

import jax
import jax.numpy as jnp
from jax import lax
from jax.sharding import Mesh, PartitionSpec as P

NFFT = 1024
LAGS = 256
SEG_PER = 4


def dft_table(length):
    fine_count = 32
    coarse_count = length // fine_count
    frequency = jnp.arange(length // 2, dtype=jnp.int32)
    scale = 2.0 * math.pi / length

    def angle_table(steps, stride):
        index = (jnp.arange(steps, dtype=jnp.int32)[:, None] * stride * frequency[None, :]) % length
        angles = index.astype(jnp.float32) * scale
        return jnp.cos(angles), jnp.sin(angles)

    coarse_cos, coarse_sin = angle_table(coarse_count, fine_count)
    fine_cos, fine_sin = angle_table(fine_count, 1)
    cos_part = coarse_cos[:, None] * fine_cos[None] - coarse_sin[:, None] * fine_sin[None]
    sin_part = coarse_sin[:, None] * fine_cos[None] + coarse_cos[:, None] * fine_sin[None]
    return jnp.concatenate([cos_part, -sin_part], axis=-1).reshape(length, length)


def lag_table(length, lag_count):
    frequency = jnp.arange(length // 2, dtype=jnp.int32)
    shifts = jnp.arange(lag_count, dtype=jnp.int32) - lag_count // 2
    angles = (frequency[:, None] * shifts[None, :] % length).astype(jnp.float32) * (
        2.0 * math.pi / length
    )
    return jnp.concatenate([jnp.cos(angles), -jnp.sin(angles)], axis=0).astype(jnp.bfloat16)


def whiten(spectrum):
    half_size = spectrum.shape[-1] // 2
    powers = spectrum[..., :half_size] ** 2 + spectrum[..., half_size:] ** 2
    mean_power = jnp.mean(powers, axis=-1, keepdims=True)
    magnitude = jnp.sqrt(powers + 0.1 * mean_power + 1e-06)
    return spectrum / jnp.concatenate([magnitude, magnitude], axis=-1)


def cross_spectra(left, sources):
    half_size = left.shape[-1] // 2
    l_re = left[:, :, None, :, :half_size].astype(jnp.float32)
    l_im = left[:, :, None, :, half_size:].astype(jnp.float32)
    s_re = sources[:, None, :, :, :half_size].astype(jnp.float32)
    s_im = sources[:, None, :, :, half_size:].astype(jnp.float32)
    real_part = jnp.sum(l_re * s_re + l_im * s_im, axis=3)
    imag_part = jnp.sum(l_re * s_im - l_im * s_re, axis=3)
    return jnp.concatenate([real_part, imag_part], axis=-1).astype(jnp.bfloat16)


def row_counts(channel_segment, segment_row, owner):
    held_rows = owner * SEG_PER + jnp.arange(SEG_PER, dtype=jnp.int32)
    matches = segment_row[None, :] == held_rows[:, None]
    segment_ids = jnp.arange(segment_row.shape[0], dtype=jnp.int32)
    held_segments = jnp.sum(jnp.where(matches, segment_ids[None, :], 0), axis=1)
    members = channel_segment[None, :] == held_segments[:, None]
    return jnp.sum(members.astype(jnp.float32), axis=1)


def shift_perm(count, shift):
    return [(i, (i + shift) % count) for i in range(count)]


def gather_relative(value, axis, count):
    if count != 4:
        parts = [value] + [lax.ppermute(value, axis, shift_perm(count, s)) for s in range(1, count)]
        return jnp.stack(parts)
    half = value.shape[-1] // 2
    from_left = lax.ppermute(value, axis, shift_perm(count, 1))
    from_right = lax.ppermute(value, axis, shift_perm(count, -1))
    far_head = lax.ppermute(from_left[..., :half], axis, shift_perm(count, 1))
    far_tail = lax.ppermute(from_right[..., half:], axis, shift_perm(count, -1))
    far = jnp.concatenate([far_head, far_tail], axis=-1)
    return jnp.stack([value, from_left, far, from_right])


def scatter_sum(value, axis, count):
    me = lax.axis_index(axis)
    blocks = value.reshape((count, value.shape[0] // count) + value.shape[1:])

    def block(offset):
        return lax.dynamic_index_in_dim(blocks, (me + offset) % count, axis=0, keepdims=False)

    if count != 4:
        total = block(0)
        for s in range(1, count):
            total = total + lax.ppermute(block(s), axis, shift_perm(count, s))
        return total
    half = blocks.shape[-1] // 2
    right, left, far, own = block(1), block(-1), block(2), block(0)
    to_right = jnp.concatenate([right[..., half:], far[..., :half]], axis=-1)
    to_left = jnp.concatenate([left[..., :half], far[..., half:]], axis=-1)
    got_left = lax.ppermute(to_right, axis, shift_perm(count, 1))
    got_right = lax.ppermute(to_left, axis, shift_perm(count, -1))
    fwd_right = right[..., :half] + got_left[..., half:]
    fwd_left = left[..., half:] + got_right[..., half:]
    got2_left = lax.ppermute(fwd_right, axis, shift_perm(count, 1))
    got2_right = lax.ppermute(fwd_left, axis, shift_perm(count, -1))
    head = own[..., :half] + got_right[..., :half] + got2_left
    tail = own[..., half:] + got_left[..., :half] + got2_right
    return jnp.concatenate([head, tail], axis=-1)


def scatter_sum_direct(value, axis, count):
    me = lax.axis_index(axis)
    blocks = value.reshape((count, value.shape[0] // count) + value.shape[1:])
    total = lax.dynamic_index_in_dim(blocks, me, axis=0, keepdims=False)
    for s in range(1, count):
        piece = lax.dynamic_index_in_dim(blocks, (me + s) % count, axis=0, keepdims=False)
        sent = lax.ppermute(piece.astype(jnp.bfloat16), axis, shift_perm(count, s))
        total = total + sent.astype(jnp.float32)
    return total


def on_device(records, window_start, channel_segment, segment_row):
    tile_size = records.shape[0]
    block_count = records.shape[1] // NFFT
    sizes = {name: lax.axis_size(name) for name in ("x", "zl", "y", "zh", "core")}
    src_count = sizes["zh"] * sizes["core"]
    x_i, zl_i, y_i = lax.axis_index("x"), lax.axis_index("zl"), lax.axis_index("y")
    zh_i, core_i = lax.axis_index("zh"), lax.axis_index("core")
    group_index = (x_i * sizes["zl"] + zl_i) * sizes["y"] + y_i
    position = zh_i * sizes["core"] + core_i
    segment_total = segment_row.shape[0]

    blocks = records.reshape(tile_size * block_count, NFFT)
    spectrum = jnp.dot(
        blocks, dft_table(NFFT), precision=lax.Precision.HIGHEST, preferred_element_type=jnp.float32
    )
    white = whiten(spectrum).astype(jnp.bfloat16).reshape(tile_size, block_count, NFFT)
    start_row = jnp.zeros((1, block_count, NFFT), jnp.bfloat16).at[0, 0, 0].set(
        window_start[0].astype(jnp.bfloat16)
    )
    extended = jnp.concatenate([white, start_row], axis=0)
    gathered = gather_relative(extended, "zh", sizes["zh"])
    partner = lax.ppermute(gathered, "core", shift_perm(sizes["core"], 1))
    gathered = jnp.stack([gathered, partner]).reshape(src_count, tile_size + 1, block_count, NFFT)
    left = gathered[:, :tile_size]
    starts = gathered[:, tile_size, 0, 0].astype(jnp.int32)
    group_size = src_count * tile_size
    window_total = group_size // 4
    k_per = window_total // src_count

    slot = jnp.arange(src_count, dtype=jnp.int32)
    slot_zh = (zh_i - slot % sizes["zh"]) % sizes["zh"]
    slot_core = (core_i + slot // sizes["zh"]) % sizes["core"]
    slot_position = slot_zh * sizes["core"] + slot_core
    k_idx = position * k_per + jnp.arange(k_per, dtype=jnp.int32)
    window_idx = starts[:, None] + k_idx[None, :]
    tile_first = (slot_position * tile_size)[:, None]
    source_idx = jnp.where(window_idx < tile_first, window_idx, window_idx + tile_size)
    source_pos = source_idx // tile_size
    source_slot = ((source_pos % sizes["core"] - core_i) % sizes["core"]) * sizes["zh"] + (
        zh_i - source_pos // sizes["core"]
    ) % sizes["zh"]
    source_row = source_slot * (tile_size + 1) + source_idx % tile_size
    sources = jnp.take(
        gathered.reshape(src_count * (tile_size + 1), block_count, NFFT),
        source_row.reshape(-1),
        axis=0,
    ).reshape(src_count, k_per, block_count, NFFT)
    cross = cross_spectra(left, sources)
    flat_rows = cross.reshape(group_size * k_per, NFFT)
    correlation = jnp.dot(
        flat_rows, lag_table(NFFT, LAGS), preferred_element_type=jnp.float32
    ) / math.sqrt(block_count * NFFT // 2)
    correlation = correlation.astype(jnp.bfloat16).reshape(group_size, k_per * LAGS)

    channel_ids = (slot_position[:, None] * tile_size + jnp.arange(tile_size, dtype=jnp.int32)[None, :]).reshape(-1)
    group_segments = jnp.take(channel_segment, group_index * group_size + channel_ids)
    seg_match = group_segments[:, None] == jnp.arange(segment_total, dtype=jnp.int32)[None, :]
    group_rows = jnp.sum(jnp.where(seg_match, segment_row[None, :], 0), axis=1)
    staged_rows = group_rows
    onehot = (
        jnp.arange(segment_total, dtype=jnp.int32)[:, None] == staged_rows[None, :]
    ).astype(jnp.bfloat16)
    partial = jnp.dot(onehot, correlation, preferred_element_type=jnp.float32).reshape(
        segment_total, k_per, LAGS
    )
    owners = sizes["x"] * sizes["zl"] * sizes["y"]
    pieces = partial.astype(jnp.bfloat16).reshape(owners, -1)
    arrived = lax.all_to_all(pieces, ("x", "zl", "y"), split_axis=0, concat_axis=0, tiled=True)
    summed = jnp.sum(arrived.astype(jnp.float32), axis=0).reshape(SEG_PER, k_per, LAGS)
    counts = row_counts(channel_segment, segment_row, group_index)
    return summed / jnp.sqrt(jnp.maximum(counts, 1.0))[:, None, None]


def solution(mesh):
    names = ("x", "zl", "y", "zh", "core")
    rcv_count, src_count = mesh.devices.shape
    zh_count = src_count // 2
    side = round(rcv_count ** (1 / 3))
    fine = Mesh(mesh.devices.reshape(side, side, rcv_count // side // side, zh_count, 2), names)
    rcv, src = ("x", "zl", "y"), ("zh", "core")
    in_specs = (P(rcv + src, None), P(rcv + src), P(), P())
    out_specs = P(rcv, src, None)
    return jax.shard_map(
        on_device, mesh=fine, in_specs=in_specs, out_specs=out_specs, check_vma=False
    )
```

```python
import math

import jax
import jax.numpy as jnp
from jax import lax
from jax.sharding import Mesh, PartitionSpec as P

NFFT = 1024
LAGS = 256
SEG_PER = 4


def dft_table(length):
    fine_count = 32
    coarse_count = length // fine_count
    frequency = jnp.arange(length // 2, dtype=jnp.int32)
    scale = 2.0 * math.pi / length

    def angle_table(steps, stride):
        index = (jnp.arange(steps, dtype=jnp.int32)[:, None] * stride * frequency[None, :]) % length
        angles = index.astype(jnp.float32) * scale
        return jnp.cos(angles), jnp.sin(angles)

    coarse_cos, coarse_sin = angle_table(coarse_count, fine_count)
    fine_cos, fine_sin = angle_table(fine_count, 1)
    cos_part = coarse_cos[:, None] * fine_cos[None] - coarse_sin[:, None] * fine_sin[None]
    sin_part = coarse_sin[:, None] * fine_cos[None] + coarse_cos[:, None] * fine_sin[None]
    return jnp.concatenate([cos_part, -sin_part], axis=-1).reshape(length, length)


def lag_table(length, lag_count):
    frequency = jnp.arange(length // 2, dtype=jnp.int32)
    shifts = jnp.arange(lag_count, dtype=jnp.int32) - lag_count // 2
    angles = (frequency[:, None] * shifts[None, :] % length).astype(jnp.float32) * (
        2.0 * math.pi / length
    )
    return jnp.concatenate([jnp.cos(angles), -jnp.sin(angles)], axis=0).astype(jnp.bfloat16)


def whiten(spectrum):
    half_size = spectrum.shape[-1] // 2
    powers = spectrum[..., :half_size] ** 2 + spectrum[..., half_size:] ** 2
    mean_power = jnp.mean(powers, axis=-1, keepdims=True)
    magnitude = jnp.sqrt(powers + 0.1 * mean_power + 1e-06)
    return spectrum / jnp.concatenate([magnitude, magnitude], axis=-1)


def cross_spectra(left, sources):
    half_size = left.shape[-1] // 2
    l_re = left[:, :, None, :, :half_size].astype(jnp.float32)
    l_im = left[:, :, None, :, half_size:].astype(jnp.float32)
    s_re = sources[:, None, :, :, :half_size].astype(jnp.float32)
    s_im = sources[:, None, :, :, half_size:].astype(jnp.float32)
    real_part = jnp.sum(l_re * s_re + l_im * s_im, axis=3)
    imag_part = jnp.sum(l_re * s_im - l_im * s_re, axis=3)
    return jnp.concatenate([real_part, imag_part], axis=-1).astype(jnp.bfloat16)


def row_counts(channel_segment, segment_row, owner):
    held_rows = owner * SEG_PER + jnp.arange(SEG_PER, dtype=jnp.int32)
    matches = segment_row[None, :] == held_rows[:, None]
    segment_ids = jnp.arange(segment_row.shape[0], dtype=jnp.int32)
    held_segments = jnp.sum(jnp.where(matches, segment_ids[None, :], 0), axis=1)
    members = channel_segment[None, :] == held_segments[:, None]
    return jnp.sum(members.astype(jnp.float32), axis=1)


def shift_perm(count, shift):
    return [(i, (i + shift) % count) for i in range(count)]


def gather_relative(value, axis, count):
    if count != 4:
        parts = [value] + [lax.ppermute(value, axis, shift_perm(count, s)) for s in range(1, count)]
        return jnp.stack(parts)
    half = value.shape[-1] // 2
    from_left = lax.ppermute(value, axis, shift_perm(count, 1))
    from_right = lax.ppermute(value, axis, shift_perm(count, -1))
    far_head = lax.ppermute(from_left[..., :half], axis, shift_perm(count, 1))
    far_tail = lax.ppermute(from_right[..., half:], axis, shift_perm(count, -1))
    far = jnp.concatenate([far_head, far_tail], axis=-1)
    return jnp.stack([value, from_left, far, from_right])


def scatter_sum(value, axis, count):
    me = lax.axis_index(axis)
    blocks = value.reshape((count, value.shape[0] // count) + value.shape[1:])

    def block(offset):
        return lax.dynamic_index_in_dim(blocks, (me + offset) % count, axis=0, keepdims=False)

    if count != 4:
        total = block(0)
        for s in range(1, count):
            total = total + lax.ppermute(block(s), axis, shift_perm(count, s))
        return total
    half = blocks.shape[-1] // 2
    right, left, far, own = block(1), block(-1), block(2), block(0)
    to_right = jnp.concatenate([right[..., half:], far[..., :half]], axis=-1)
    to_left = jnp.concatenate([left[..., :half], far[..., half:]], axis=-1)
    got_left = lax.ppermute(to_right, axis, shift_perm(count, 1))
    got_right = lax.ppermute(to_left, axis, shift_perm(count, -1))
    fwd_right = right[..., :half] + got_left[..., half:]
    fwd_left = left[..., half:] + got_right[..., half:]
    got2_left = lax.ppermute(fwd_right, axis, shift_perm(count, 1))
    got2_right = lax.ppermute(fwd_left, axis, shift_perm(count, -1))
    head = own[..., :half] + got_right[..., :half] + got2_left
    tail = own[..., half:] + got_left[..., :half] + got2_right
    return jnp.concatenate([head, tail], axis=-1)


def scatter_sum_direct(value, axis, count):
    me = lax.axis_index(axis)
    blocks = value.reshape((count, value.shape[0] // count) + value.shape[1:])
    total = lax.dynamic_index_in_dim(blocks, me, axis=0, keepdims=False)
    for s in range(1, count):
        piece = lax.dynamic_index_in_dim(blocks, (me + s) % count, axis=0, keepdims=False)
        sent = lax.ppermute(piece.astype(jnp.bfloat16), axis, shift_perm(count, s))
        total = total + sent.astype(jnp.float32)
    return total


def on_device(records, window_start, channel_segment, segment_row):
    tile_size = records.shape[0]
    block_count = records.shape[1] // NFFT
    sizes = {name: lax.axis_size(name) for name in ("x", "zl", "y", "zh", "core")}
    src_count = sizes["zh"] * sizes["core"]
    x_i, zl_i, y_i = lax.axis_index("x"), lax.axis_index("zl"), lax.axis_index("y")
    zh_i, core_i = lax.axis_index("zh"), lax.axis_index("core")
    group_index = (x_i * sizes["zl"] + zl_i) * sizes["y"] + y_i
    position = zh_i * sizes["core"] + core_i
    segment_total = segment_row.shape[0]

    blocks = records.reshape(tile_size * block_count, NFFT)
    spectrum = jnp.dot(
        blocks, dft_table(NFFT), precision=lax.Precision.HIGHEST, preferred_element_type=jnp.float32
    )
    white = whiten(spectrum).astype(jnp.bfloat16).reshape(tile_size, block_count, NFFT)
    start_row = jnp.zeros((1, block_count, NFFT), jnp.bfloat16).at[0, 0, 0].set(
        window_start[0].astype(jnp.bfloat16)
    )
    extended = jnp.concatenate([white, start_row], axis=0)
    gathered = gather_relative(extended, "zh", sizes["zh"])
    partner = lax.ppermute(gathered, "core", shift_perm(sizes["core"], 1))
    gathered = jnp.stack([gathered, partner]).reshape(src_count, tile_size + 1, block_count, NFFT)
    left = gathered[:, :tile_size]
    starts = gathered[:, tile_size, 0, 0].astype(jnp.int32)
    group_size = src_count * tile_size
    window_total = group_size // 4
    k_per = window_total // src_count

    slot = jnp.arange(src_count, dtype=jnp.int32)
    slot_zh = (zh_i - slot % sizes["zh"]) % sizes["zh"]
    slot_core = (core_i + slot // sizes["zh"]) % sizes["core"]
    slot_position = slot_zh * sizes["core"] + slot_core
    k_idx = position * k_per + jnp.arange(k_per, dtype=jnp.int32)
    window_idx = starts[:, None] + k_idx[None, :]
    tile_first = (slot_position * tile_size)[:, None]
    source_idx = jnp.where(window_idx < tile_first, window_idx, window_idx + tile_size)
    source_pos = source_idx // tile_size
    source_slot = ((source_pos % sizes["core"] - core_i) % sizes["core"]) * sizes["zh"] + (
        zh_i - source_pos // sizes["core"]
    ) % sizes["zh"]
    source_row = source_slot * (tile_size + 1) + source_idx % tile_size
    sources = jnp.take(
        gathered.reshape(src_count * (tile_size + 1), block_count, NFFT),
        source_row.reshape(-1),
        axis=0,
    ).reshape(src_count, k_per, block_count, NFFT)
    cross = cross_spectra(left, sources)
    flat_rows = cross.reshape(group_size * k_per, NFFT)
    correlation = jnp.dot(
        flat_rows, lag_table(NFFT, LAGS), preferred_element_type=jnp.float32
    ) / math.sqrt(block_count * NFFT // 2)
    correlation = correlation.astype(jnp.bfloat16).reshape(group_size, k_per * LAGS)

    channel_ids = (slot_position[:, None] * tile_size + jnp.arange(tile_size, dtype=jnp.int32)[None, :]).reshape(-1)
    group_segments = jnp.take(channel_segment, group_index * group_size + channel_ids)
    seg_match = group_segments[:, None] == jnp.arange(segment_total, dtype=jnp.int32)[None, :]
    group_rows = jnp.sum(jnp.where(seg_match, segment_row[None, :], 0), axis=1)
    staged_rows = group_rows
    onehot = (
        jnp.arange(segment_total, dtype=jnp.int32)[:, None] == staged_rows[None, :]
    ).astype(jnp.bfloat16)
    partial = jnp.dot(onehot, correlation, preferred_element_type=jnp.float32).reshape(
        segment_total, k_per, LAGS
    )
    owners = sizes["x"] * sizes["zl"] * sizes["y"]
    pieces = partial.astype(jnp.bfloat16).reshape((owners, partial.shape[0] // owners) + partial.shape[1:])
    arrived = lax.all_to_all(pieces, ("x", "zl", "y"), split_axis=0, concat_axis=0, tiled=True)
    summed = jnp.sum(arrived.astype(jnp.float32), axis=0)
    counts = row_counts(channel_segment, segment_row, group_index)
    return summed / jnp.sqrt(jnp.maximum(counts, 1.0))[:, None, None]


def solution(mesh):
    names = ("x", "zl", "y", "zh", "core")
    rcv_count, src_count = mesh.devices.shape
    zh_count = src_count // 2
    side = round(rcv_count ** (1 / 3))
    fine = Mesh(mesh.devices.reshape(side, side, rcv_count // side // side, zh_count, 2), names)
    rcv, src = ("x", "zl", "y"), ("zh", "core")
    in_specs = (P(rcv + src, None), P(rcv + src), P(), P())
    out_specs = P(rcv, src, None)
    return jax.shard_map(
        on_device, mesh=fine, in_specs=in_specs, out_specs=out_specs, check_vma=False
    )
```

```python
import math

import jax
import jax.numpy as jnp
from jax import lax
from jax.experimental import pallas as pl
from jax.experimental.pallas import tpu as pltpu
from jax.sharding import Mesh, PartitionSpec as P

NFFT = 1024
LAGS = 256
SEG_PER = 4


def dft_table(length):
    fine_count = 32
    coarse_count = length // fine_count
    frequency = jnp.arange(length // 2, dtype=jnp.int32)
    scale = 2.0 * math.pi / length

    def angle_table(steps, stride):
        index = (jnp.arange(steps, dtype=jnp.int32)[:, None] * stride * frequency[None, :]) % length
        angles = index.astype(jnp.float32) * scale
        return jnp.cos(angles), jnp.sin(angles)

    coarse_cos, coarse_sin = angle_table(coarse_count, fine_count)
    fine_cos, fine_sin = angle_table(fine_count, 1)
    cos_part = coarse_cos[:, None] * fine_cos[None] - coarse_sin[:, None] * fine_sin[None]
    sin_part = coarse_sin[:, None] * fine_cos[None] + coarse_cos[:, None] * fine_sin[None]
    return jnp.concatenate([cos_part, -sin_part], axis=-1).reshape(length, length)


def lag_table(length, lag_count):
    frequency = jnp.arange(length // 2, dtype=jnp.int32)
    shifts = jnp.arange(lag_count, dtype=jnp.int32) - lag_count // 2
    angles = (frequency[:, None] * shifts[None, :] % length).astype(jnp.float32) * (
        2.0 * math.pi / length
    )
    return jnp.concatenate([jnp.cos(angles), -jnp.sin(angles)], axis=0).astype(jnp.bfloat16)


def whiten(spectrum):
    half_size = spectrum.shape[-1] // 2
    powers = spectrum[..., :half_size] ** 2 + spectrum[..., half_size:] ** 2
    mean_power = jnp.mean(powers, axis=-1, keepdims=True)
    magnitude = jnp.sqrt(powers + 0.1 * mean_power + 1e-06)
    return spectrum / jnp.concatenate([magnitude, magnitude], axis=-1)


def correlate_kernel(left_ref, src_ref, lag_ref, out_ref, cross_ref):
    block_count, rows, width = left_ref.shape[1], left_ref.shape[2], left_ref.shape[3]
    k_count = src_ref.shape[2]
    half = width // 2
    left = [left_ref[0, b].astype(jnp.float32) for b in range(block_count)]
    source_rows = [src_ref[0, b].astype(jnp.float32) for b in range(block_count)]
    for k in range(k_count):
        real_part = None
        imag_part = None
        for b in range(block_count):
            source = source_rows[b][k:k + 1, :]
            l_re, l_im = left[b][:, :half], left[b][:, half:]
            s_re, s_im = source[:, :half], source[:, half:]
            re_term = l_re * s_re + l_im * s_im
            im_term = l_re * s_im - l_im * s_re
            real_part = re_term if real_part is None else real_part + re_term
            imag_part = im_term if imag_part is None else imag_part + im_term
        cross_ref[k * rows:(k + 1) * rows, :half] = real_part.astype(jnp.bfloat16)
        cross_ref[k * rows:(k + 1) * rows, half:] = imag_part.astype(jnp.bfloat16)
    product = jnp.dot(cross_ref[...], lag_ref[...], preferred_element_type=jnp.float32)
    out_ref[0] = (product / math.sqrt(block_count * half)).astype(out_ref.dtype)


def correlate(left, sources, lag_rows, rows):
    slots, block_count, _, width = left.shape
    k_count = sources.shape[2]
    lag_count = lag_rows.shape[1]
    flops = slots * k_count * rows * (block_count * width * 4 + 2 * width * lag_count)
    return pl.pallas_call(
        correlate_kernel,
        grid=(slots,),
        in_specs=[
            pl.BlockSpec((1, block_count, rows, width), lambda q: (q, 0, 0, 0)),
            pl.BlockSpec((1, block_count, k_count, width), lambda q: (q, 0, 0, 0)),
            pl.BlockSpec((width, lag_count), lambda q: (0, 0)),
        ],
        out_specs=pl.BlockSpec((1, k_count * rows, lag_count), lambda q: (q, 0, 0)),
        out_shape=jax.ShapeDtypeStruct((slots, k_count * rows, lag_count), jnp.bfloat16),
        scratch_shapes=[pltpu.VMEM((k_count * rows, width), jnp.bfloat16)],
        cost_estimate=pl.CostEstimate(
            flops=flops,
            bytes_accessed=2 * (left.size // left.shape[2] * rows + sources.size + lag_rows.size)
            + 2 * slots * k_count * rows * lag_count,
            transcendentals=0,
        ),
    )(left, sources, lag_rows)


def row_counts(channel_segment, segment_row, owner):
    held_rows = owner * SEG_PER + jnp.arange(SEG_PER, dtype=jnp.int32)
    matches = segment_row[None, :] == held_rows[:, None]
    segment_ids = jnp.arange(segment_row.shape[0], dtype=jnp.int32)
    held_segments = jnp.sum(jnp.where(matches, segment_ids[None, :], 0), axis=1)
    members = channel_segment[None, :] == held_segments[:, None]
    return jnp.sum(members.astype(jnp.float32), axis=1)


def shift_perm(count, shift):
    return [(i, (i + shift) % count) for i in range(count)]


def gather_relative(value, axis, count):
    if count != 4:
        parts = [value] + [lax.ppermute(value, axis, shift_perm(count, s)) for s in range(1, count)]
        return jnp.stack(parts)
    half = value.shape[-1] // 2
    from_left = lax.ppermute(value, axis, shift_perm(count, 1))
    from_right = lax.ppermute(value, axis, shift_perm(count, -1))
    far_head = lax.ppermute(from_left[..., :half], axis, shift_perm(count, 1))
    far_tail = lax.ppermute(from_right[..., half:], axis, shift_perm(count, -1))
    far = jnp.concatenate([far_head, far_tail], axis=-1)
    return jnp.stack([value, from_left, far, from_right])


def scatter_sum(value, axis, count):
    me = lax.axis_index(axis)
    blocks = value.reshape((count, value.shape[0] // count) + value.shape[1:])

    def block(offset):
        return lax.dynamic_index_in_dim(blocks, (me + offset) % count, axis=0, keepdims=False)

    if count != 4:
        total = block(0)
        for s in range(1, count):
            total = total + lax.ppermute(block(s), axis, shift_perm(count, s))
        return total
    half = blocks.shape[-1] // 2
    right, left, far, own = block(1), block(-1), block(2), block(0)
    to_right = jnp.concatenate([right[..., half:], far[..., :half]], axis=-1)
    to_left = jnp.concatenate([left[..., :half], far[..., half:]], axis=-1)
    got_left = lax.ppermute(to_right, axis, shift_perm(count, 1))
    got_right = lax.ppermute(to_left, axis, shift_perm(count, -1))
    fwd_right = right[..., :half] + got_left[..., half:]
    fwd_left = left[..., half:] + got_right[..., half:]
    got2_left = lax.ppermute(fwd_right, axis, shift_perm(count, 1))
    got2_right = lax.ppermute(fwd_left, axis, shift_perm(count, -1))
    head = own[..., :half] + got_right[..., :half] + got2_left
    tail = own[..., half:] + got_left[..., :half] + got2_right
    return jnp.concatenate([head, tail], axis=-1)


def scatter_sum_direct(value, axis, count):
    me = lax.axis_index(axis)
    blocks = value.reshape((count, value.shape[0] // count) + value.shape[1:])
    total = lax.dynamic_index_in_dim(blocks, me, axis=0, keepdims=False)
    for s in range(1, count):
        piece = lax.dynamic_index_in_dim(blocks, (me + s) % count, axis=0, keepdims=False)
        sent = lax.ppermute(piece.astype(jnp.bfloat16), axis, shift_perm(count, s))
        total = total + sent.astype(jnp.float32)
    return total


def on_device(records, window_start, channel_segment, segment_row):
    tile_size = records.shape[0]
    block_count = records.shape[1] // NFFT
    sizes = {name: lax.axis_size(name) for name in ("x", "zl", "y", "zh", "core")}
    src_count = sizes["zh"] * sizes["core"]
    x_i, zl_i, y_i = lax.axis_index("x"), lax.axis_index("zl"), lax.axis_index("y")
    zh_i, core_i = lax.axis_index("zh"), lax.axis_index("core")
    group_index = (x_i * sizes["zl"] + zl_i) * sizes["y"] + y_i
    position = zh_i * sizes["core"] + core_i
    segment_total = segment_row.shape[0]

    blocks = records.reshape(tile_size * block_count, NFFT)
    spectrum = jnp.dot(
        blocks, dft_table(NFFT), precision=lax.Precision.HIGHEST, preferred_element_type=jnp.float32
    )
    white = whiten(spectrum).astype(jnp.bfloat16).reshape(tile_size, block_count, NFFT)
    start_row = jnp.zeros((1, block_count, NFFT), jnp.bfloat16).at[0, 0, 0].set(
        window_start[0].astype(jnp.bfloat16)
    )
    extended = jnp.concatenate([white, start_row], axis=0).transpose(1, 0, 2)
    gathered = gather_relative(extended, "zh", sizes["zh"])
    partner = lax.ppermute(gathered, "core", shift_perm(sizes["core"], 1))
    gathered = jnp.stack([gathered, partner]).reshape(src_count, block_count, tile_size + 1, NFFT)
    starts = gathered[:, 0, tile_size, 0].astype(jnp.int32)
    group_size = src_count * tile_size
    window_total = group_size // 4
    k_per = window_total // src_count

    slot = jnp.arange(src_count, dtype=jnp.int32)
    slot_zh = (zh_i - slot % sizes["zh"]) % sizes["zh"]
    slot_core = (core_i + slot // sizes["zh"]) % sizes["core"]
    slot_position = slot_zh * sizes["core"] + slot_core
    k_idx = position * k_per + jnp.arange(k_per, dtype=jnp.int32)
    window_idx = starts[:, None] + k_idx[None, :]
    tile_first = (slot_position * tile_size)[:, None]
    source_idx = jnp.where(window_idx < tile_first, window_idx, window_idx + tile_size)
    source_pos = source_idx // tile_size
    source_slot = ((source_pos % sizes["core"] - core_i) % sizes["core"]) * sizes["zh"] + (
        zh_i - source_pos // sizes["core"]
    ) % sizes["zh"]
    block_ids = jnp.arange(block_count, dtype=jnp.int32)
    sources = gathered[
        source_slot[:, None, :], block_ids[None, :, None], (source_idx % tile_size)[:, None, :]
    ]
    correlation = correlate(gathered, sources, lag_table(NFFT, LAGS), tile_size)
    correlation = correlation.reshape(src_count, k_per, tile_size, LAGS)

    channel_ids = (slot_position[:, None] * tile_size + jnp.arange(tile_size, dtype=jnp.int32)[None, :]).reshape(-1)
    group_segments = jnp.take(channel_segment, group_index * group_size + channel_ids)
    seg_match = group_segments[:, None] == jnp.arange(segment_total, dtype=jnp.int32)[None, :]
    group_rows = jnp.sum(jnp.where(seg_match, segment_row[None, :], 0), axis=1)
    staged_rows = group_rows
    onehot = (
        jnp.arange(segment_total, dtype=jnp.int32)[:, None] == staged_rows[None, :]
    ).astype(jnp.bfloat16)
    onehot = onehot.reshape(segment_total, src_count, tile_size)
    partial = jnp.einsum("rqi,qkim->rkm", onehot, correlation, preferred_element_type=jnp.float32)
    owners = sizes["x"] * sizes["zl"] * sizes["y"]
    pieces = partial.astype(jnp.bfloat16).reshape((owners, partial.shape[0] // owners) + partial.shape[1:])
    arrived = lax.all_to_all(pieces, ("x", "zl", "y"), split_axis=0, concat_axis=0, tiled=True)
    summed = jnp.sum(arrived.astype(jnp.float32), axis=0)
    counts = row_counts(channel_segment, segment_row, group_index)
    return summed / jnp.sqrt(jnp.maximum(counts, 1.0))[:, None, None]


def solution(mesh):
    names = ("x", "zl", "y", "zh", "core")
    rcv_count, src_count = mesh.devices.shape
    zh_count = src_count // 2
    side = round(rcv_count ** (1 / 3))
    fine = Mesh(mesh.devices.reshape(side, side, rcv_count // side // side, zh_count, 2), names)
    rcv, src = ("x", "zl", "y"), ("zh", "core")
    in_specs = (P(rcv + src, None), P(rcv + src), P(), P())
    out_specs = P(rcv, src, None)
    return jax.shard_map(
        on_device, mesh=fine, in_specs=in_specs, out_specs=out_specs, check_vma=False
    )
```

```python
import math

import jax
import jax.numpy as jnp
from jax import lax
from jax.experimental import pallas as pl
from jax.experimental.pallas import tpu as pltpu
from jax.sharding import Mesh, PartitionSpec as P

NFFT = 1024
LAGS = 256
SEG_PER = 4


def dft_table(length):
    fine_count = 32
    coarse_count = length // fine_count
    frequency = jnp.arange(length // 2, dtype=jnp.int32)
    scale = 2.0 * math.pi / length

    def angle_table(steps, stride):
        index = (jnp.arange(steps, dtype=jnp.int32)[:, None] * stride * frequency[None, :]) % length
        angles = index.astype(jnp.float32) * scale
        return jnp.cos(angles), jnp.sin(angles)

    coarse_cos, coarse_sin = angle_table(coarse_count, fine_count)
    fine_cos, fine_sin = angle_table(fine_count, 1)
    cos_part = coarse_cos[:, None] * fine_cos[None] - coarse_sin[:, None] * fine_sin[None]
    sin_part = coarse_sin[:, None] * fine_cos[None] + coarse_cos[:, None] * fine_sin[None]
    return jnp.concatenate([cos_part, -sin_part], axis=-1).reshape(length, length)


def lag_table(length, lag_count):
    frequency = jnp.arange(length // 2, dtype=jnp.int32)
    shifts = jnp.arange(lag_count, dtype=jnp.int32) - lag_count // 2
    angles = (frequency[:, None] * shifts[None, :] % length).astype(jnp.float32) * (
        2.0 * math.pi / length
    )
    return jnp.concatenate([jnp.cos(angles), -jnp.sin(angles)], axis=0).astype(jnp.bfloat16)


def whiten(spectrum):
    half_size = spectrum.shape[-1] // 2
    powers = spectrum[..., :half_size] ** 2 + spectrum[..., half_size:] ** 2
    mean_power = jnp.mean(powers, axis=-1, keepdims=True)
    magnitude = jnp.sqrt(powers + 0.1 * mean_power + 1e-06)
    return spectrum / jnp.concatenate([magnitude, magnitude], axis=-1)


def correlate_kernel(left_ref, src_ref, lag_ref, out_ref, cross_ref):
    block_count, rows, width = left_ref.shape[1], left_ref.shape[2], left_ref.shape[3]
    k_count = src_ref.shape[2]
    half = width // 2
    left = [left_ref[0, b].astype(jnp.float32) for b in range(block_count)]
    source_rows = [src_ref[0, b].astype(jnp.float32) for b in range(block_count)]
    for k in range(k_count):
        real_part = None
        imag_part = None
        for b in range(block_count):
            source = source_rows[b][k:k + 1, :]
            l_re, l_im = left[b][:, :half], left[b][:, half:]
            s_re, s_im = source[:, :half], source[:, half:]
            re_term = l_re * s_re + l_im * s_im
            im_term = l_re * s_im - l_im * s_re
            real_part = re_term if real_part is None else real_part + re_term
            imag_part = im_term if imag_part is None else imag_part + im_term
        cross_ref[k * rows:(k + 1) * rows, :half] = real_part.astype(jnp.bfloat16)
        cross_ref[k * rows:(k + 1) * rows, half:] = imag_part.astype(jnp.bfloat16)
    product = jnp.dot(cross_ref[...], lag_ref[...], preferred_element_type=jnp.float32)
    out_ref[0] = (product / math.sqrt(block_count * half)).astype(out_ref.dtype)


def correlate(left, sources, lag_rows, rows):
    slots, block_count, _, width = left.shape
    k_count = sources.shape[2]
    lag_count = lag_rows.shape[1]
    flops = slots * k_count * rows * (block_count * width * 4 + 2 * width * lag_count)
    return pl.pallas_call(
        correlate_kernel,
        grid=(slots,),
        in_specs=[
            pl.BlockSpec((1, block_count, rows, width), lambda q: (q, 0, 0, 0)),
            pl.BlockSpec((1, block_count, k_count, width), lambda q: (q, 0, 0, 0)),
            pl.BlockSpec((width, lag_count), lambda q: (0, 0)),
        ],
        out_specs=pl.BlockSpec((1, k_count * rows, lag_count), lambda q: (q, 0, 0)),
        out_shape=jax.ShapeDtypeStruct((slots, k_count * rows, lag_count), jnp.bfloat16),
        scratch_shapes=[pltpu.VMEM((k_count * rows, width), jnp.bfloat16)],
        cost_estimate=pl.CostEstimate(
            flops=flops,
            bytes_accessed=2 * (left.size // left.shape[2] * rows + sources.size + lag_rows.size)
            + 2 * slots * k_count * rows * lag_count,
            transcendentals=0,
        ),
    )(left, sources, lag_rows)


def row_counts(channel_segment, segment_row, owner):
    held_rows = owner * SEG_PER + jnp.arange(SEG_PER, dtype=jnp.int32)
    matches = segment_row[None, :] == held_rows[:, None]
    segment_ids = jnp.arange(segment_row.shape[0], dtype=jnp.int32)
    held_segments = jnp.sum(jnp.where(matches, segment_ids[None, :], 0), axis=1)
    members = channel_segment[None, :] == held_segments[:, None]
    return jnp.sum(members.astype(jnp.float32), axis=1)


def shift_perm(count, shift):
    return [(i, (i + shift) % count) for i in range(count)]


def gather_relative(value, axis, count):
    if count != 4:
        parts = [value] + [lax.ppermute(value, axis, shift_perm(count, s)) for s in range(1, count)]
        return jnp.stack(parts)
    half = value.shape[-1] // 2
    from_left = lax.ppermute(value, axis, shift_perm(count, 1))
    from_right = lax.ppermute(value, axis, shift_perm(count, -1))
    far_head = lax.ppermute(from_left[..., :half], axis, shift_perm(count, 1))
    far_tail = lax.ppermute(from_right[..., half:], axis, shift_perm(count, -1))
    far = jnp.concatenate([far_head, far_tail], axis=-1)
    return jnp.stack([value, from_left, far, from_right])


def scatter_sum(value, axis, count):
    me = lax.axis_index(axis)
    blocks = value.reshape((count, value.shape[0] // count) + value.shape[1:])

    def block(offset):
        return lax.dynamic_index_in_dim(blocks, (me + offset) % count, axis=0, keepdims=False)

    if count != 4:
        total = block(0)
        for s in range(1, count):
            total = total + lax.ppermute(block(s), axis, shift_perm(count, s))
        return total
    half = blocks.shape[-1] // 2
    right, left, far, own = block(1), block(-1), block(2), block(0)
    to_right = jnp.concatenate([right[..., half:], far[..., :half]], axis=-1)
    to_left = jnp.concatenate([left[..., :half], far[..., half:]], axis=-1)
    got_left = lax.ppermute(to_right, axis, shift_perm(count, 1))
    got_right = lax.ppermute(to_left, axis, shift_perm(count, -1))
    fwd_right = right[..., :half] + got_left[..., half:]
    fwd_left = left[..., half:] + got_right[..., half:]
    got2_left = lax.ppermute(fwd_right, axis, shift_perm(count, 1))
    got2_right = lax.ppermute(fwd_left, axis, shift_perm(count, -1))
    head = own[..., :half] + got_right[..., :half] + got2_left
    tail = own[..., half:] + got_left[..., :half] + got2_right
    return jnp.concatenate([head, tail], axis=-1)


def scatter_sum_direct(value, axis, count):
    me = lax.axis_index(axis)
    blocks = value.reshape((count, value.shape[0] // count) + value.shape[1:])
    total = lax.dynamic_index_in_dim(blocks, me, axis=0, keepdims=False)
    for s in range(1, count):
        piece = lax.dynamic_index_in_dim(blocks, (me + s) % count, axis=0, keepdims=False)
        sent = lax.ppermute(piece.astype(jnp.bfloat16), axis, shift_perm(count, s))
        total = total + sent.astype(jnp.float32)
    return total


def on_device(records, window_start, channel_segment, segment_row):
    tile_size = records.shape[0]
    block_count = records.shape[1] // NFFT
    sizes = {name: lax.axis_size(name) for name in ("x", "zl", "y", "zh", "core")}
    src_count = sizes["zh"] * sizes["core"]
    x_i, zl_i, y_i = lax.axis_index("x"), lax.axis_index("zl"), lax.axis_index("y")
    zh_i, core_i = lax.axis_index("zh"), lax.axis_index("core")
    group_index = (x_i * sizes["zl"] + zl_i) * sizes["y"] + y_i
    position = zh_i * sizes["core"] + core_i
    segment_total = segment_row.shape[0]

    blocks = records.reshape(tile_size * block_count, NFFT)
    spectrum = jnp.dot(
        blocks, dft_table(NFFT), precision=lax.Precision.HIGHEST, preferred_element_type=jnp.float32
    )
    white = whiten(spectrum).astype(jnp.bfloat16).reshape(tile_size, block_count, NFFT)
    start_row = jnp.zeros((1, block_count, NFFT), jnp.bfloat16).at[0, 0, 0].set(
        window_start[0].astype(jnp.bfloat16)
    )
    extended = jnp.concatenate([white, start_row], axis=0).transpose(1, 0, 2)
    gathered = gather_relative(extended, "zh", sizes["zh"])
    partner = lax.ppermute(gathered, "core", shift_perm(sizes["core"], 1))
    gathered = jnp.stack([gathered, partner]).reshape(src_count, block_count, tile_size + 1, NFFT)
    starts = gathered[:, 0, tile_size, 0].astype(jnp.int32)
    group_size = src_count * tile_size
    window_total = group_size // 4
    k_per = window_total // src_count

    slot = jnp.arange(src_count, dtype=jnp.int32)
    slot_zh = (zh_i - slot % sizes["zh"]) % sizes["zh"]
    slot_core = (core_i + slot // sizes["zh"]) % sizes["core"]
    slot_position = slot_zh * sizes["core"] + slot_core
    k_idx = position * k_per + jnp.arange(k_per, dtype=jnp.int32)
    window_idx = starts[:, None] + k_idx[None, :]
    tile_first = (slot_position * tile_size)[:, None]
    source_idx = jnp.where(window_idx < tile_first, window_idx, window_idx + tile_size)
    source_pos = source_idx // tile_size
    source_slot = ((source_pos % sizes["core"] - core_i) % sizes["core"]) * sizes["zh"] + (
        zh_i - source_pos // sizes["core"]
    ) % sizes["zh"]
    source_row = (source_slot * (tile_size + 1) + source_idx % tile_size).reshape(-1)
    sources = jnp.stack(
        [
            jnp.take(gathered[:, b].reshape(-1, NFFT), source_row, axis=0).reshape(
                src_count, k_per, NFFT
            )
            for b in range(block_count)
        ],
        axis=1,
    )
    correlation = correlate(gathered, sources, lag_table(NFFT, LAGS), tile_size)
    correlation = correlation.reshape(src_count, k_per, tile_size, LAGS)

    channel_ids = (slot_position[:, None] * tile_size + jnp.arange(tile_size, dtype=jnp.int32)[None, :]).reshape(-1)
    group_segments = jnp.take(channel_segment, group_index * group_size + channel_ids)
    seg_match = group_segments[:, None] == jnp.arange(segment_total, dtype=jnp.int32)[None, :]
    group_rows = jnp.sum(jnp.where(seg_match, segment_row[None, :], 0), axis=1)
    staged_rows = group_rows
    onehot = (
        jnp.arange(segment_total, dtype=jnp.int32)[:, None] == staged_rows[None, :]
    ).astype(jnp.bfloat16)
    onehot = onehot.reshape(segment_total, src_count, tile_size)
    partial = jnp.einsum("rqi,qkim->rkm", onehot, correlation, preferred_element_type=jnp.float32)
    owners = sizes["x"] * sizes["zl"] * sizes["y"]
    pieces = partial.astype(jnp.bfloat16).reshape((owners, partial.shape[0] // owners) + partial.shape[1:])
    arrived = lax.all_to_all(pieces, ("x", "zl", "y"), split_axis=0, concat_axis=0, tiled=True)
    summed = jnp.sum(arrived.astype(jnp.float32), axis=0)
    counts = row_counts(channel_segment, segment_row, group_index)
    return summed / jnp.sqrt(jnp.maximum(counts, 1.0))[:, None, None]


def solution(mesh):
    names = ("x", "zl", "y", "zh", "core")
    rcv_count, src_count = mesh.devices.shape
    zh_count = src_count // 2
    side = round(rcv_count ** (1 / 3))
    fine = Mesh(mesh.devices.reshape(side, side, rcv_count // side // side, zh_count, 2), names)
    rcv, src = ("x", "zl", "y"), ("zh", "core")
    in_specs = (P(rcv + src, None), P(rcv + src), P(), P())
    out_specs = P(rcv, src, None)
    return jax.shard_map(
        on_device, mesh=fine, in_specs=in_specs, out_specs=out_specs, check_vma=False
    )
```

```python
import math

import jax
import jax.numpy as jnp
from jax import lax
from jax.experimental import pallas as pl
from jax.experimental.pallas import tpu as pltpu
from jax.sharding import Mesh, PartitionSpec as P

NFFT = 1024
LAGS = 256
SEG_PER = 4


def dft_table(length):
    fine_count = 32
    coarse_count = length // fine_count
    frequency = jnp.arange(length // 2, dtype=jnp.int32)
    scale = 2.0 * math.pi / length

    def angle_table(steps, stride):
        index = (jnp.arange(steps, dtype=jnp.int32)[:, None] * stride * frequency[None, :]) % length
        angles = index.astype(jnp.float32) * scale
        return jnp.cos(angles), jnp.sin(angles)

    coarse_cos, coarse_sin = angle_table(coarse_count, fine_count)
    fine_cos, fine_sin = angle_table(fine_count, 1)
    cos_part = coarse_cos[:, None] * fine_cos[None] - coarse_sin[:, None] * fine_sin[None]
    sin_part = coarse_sin[:, None] * fine_cos[None] + coarse_cos[:, None] * fine_sin[None]
    return jnp.concatenate([cos_part, -sin_part], axis=-1).reshape(length, length)


def lag_table(length, lag_count):
    frequency = jnp.arange(length // 2, dtype=jnp.int32)
    shifts = jnp.arange(lag_count, dtype=jnp.int32) - lag_count // 2
    angles = (frequency[:, None] * shifts[None, :] % length).astype(jnp.float32) * (
        2.0 * math.pi / length
    )
    return jnp.concatenate([jnp.cos(angles), -jnp.sin(angles)], axis=0).astype(jnp.bfloat16)


def whiten(spectrum):
    half_size = spectrum.shape[-1] // 2
    powers = spectrum[..., :half_size] ** 2 + spectrum[..., half_size:] ** 2
    mean_power = jnp.mean(powers, axis=-1, keepdims=True)
    magnitude = jnp.sqrt(powers + 0.1 * mean_power + 1e-06)
    return spectrum / jnp.concatenate([magnitude, magnitude], axis=-1)


def correlate_kernel(left_ref, src_ref, lag_ref, out_ref, cross_ref):
    block_count, rows, width = left_ref.shape[1], left_ref.shape[2], left_ref.shape[3]
    k_count = src_ref.shape[2]
    half = width // 2
    left = [left_ref[0, b].astype(jnp.float32) for b in range(block_count)]
    source_rows = [src_ref[0, b].astype(jnp.float32) for b in range(block_count)]
    for k in range(k_count):
        real_part = None
        imag_part = None
        for b in range(block_count):
            source = source_rows[b][k:k + 1, :]
            l_re, l_im = left[b][:, :half], left[b][:, half:]
            s_re, s_im = source[:, :half], source[:, half:]
            re_term = l_re * s_re + l_im * s_im
            im_term = l_re * s_im - l_im * s_re
            real_part = re_term if real_part is None else real_part + re_term
            imag_part = im_term if imag_part is None else imag_part + im_term
        cross_ref[k * rows:(k + 1) * rows, :half] = real_part.astype(jnp.bfloat16)
        cross_ref[k * rows:(k + 1) * rows, half:] = imag_part.astype(jnp.bfloat16)
    product = jnp.dot(cross_ref[...], lag_ref[...], preferred_element_type=jnp.float32)
    out_ref[0] = (product / math.sqrt(block_count * half)).astype(out_ref.dtype)


def correlate(left, sources, lag_rows, rows):
    slots, block_count, _, width = left.shape
    k_count = sources.shape[2]
    lag_count = lag_rows.shape[1]
    flops = slots * k_count * rows * (block_count * width * 4 + 2 * width * lag_count)
    return pl.pallas_call(
        correlate_kernel,
        grid=(slots,),
        in_specs=[
            pl.BlockSpec((1, block_count, rows, width), lambda q: (q, 0, 0, 0)),
            pl.BlockSpec((1, block_count, k_count, width), lambda q: (q, 0, 0, 0)),
            pl.BlockSpec((width, lag_count), lambda q: (0, 0)),
        ],
        out_specs=pl.BlockSpec((1, k_count * rows, lag_count), lambda q: (q, 0, 0)),
        out_shape=jax.ShapeDtypeStruct((slots, k_count * rows, lag_count), jnp.bfloat16),
        scratch_shapes=[pltpu.VMEM((k_count * rows, width), jnp.bfloat16)],
        cost_estimate=pl.CostEstimate(
            flops=flops,
            bytes_accessed=2 * (left.size // left.shape[2] * rows + sources.size + lag_rows.size)
            + 2 * slots * k_count * rows * lag_count,
            transcendentals=0,
        ),
    )(left, sources, lag_rows)


def row_counts(channel_segment, segment_row, owner):
    held_rows = owner * SEG_PER + jnp.arange(SEG_PER, dtype=jnp.int32)
    matches = segment_row[None, :] == held_rows[:, None]
    segment_ids = jnp.arange(segment_row.shape[0], dtype=jnp.int32)
    held_segments = jnp.sum(jnp.where(matches, segment_ids[None, :], 0), axis=1)
    members = channel_segment[None, :] == held_segments[:, None]
    return jnp.sum(members.astype(jnp.float32), axis=1)


def shift_perm(count, shift):
    return [(i, (i + shift) % count) for i in range(count)]


def gather_relative(value, axis, count):
    if count != 4:
        parts = [value] + [lax.ppermute(value, axis, shift_perm(count, s)) for s in range(1, count)]
        return jnp.stack(parts)
    half = value.shape[-1] // 2
    from_left = lax.ppermute(value, axis, shift_perm(count, 1))
    from_right = lax.ppermute(value, axis, shift_perm(count, -1))
    far_head = lax.ppermute(from_left[..., :half], axis, shift_perm(count, 1))
    far_tail = lax.ppermute(from_right[..., half:], axis, shift_perm(count, -1))
    far = jnp.concatenate([far_head, far_tail], axis=-1)
    return jnp.stack([value, from_left, far, from_right])


def scatter_sum(value, axis, count):
    me = lax.axis_index(axis)
    blocks = value.reshape((count, value.shape[0] // count) + value.shape[1:])

    def block(offset):
        return lax.dynamic_index_in_dim(blocks, (me + offset) % count, axis=0, keepdims=False)

    if count != 4:
        total = block(0)
        for s in range(1, count):
            total = total + lax.ppermute(block(s), axis, shift_perm(count, s))
        return total
    half = blocks.shape[-1] // 2
    right, left, far, own = block(1), block(-1), block(2), block(0)
    to_right = jnp.concatenate([right[..., half:], far[..., :half]], axis=-1)
    to_left = jnp.concatenate([left[..., :half], far[..., half:]], axis=-1)
    got_left = lax.ppermute(to_right, axis, shift_perm(count, 1))
    got_right = lax.ppermute(to_left, axis, shift_perm(count, -1))
    fwd_right = right[..., :half] + got_left[..., half:]
    fwd_left = left[..., half:] + got_right[..., half:]
    got2_left = lax.ppermute(fwd_right, axis, shift_perm(count, 1))
    got2_right = lax.ppermute(fwd_left, axis, shift_perm(count, -1))
    head = own[..., :half] + got_right[..., :half] + got2_left
    tail = own[..., half:] + got_left[..., :half] + got2_right
    return jnp.concatenate([head, tail], axis=-1)


def scatter_sum_direct(value, axis, count):
    me = lax.axis_index(axis)
    blocks = value.reshape((count, value.shape[0] // count) + value.shape[1:])
    total = lax.dynamic_index_in_dim(blocks, me, axis=0, keepdims=False)
    for s in range(1, count):
        piece = lax.dynamic_index_in_dim(blocks, (me + s) % count, axis=0, keepdims=False)
        sent = lax.ppermute(piece.astype(jnp.bfloat16), axis, shift_perm(count, s))
        total = total + sent.astype(jnp.float32)
    return total


def on_device(records, window_start, channel_segment, segment_row):
    tile_size = records.shape[0]
    block_count = records.shape[1] // NFFT
    sizes = {name: lax.axis_size(name) for name in ("x", "zl", "y", "zh", "core")}
    src_count = sizes["zh"] * sizes["core"]
    x_i, zl_i, y_i = lax.axis_index("x"), lax.axis_index("zl"), lax.axis_index("y")
    zh_i, core_i = lax.axis_index("zh"), lax.axis_index("core")
    group_index = (x_i * sizes["zl"] + zl_i) * sizes["y"] + y_i
    position = zh_i * sizes["core"] + core_i
    segment_total = segment_row.shape[0]

    blocks = records.reshape(tile_size * block_count, NFFT)
    spectrum = jnp.dot(
        blocks, dft_table(NFFT), precision=lax.Precision.HIGHEST, preferred_element_type=jnp.float32
    )
    white = whiten(spectrum).astype(jnp.bfloat16).reshape(tile_size, block_count, NFFT)
    start_row = jnp.zeros((1, block_count, NFFT), jnp.bfloat16).at[0, 0, 0].set(
        window_start[0].astype(jnp.bfloat16)
    )
    extended = jnp.concatenate([white, start_row], axis=0).transpose(1, 0, 2)
    half = NFFT // 2
    offload = lax.all_gather(extended[..., :half], "zh", axis=0)
    offload = jnp.take(offload, (zh_i - jnp.arange(sizes["zh"], dtype=jnp.int32)) % sizes["zh"], axis=0)
    ring = gather_relative(extended[..., half:], "zh", sizes["zh"])
    gathered = jnp.concatenate([offload, ring], axis=-1)
    partner = lax.ppermute(gathered, "core", shift_perm(sizes["core"], 1))
    gathered = jnp.stack([gathered, partner]).reshape(src_count, block_count, tile_size + 1, NFFT)
    starts = gathered[:, 0, tile_size, 0].astype(jnp.int32)
    group_size = src_count * tile_size
    window_total = group_size // 4
    k_per = window_total // src_count

    slot = jnp.arange(src_count, dtype=jnp.int32)
    slot_zh = (zh_i - slot % sizes["zh"]) % sizes["zh"]
    slot_core = (core_i + slot // sizes["zh"]) % sizes["core"]
    slot_position = slot_zh * sizes["core"] + slot_core
    k_idx = position * k_per + jnp.arange(k_per, dtype=jnp.int32)
    window_idx = starts[:, None] + k_idx[None, :]
    tile_first = (slot_position * tile_size)[:, None]
    source_idx = jnp.where(window_idx < tile_first, window_idx, window_idx + tile_size)
    source_pos = source_idx // tile_size
    source_slot = ((source_pos % sizes["core"] - core_i) % sizes["core"]) * sizes["zh"] + (
        zh_i - source_pos // sizes["core"]
    ) % sizes["zh"]
    source_row = (source_slot * (tile_size + 1) + source_idx % tile_size).reshape(-1)
    sources = jnp.stack(
        [
            jnp.take(gathered[:, b].reshape(-1, NFFT), source_row, axis=0).reshape(
                src_count, k_per, NFFT
            )
            for b in range(block_count)
        ],
        axis=1,
    )
    correlation = correlate(gathered, sources, lag_table(NFFT, LAGS), tile_size)
    correlation = correlation.reshape(src_count, k_per, tile_size, LAGS)

    channel_ids = (slot_position[:, None] * tile_size + jnp.arange(tile_size, dtype=jnp.int32)[None, :]).reshape(-1)
    group_segments = jnp.take(channel_segment, group_index * group_size + channel_ids)
    seg_match = group_segments[:, None] == jnp.arange(segment_total, dtype=jnp.int32)[None, :]
    group_rows = jnp.sum(jnp.where(seg_match, segment_row[None, :], 0), axis=1)
    staged_rows = group_rows
    onehot = (
        jnp.arange(segment_total, dtype=jnp.int32)[:, None] == staged_rows[None, :]
    ).astype(jnp.bfloat16)
    onehot = onehot.reshape(segment_total, src_count, tile_size)
    partial = jnp.einsum("rqi,qkim->rkm", onehot, correlation, preferred_element_type=jnp.float32)
    owners = sizes["x"] * sizes["zl"] * sizes["y"]
    pieces = partial.astype(jnp.bfloat16).reshape((owners, partial.shape[0] // owners) + partial.shape[1:])
    arrived = lax.all_to_all(pieces, ("x", "zl", "y"), split_axis=0, concat_axis=0, tiled=True)
    summed = jnp.sum(arrived.astype(jnp.float32), axis=0)
    counts = row_counts(channel_segment, segment_row, group_index)
    return summed / jnp.sqrt(jnp.maximum(counts, 1.0))[:, None, None]


def solution(mesh):
    names = ("x", "zl", "y", "zh", "core")
    rcv_count, src_count = mesh.devices.shape
    zh_count = src_count // 2
    side = round(rcv_count ** (1 / 3))
    fine = Mesh(mesh.devices.reshape(side, side, rcv_count // side // side, zh_count, 2), names)
    rcv, src = ("x", "zl", "y"), ("zh", "core")
    in_specs = (P(rcv + src, None), P(rcv + src), P(), P())
    out_specs = P(rcv, src, None)
    return jax.shard_map(
        on_device, mesh=fine, in_specs=in_specs, out_specs=out_specs, check_vma=False
    )
```

```python
import math

import jax
import jax.numpy as jnp
from jax import lax
from jax.experimental import pallas as pl
from jax.experimental.pallas import tpu as pltpu
from jax.sharding import Mesh, PartitionSpec as P

NFFT = 1024
LAGS = 256
SEG_PER = 4


def dft_table(length):
    fine_count = 32
    coarse_count = length // fine_count
    frequency = jnp.arange(length // 2, dtype=jnp.int32)
    scale = 2.0 * math.pi / length

    def angle_table(steps, stride):
        index = (jnp.arange(steps, dtype=jnp.int32)[:, None] * stride * frequency[None, :]) % length
        angles = index.astype(jnp.float32) * scale
        return jnp.cos(angles), jnp.sin(angles)

    coarse_cos, coarse_sin = angle_table(coarse_count, fine_count)
    fine_cos, fine_sin = angle_table(fine_count, 1)
    cos_part = coarse_cos[:, None] * fine_cos[None] - coarse_sin[:, None] * fine_sin[None]
    sin_part = coarse_sin[:, None] * fine_cos[None] + coarse_cos[:, None] * fine_sin[None]
    return jnp.concatenate([cos_part, -sin_part], axis=-1).reshape(length, length)


def lag_table(length, lag_count):
    frequency = jnp.arange(length // 2, dtype=jnp.int32)
    shifts = jnp.arange(lag_count, dtype=jnp.int32) - lag_count // 2
    angles = (frequency[:, None] * shifts[None, :] % length).astype(jnp.float32) * (
        2.0 * math.pi / length
    )
    return jnp.concatenate([jnp.cos(angles), -jnp.sin(angles)], axis=0).astype(jnp.bfloat16)


def whiten(spectrum):
    half_size = spectrum.shape[-1] // 2
    powers = spectrum[..., :half_size] ** 2 + spectrum[..., half_size:] ** 2
    mean_power = jnp.mean(powers, axis=-1, keepdims=True)
    magnitude = jnp.sqrt(powers + 0.1 * mean_power + 1e-06)
    return spectrum / jnp.concatenate([magnitude, magnitude], axis=-1)


def correlate_kernel(left_ref, src_ref, lag_ref, out_ref, cross_ref):
    block_count, rows, width = left_ref.shape[1], left_ref.shape[2], left_ref.shape[3]
    k_count = src_ref.shape[2]
    half = width // 2
    left = [left_ref[0, b].astype(jnp.float32) for b in range(block_count)]
    source_rows = [src_ref[0, b].astype(jnp.float32) for b in range(block_count)]
    for k in range(k_count):
        real_part = None
        imag_part = None
        for b in range(block_count):
            source = source_rows[b][k:k + 1, :]
            l_re, l_im = left[b][:, :half], left[b][:, half:]
            s_re, s_im = source[:, :half], source[:, half:]
            re_term = l_re * s_re + l_im * s_im
            im_term = l_re * s_im - l_im * s_re
            real_part = re_term if real_part is None else real_part + re_term
            imag_part = im_term if imag_part is None else imag_part + im_term
        cross_ref[k * rows:(k + 1) * rows, :half] = real_part.astype(jnp.bfloat16)
        cross_ref[k * rows:(k + 1) * rows, half:] = imag_part.astype(jnp.bfloat16)
    product = jnp.dot(cross_ref[...], lag_ref[...], preferred_element_type=jnp.float32)
    out_ref[0] = (product / math.sqrt(block_count * half)).astype(out_ref.dtype)


def correlate(left, sources, lag_rows, rows):
    slots, block_count, _, width = left.shape
    k_count = sources.shape[2]
    lag_count = lag_rows.shape[1]
    flops = slots * k_count * rows * (block_count * width * 4 + 2 * width * lag_count)
    return pl.pallas_call(
        correlate_kernel,
        grid=(slots,),
        in_specs=[
            pl.BlockSpec((1, block_count, rows, width), lambda q: (q, 0, 0, 0)),
            pl.BlockSpec((1, block_count, k_count, width), lambda q: (q, 0, 0, 0)),
            pl.BlockSpec((width, lag_count), lambda q: (0, 0)),
        ],
        out_specs=pl.BlockSpec((1, k_count * rows, lag_count), lambda q: (q, 0, 0)),
        out_shape=jax.ShapeDtypeStruct((slots, k_count * rows, lag_count), jnp.bfloat16),
        scratch_shapes=[pltpu.VMEM((k_count * rows, width), jnp.bfloat16)],
        cost_estimate=pl.CostEstimate(
            flops=flops,
            bytes_accessed=2 * (left.size // left.shape[2] * rows + sources.size + lag_rows.size)
            + 2 * slots * k_count * rows * lag_count,
            transcendentals=0,
        ),
    )(left, sources, lag_rows)


def row_counts(channel_segment, segment_row, owner):
    held_rows = owner * SEG_PER + jnp.arange(SEG_PER, dtype=jnp.int32)
    matches = segment_row[None, :] == held_rows[:, None]
    segment_ids = jnp.arange(segment_row.shape[0], dtype=jnp.int32)
    held_segments = jnp.sum(jnp.where(matches, segment_ids[None, :], 0), axis=1)
    members = channel_segment[None, :] == held_segments[:, None]
    return jnp.sum(members.astype(jnp.float32), axis=1)


def shift_perm(count, shift):
    return [(i, (i + shift) % count) for i in range(count)]


def gather_relative(value, axis, count):
    if count != 4:
        parts = [value] + [lax.ppermute(value, axis, shift_perm(count, s)) for s in range(1, count)]
        return jnp.stack(parts)
    half = value.shape[-1] // 2
    from_left = lax.ppermute(value, axis, shift_perm(count, 1))
    from_right = lax.ppermute(value, axis, shift_perm(count, -1))
    far_head = lax.ppermute(from_left[..., :half], axis, shift_perm(count, 1))
    far_tail = lax.ppermute(from_right[..., half:], axis, shift_perm(count, -1))
    far = jnp.concatenate([far_head, far_tail], axis=-1)
    return jnp.stack([value, from_left, far, from_right])


def scatter_sum(value, axis, count):
    me = lax.axis_index(axis)
    blocks = value.reshape((count, value.shape[0] // count) + value.shape[1:])

    def block(offset):
        return lax.dynamic_index_in_dim(blocks, (me + offset) % count, axis=0, keepdims=False)

    if count != 4:
        total = block(0)
        for s in range(1, count):
            total = total + lax.ppermute(block(s), axis, shift_perm(count, s))
        return total
    half = blocks.shape[-1] // 2
    right, left, far, own = block(1), block(-1), block(2), block(0)
    to_right = jnp.concatenate([right[..., half:], far[..., :half]], axis=-1)
    to_left = jnp.concatenate([left[..., :half], far[..., half:]], axis=-1)
    got_left = lax.ppermute(to_right, axis, shift_perm(count, 1))
    got_right = lax.ppermute(to_left, axis, shift_perm(count, -1))
    fwd_right = right[..., :half] + got_left[..., half:]
    fwd_left = left[..., half:] + got_right[..., half:]
    got2_left = lax.ppermute(fwd_right, axis, shift_perm(count, 1))
    got2_right = lax.ppermute(fwd_left, axis, shift_perm(count, -1))
    head = own[..., :half] + got_right[..., :half] + got2_left
    tail = own[..., half:] + got_left[..., :half] + got2_right
    return jnp.concatenate([head, tail], axis=-1)


def scatter_sum_direct(value, axis, count):
    me = lax.axis_index(axis)
    blocks = value.reshape((count, value.shape[0] // count) + value.shape[1:])
    total = lax.dynamic_index_in_dim(blocks, me, axis=0, keepdims=False)
    for s in range(1, count):
        piece = lax.dynamic_index_in_dim(blocks, (me + s) % count, axis=0, keepdims=False)
        sent = lax.ppermute(piece.astype(jnp.bfloat16), axis, shift_perm(count, s))
        total = total + sent.astype(jnp.float32)
    return total


def on_device(records, window_start, channel_segment, segment_row):
    tile_size = records.shape[0]
    block_count = records.shape[1] // NFFT
    sizes = {name: lax.axis_size(name) for name in ("x", "zl", "y", "zh", "core")}
    src_count = sizes["zh"] * sizes["core"]
    x_i, zl_i, y_i = lax.axis_index("x"), lax.axis_index("zl"), lax.axis_index("y")
    zh_i, core_i = lax.axis_index("zh"), lax.axis_index("core")
    group_index = (x_i * sizes["zl"] + zl_i) * sizes["y"] + y_i
    position = zh_i * sizes["core"] + core_i
    segment_total = segment_row.shape[0]

    table = dft_table(NFFT)
    white = jnp.stack(
        [
            whiten(
                jnp.dot(
                    records[:, b * NFFT:(b + 1) * NFFT],
                    table,
                    precision=lax.Precision.HIGHEST,
                    preferred_element_type=jnp.float32,
                )
            ).astype(jnp.bfloat16)
            for b in range(block_count)
        ]
    )
    start_row = jnp.zeros((block_count, 1, NFFT), jnp.bfloat16).at[0, 0, 0].set(
        window_start[0].astype(jnp.bfloat16)
    )
    extended = jnp.concatenate([white, start_row], axis=1)
    gathered = gather_relative(extended, "zh", sizes["zh"])
    partner = lax.ppermute(gathered, "core", shift_perm(sizes["core"], 1))
    gathered = jnp.stack([gathered, partner]).reshape(src_count, block_count, tile_size + 1, NFFT)
    starts = gathered[:, 0, tile_size, 0].astype(jnp.int32)
    group_size = src_count * tile_size
    window_total = group_size // 4
    k_per = window_total // src_count

    slot = jnp.arange(src_count, dtype=jnp.int32)
    slot_zh = (zh_i - slot % sizes["zh"]) % sizes["zh"]
    slot_core = (core_i + slot // sizes["zh"]) % sizes["core"]
    slot_position = slot_zh * sizes["core"] + slot_core
    k_idx = position * k_per + jnp.arange(k_per, dtype=jnp.int32)
    window_idx = starts[:, None] + k_idx[None, :]
    tile_first = (slot_position * tile_size)[:, None]
    source_idx = jnp.where(window_idx < tile_first, window_idx, window_idx + tile_size)
    source_pos = source_idx // tile_size
    source_slot = ((source_pos % sizes["core"] - core_i) % sizes["core"]) * sizes["zh"] + (
        zh_i - source_pos // sizes["core"]
    ) % sizes["zh"]
    source_row = (source_slot * (tile_size + 1) + source_idx % tile_size).reshape(-1)
    sources = jnp.stack(
        [
            jnp.take(gathered[:, b].reshape(-1, NFFT), source_row, axis=0).reshape(
                src_count, k_per, NFFT
            )
            for b in range(block_count)
        ],
        axis=1,
    )
    correlation = correlate(gathered, sources, lag_table(NFFT, LAGS), tile_size)
    correlation = correlation.reshape(src_count, k_per, tile_size, LAGS)

    channel_ids = (slot_position[:, None] * tile_size + jnp.arange(tile_size, dtype=jnp.int32)[None, :]).reshape(-1)
    group_segments = jnp.take(channel_segment, group_index * group_size + channel_ids)
    seg_match = group_segments[:, None] == jnp.arange(segment_total, dtype=jnp.int32)[None, :]
    group_rows = jnp.sum(jnp.where(seg_match, segment_row[None, :], 0), axis=1)
    staged_rows = group_rows
    onehot = (
        jnp.arange(segment_total, dtype=jnp.int32)[:, None] == staged_rows[None, :]
    ).astype(jnp.bfloat16)
    onehot = onehot.reshape(segment_total, src_count, tile_size)
    partial = jnp.einsum("rqi,qkim->rkm", onehot, correlation, preferred_element_type=jnp.float32)
    owners = sizes["x"] * sizes["zl"] * sizes["y"]
    pieces = partial.astype(jnp.bfloat16).reshape((owners, partial.shape[0] // owners) + partial.shape[1:])
    arrived = lax.all_to_all(pieces, ("x", "zl", "y"), split_axis=0, concat_axis=0, tiled=True)
    summed = jnp.sum(arrived.astype(jnp.float32), axis=0)
    counts = row_counts(channel_segment, segment_row, group_index)
    return summed / jnp.sqrt(jnp.maximum(counts, 1.0))[:, None, None]


def solution(mesh):
    names = ("x", "zl", "y", "zh", "core")
    rcv_count, src_count = mesh.devices.shape
    zh_count = src_count // 2
    side = round(rcv_count ** (1 / 3))
    fine = Mesh(mesh.devices.reshape(side, side, rcv_count // side // side, zh_count, 2), names)
    rcv, src = ("x", "zl", "y"), ("zh", "core")
    in_specs = (P(rcv + src, None), P(rcv + src), P(), P())
    out_specs = P(rcv, src, None)
    return jax.shard_map(
        on_device, mesh=fine, in_specs=in_specs, out_specs=out_specs, check_vma=False
    )
```

```python
import math

import jax
import jax.numpy as jnp
from jax import lax
from jax.experimental import pallas as pl
from jax.experimental.pallas import tpu as pltpu
from jax.sharding import Mesh, PartitionSpec as P

NFFT = 1024
LAGS = 256
SEG_PER = 4


def dft_table(length):
    fine_count = 32
    coarse_count = length // fine_count
    frequency = jnp.arange(length // 2, dtype=jnp.int32)
    scale = 2.0 * math.pi / length

    def angle_table(steps, stride):
        index = (jnp.arange(steps, dtype=jnp.int32)[:, None] * stride * frequency[None, :]) % length
        angles = index.astype(jnp.float32) * scale
        return jnp.cos(angles), jnp.sin(angles)

    coarse_cos, coarse_sin = angle_table(coarse_count, fine_count)
    fine_cos, fine_sin = angle_table(fine_count, 1)
    cos_part = coarse_cos[:, None] * fine_cos[None] - coarse_sin[:, None] * fine_sin[None]
    sin_part = coarse_sin[:, None] * fine_cos[None] + coarse_cos[:, None] * fine_sin[None]
    return jnp.concatenate([cos_part, -sin_part], axis=-1).reshape(length, length)


def lag_table(length, lag_count):
    frequency = jnp.arange(length // 2, dtype=jnp.int32)
    shifts = jnp.arange(lag_count, dtype=jnp.int32) - lag_count // 2
    angles = (frequency[:, None] * shifts[None, :] % length).astype(jnp.float32) * (
        2.0 * math.pi / length
    )
    return jnp.concatenate([jnp.cos(angles), -jnp.sin(angles)], axis=0).astype(jnp.bfloat16)


def whiten(spectrum):
    half_size = spectrum.shape[-1] // 2
    powers = spectrum[..., :half_size] ** 2 + spectrum[..., half_size:] ** 2
    mean_power = jnp.mean(powers, axis=-1, keepdims=True)
    magnitude = jnp.sqrt(powers + 0.1 * mean_power + 1e-06)
    return spectrum / jnp.concatenate([magnitude, magnitude], axis=-1)


def correlate_kernel(own_ref, partner_ref, src_ref, lag_ref, out_ref, cross_ref):
    block_count, rows, width = own_ref.shape[1], own_ref.shape[2], own_ref.shape[3]
    k_count = src_ref.shape[2]
    half = width // 2
    mine = pl.program_id(0) < pl.num_programs(0) // 2
    left = [
        jnp.where(mine, own_ref[0, b], partner_ref[0, b]).astype(jnp.float32)
        for b in range(block_count)
    ]
    source_rows = [src_ref[0, b].astype(jnp.float32) for b in range(block_count)]
    for k in range(k_count):
        real_part = None
        imag_part = None
        for b in range(block_count):
            source = source_rows[b][k:k + 1, :]
            l_re, l_im = left[b][:, :half], left[b][:, half:]
            s_re, s_im = source[:, :half], source[:, half:]
            re_term = l_re * s_re + l_im * s_im
            im_term = l_re * s_im - l_im * s_re
            real_part = re_term if real_part is None else real_part + re_term
            imag_part = im_term if imag_part is None else imag_part + im_term
        cross_ref[k * rows:(k + 1) * rows, :half] = real_part.astype(jnp.bfloat16)
        cross_ref[k * rows:(k + 1) * rows, half:] = imag_part.astype(jnp.bfloat16)
    product = jnp.dot(cross_ref[...], lag_ref[...], preferred_element_type=jnp.float32)
    out_ref[0] = (product / math.sqrt(block_count * half)).astype(out_ref.dtype)


def correlate(own, partner, sources, lag_rows, rows):
    block_count, width = own.shape[1], own.shape[3]
    slots = 2 * own.shape[0]
    last = own.shape[0] - 1
    k_count = sources.shape[2]
    lag_count = lag_rows.shape[1]
    flops = slots * k_count * rows * (block_count * width * 4 + 2 * width * lag_count)
    return pl.pallas_call(
        correlate_kernel,
        grid=(slots,),
        in_specs=[
            pl.BlockSpec((1, block_count, rows, width), lambda q: (jnp.minimum(q, last), 0, 0, 0)),
            pl.BlockSpec(
                (1, block_count, rows, width), lambda q: (jnp.maximum(q - last - 1, 0), 0, 0, 0)
            ),
            pl.BlockSpec((1, block_count, k_count, width), lambda q: (q, 0, 0, 0)),
            pl.BlockSpec((width, lag_count), lambda q: (0, 0)),
        ],
        out_specs=pl.BlockSpec((1, k_count * rows, lag_count), lambda q: (q, 0, 0)),
        out_shape=jax.ShapeDtypeStruct((slots, k_count * rows, lag_count), jnp.bfloat16),
        scratch_shapes=[pltpu.VMEM((k_count * rows, width), jnp.bfloat16)],
        cost_estimate=pl.CostEstimate(
            flops=flops,
            bytes_accessed=2 * (2 * own.size // own.shape[2] * rows + sources.size + lag_rows.size)
            + 2 * slots * k_count * rows * lag_count,
            transcendentals=0,
        ),
    )(own, partner, sources, lag_rows)


def row_counts(channel_segment, segment_row, owner):
    held_rows = owner * SEG_PER + jnp.arange(SEG_PER, dtype=jnp.int32)
    matches = segment_row[None, :] == held_rows[:, None]
    segment_ids = jnp.arange(segment_row.shape[0], dtype=jnp.int32)
    held_segments = jnp.sum(jnp.where(matches, segment_ids[None, :], 0), axis=1)
    members = channel_segment[None, :] == held_segments[:, None]
    return jnp.sum(members.astype(jnp.float32), axis=1)


def shift_perm(count, shift):
    return [(i, (i + shift) % count) for i in range(count)]


def gather_relative(value, axis, count):
    if count != 4:
        parts = [value] + [lax.ppermute(value, axis, shift_perm(count, s)) for s in range(1, count)]
        return jnp.stack(parts)
    half = value.shape[-1] // 2
    from_left = lax.ppermute(value, axis, shift_perm(count, 1))
    from_right = lax.ppermute(value, axis, shift_perm(count, -1))
    far_head = lax.ppermute(from_left[..., :half], axis, shift_perm(count, 1))
    far_tail = lax.ppermute(from_right[..., half:], axis, shift_perm(count, -1))
    far = jnp.concatenate([far_head, far_tail], axis=-1)
    return jnp.stack([value, from_left, far, from_right])


def scatter_sum(value, axis, count):
    me = lax.axis_index(axis)
    blocks = value.reshape((count, value.shape[0] // count) + value.shape[1:])

    def block(offset):
        return lax.dynamic_index_in_dim(blocks, (me + offset) % count, axis=0, keepdims=False)

    if count != 4:
        total = block(0)
        for s in range(1, count):
            total = total + lax.ppermute(block(s), axis, shift_perm(count, s))
        return total
    half = blocks.shape[-1] // 2
    right, left, far, own = block(1), block(-1), block(2), block(0)
    to_right = jnp.concatenate([right[..., half:], far[..., :half]], axis=-1)
    to_left = jnp.concatenate([left[..., :half], far[..., half:]], axis=-1)
    got_left = lax.ppermute(to_right, axis, shift_perm(count, 1))
    got_right = lax.ppermute(to_left, axis, shift_perm(count, -1))
    fwd_right = right[..., :half] + got_left[..., half:]
    fwd_left = left[..., half:] + got_right[..., half:]
    got2_left = lax.ppermute(fwd_right, axis, shift_perm(count, 1))
    got2_right = lax.ppermute(fwd_left, axis, shift_perm(count, -1))
    head = own[..., :half] + got_right[..., :half] + got2_left
    tail = own[..., half:] + got_left[..., :half] + got2_right
    return jnp.concatenate([head, tail], axis=-1)


def scatter_sum_direct(value, axis, count):
    me = lax.axis_index(axis)
    blocks = value.reshape((count, value.shape[0] // count) + value.shape[1:])
    total = lax.dynamic_index_in_dim(blocks, me, axis=0, keepdims=False)
    for s in range(1, count):
        piece = lax.dynamic_index_in_dim(blocks, (me + s) % count, axis=0, keepdims=False)
        sent = lax.ppermute(piece.astype(jnp.bfloat16), axis, shift_perm(count, s))
        total = total + sent.astype(jnp.float32)
    return total


def on_device(records, window_start, channel_segment, segment_row):
    tile_size = records.shape[0]
    block_count = records.shape[1] // NFFT
    sizes = {name: lax.axis_size(name) for name in ("x", "zl", "y", "zh", "core")}
    src_count = sizes["zh"] * sizes["core"]
    x_i, zl_i, y_i = lax.axis_index("x"), lax.axis_index("zl"), lax.axis_index("y")
    zh_i, core_i = lax.axis_index("zh"), lax.axis_index("core")
    group_index = (x_i * sizes["zl"] + zl_i) * sizes["y"] + y_i
    position = zh_i * sizes["core"] + core_i
    segment_total = segment_row.shape[0]

    blocks = records.reshape(tile_size * block_count, NFFT)
    spectrum = jnp.dot(
        blocks, dft_table(NFFT), precision=lax.Precision.HIGHEST, preferred_element_type=jnp.float32
    )
    white = whiten(spectrum).astype(jnp.bfloat16).reshape(tile_size, block_count, NFFT)
    start_row = jnp.zeros((1, block_count, NFFT), jnp.bfloat16).at[0, 0, 0].set(
        window_start[0].astype(jnp.bfloat16)
    )
    extended = jnp.concatenate([white, start_row], axis=0).transpose(1, 0, 2)
    own = gather_relative(extended, "zh", sizes["zh"])
    partner = lax.ppermute(own, "core", shift_perm(sizes["core"], 1))
    starts = jnp.concatenate([own[:, 0, tile_size, 0], partner[:, 0, tile_size, 0]]).astype(jnp.int32)
    group_size = src_count * tile_size
    window_total = group_size // 4
    k_per = window_total // src_count

    slot = jnp.arange(src_count, dtype=jnp.int32)
    slot_zh = (zh_i - slot % sizes["zh"]) % sizes["zh"]
    slot_core = (core_i + slot // sizes["zh"]) % sizes["core"]
    slot_position = slot_zh * sizes["core"] + slot_core
    k_idx = position * k_per + jnp.arange(k_per, dtype=jnp.int32)
    window_idx = starts[:, None] + k_idx[None, :]
    tile_first = (slot_position * tile_size)[:, None]
    source_idx = jnp.where(window_idx < tile_first, window_idx, window_idx + tile_size)
    source_pos = source_idx // tile_size
    source_slot = ((source_pos % sizes["core"] - core_i) % sizes["core"]) * sizes["zh"] + (
        zh_i - source_pos // sizes["core"]
    ) % sizes["zh"]
    source_row = ((source_slot % sizes["zh"]) * (tile_size + 1) + source_idx % tile_size).reshape(-1)
    from_own = (source_slot < sizes["zh"]).reshape(-1, 1)

    def pick(b):
        own_rows = jnp.take(own[:, b].reshape(-1, NFFT), source_row, axis=0)
        partner_rows = jnp.take(partner[:, b].reshape(-1, NFFT), source_row, axis=0)
        return jnp.where(from_own, own_rows, partner_rows).reshape(src_count, k_per, NFFT)

    sources = jnp.stack([pick(b) for b in range(block_count)], axis=1)
    correlation = correlate(own, partner, sources, lag_table(NFFT, LAGS), tile_size)
    correlation = correlation.reshape(src_count, k_per, tile_size, LAGS)

    channel_ids = (slot_position[:, None] * tile_size + jnp.arange(tile_size, dtype=jnp.int32)[None, :]).reshape(-1)
    group_segments = jnp.take(channel_segment, group_index * group_size + channel_ids)
    seg_match = group_segments[:, None] == jnp.arange(segment_total, dtype=jnp.int32)[None, :]
    group_rows = jnp.sum(jnp.where(seg_match, segment_row[None, :], 0), axis=1)
    staged_rows = group_rows
    onehot = (
        jnp.arange(segment_total, dtype=jnp.int32)[:, None] == staged_rows[None, :]
    ).astype(jnp.bfloat16)
    onehot = onehot.reshape(segment_total, src_count, tile_size)
    partial = jnp.einsum("rqi,qkim->rkm", onehot, correlation, preferred_element_type=jnp.float32)
    owners = sizes["x"] * sizes["zl"] * sizes["y"]
    pieces = partial.astype(jnp.bfloat16).reshape((owners, partial.shape[0] // owners) + partial.shape[1:])
    arrived = lax.all_to_all(pieces, ("x", "zl", "y"), split_axis=0, concat_axis=0, tiled=True)
    summed = jnp.sum(arrived.astype(jnp.float32), axis=0)
    counts = row_counts(channel_segment, segment_row, group_index)
    return summed / jnp.sqrt(jnp.maximum(counts, 1.0))[:, None, None]


def solution(mesh):
    names = ("x", "zl", "y", "zh", "core")
    rcv_count, src_count = mesh.devices.shape
    zh_count = src_count // 2
    side = round(rcv_count ** (1 / 3))
    fine = Mesh(mesh.devices.reshape(side, side, rcv_count // side // side, zh_count, 2), names)
    rcv, src = ("x", "zl", "y"), ("zh", "core")
    in_specs = (P(rcv + src, None), P(rcv + src), P(), P())
    out_specs = P(rcv, src, None)
    return jax.shard_map(
        on_device, mesh=fine, in_specs=in_specs, out_specs=out_specs, check_vma=False
    )
```

```python
import math

import jax
import jax.numpy as jnp
from jax import lax
from jax.experimental import pallas as pl
from jax.experimental.pallas import tpu as pltpu
from jax.sharding import Mesh, PartitionSpec as P

NFFT = 1024
LAGS = 256
SEG_PER = 4


def dft_table(length):
    fine_count = 32
    coarse_count = length // fine_count
    frequency = jnp.arange(length // 2, dtype=jnp.int32)
    scale = 2.0 * math.pi / length

    def angle_table(steps, stride):
        index = (jnp.arange(steps, dtype=jnp.int32)[:, None] * stride * frequency[None, :]) % length
        angles = index.astype(jnp.float32) * scale
        return jnp.cos(angles), jnp.sin(angles)

    coarse_cos, coarse_sin = angle_table(coarse_count, fine_count)
    fine_cos, fine_sin = angle_table(fine_count, 1)
    cos_part = coarse_cos[:, None] * fine_cos[None] - coarse_sin[:, None] * fine_sin[None]
    sin_part = coarse_sin[:, None] * fine_cos[None] + coarse_cos[:, None] * fine_sin[None]
    return jnp.concatenate([cos_part, -sin_part], axis=-1).reshape(length, length)


def lag_table(length, lag_count):
    frequency = jnp.arange(length // 2, dtype=jnp.int32)
    shifts = jnp.arange(lag_count, dtype=jnp.int32) - lag_count // 2
    angles = (frequency[:, None] * shifts[None, :] % length).astype(jnp.float32) * (
        2.0 * math.pi / length
    )
    return jnp.concatenate([jnp.cos(angles), -jnp.sin(angles)], axis=0).astype(jnp.bfloat16)


def whiten(spectrum):
    half_size = spectrum.shape[-1] // 2
    powers = spectrum[..., :half_size] ** 2 + spectrum[..., half_size:] ** 2
    mean_power = jnp.mean(powers, axis=-1, keepdims=True)
    magnitude = jnp.sqrt(powers + 0.1 * mean_power + 1e-06)
    return spectrum / jnp.concatenate([magnitude, magnitude], axis=-1)


def correlate_kernel(left_ref, src_ref, lag_ref, out_ref, cross_ref):
    block_count, rows, width = left_ref.shape[1], left_ref.shape[2], left_ref.shape[3]
    k_count = src_ref.shape[2]
    half = width // 2
    left = [left_ref[0, b].astype(jnp.float32) for b in range(block_count)]
    source_rows = [src_ref[0, b].astype(jnp.float32) for b in range(block_count)]
    for k in range(k_count):
        real_part = None
        imag_part = None
        for b in range(block_count):
            source = source_rows[b][k:k + 1, :]
            l_re, l_im = left[b][:, :half], left[b][:, half:]
            s_re, s_im = source[:, :half], source[:, half:]
            re_term = l_re * s_re + l_im * s_im
            im_term = l_re * s_im - l_im * s_re
            real_part = re_term if real_part is None else real_part + re_term
            imag_part = im_term if imag_part is None else imag_part + im_term
        cross_ref[k * rows:(k + 1) * rows, :half] = real_part.astype(jnp.bfloat16)
        cross_ref[k * rows:(k + 1) * rows, half:] = imag_part.astype(jnp.bfloat16)
    product = jnp.dot(cross_ref[...], lag_ref[...], preferred_element_type=jnp.float32)
    out_ref[0] = (product / math.sqrt(block_count * half)).astype(out_ref.dtype)


def correlate(left, sources, lag_rows, rows):
    slots, block_count, _, width = left.shape
    k_count = sources.shape[2]
    lag_count = lag_rows.shape[1]
    flops = slots * k_count * rows * (block_count * width * 4 + 2 * width * lag_count)
    return pl.pallas_call(
        correlate_kernel,
        grid=(slots,),
        in_specs=[
            pl.BlockSpec((1, block_count, rows, width), lambda q: (q, 0, 0, 0)),
            pl.BlockSpec((1, block_count, k_count, width), lambda q: (q, 0, 0, 0)),
            pl.BlockSpec((width, lag_count), lambda q: (0, 0)),
        ],
        out_specs=pl.BlockSpec((1, k_count * rows, lag_count), lambda q: (q, 0, 0)),
        out_shape=jax.ShapeDtypeStruct((slots, k_count * rows, lag_count), jnp.bfloat16),
        scratch_shapes=[pltpu.VMEM((k_count * rows, width), jnp.bfloat16)],
        cost_estimate=pl.CostEstimate(
            flops=flops,
            bytes_accessed=2 * (left.size // left.shape[2] * rows + sources.size + lag_rows.size)
            + 2 * slots * k_count * rows * lag_count,
            transcendentals=0,
        ),
    )(left, sources, lag_rows)


def row_counts(channel_segment, segment_row, owner):
    held_rows = owner * SEG_PER + jnp.arange(SEG_PER, dtype=jnp.int32)
    matches = segment_row[None, :] == held_rows[:, None]
    segment_ids = jnp.arange(segment_row.shape[0], dtype=jnp.int32)
    held_segments = jnp.sum(jnp.where(matches, segment_ids[None, :], 0), axis=1)
    members = channel_segment[None, :] == held_segments[:, None]
    return jnp.sum(members.astype(jnp.float32), axis=1)


def shift_perm(count, shift):
    return [(i, (i + shift) % count) for i in range(count)]


def gather_relative(value, axis, count):
    if count != 4:
        parts = [value] + [lax.ppermute(value, axis, shift_perm(count, s)) for s in range(1, count)]
        return jnp.stack(parts)
    half = value.shape[-1] // 2
    from_left = lax.ppermute(value, axis, shift_perm(count, 1))
    from_right = lax.ppermute(value, axis, shift_perm(count, -1))
    far_head = lax.ppermute(from_left[..., :half], axis, shift_perm(count, 1))
    far_tail = lax.ppermute(from_right[..., half:], axis, shift_perm(count, -1))
    far = jnp.concatenate([far_head, far_tail], axis=-1)
    return jnp.stack([value, from_left, far, from_right])


def scatter_sum(value, axis, count):
    me = lax.axis_index(axis)
    blocks = value.reshape((count, value.shape[0] // count) + value.shape[1:])

    def block(offset):
        return lax.dynamic_index_in_dim(blocks, (me + offset) % count, axis=0, keepdims=False)

    if count != 4:
        total = block(0)
        for s in range(1, count):
            total = total + lax.ppermute(block(s), axis, shift_perm(count, s))
        return total
    half = blocks.shape[-1] // 2
    right, left, far, own = block(1), block(-1), block(2), block(0)
    to_right = jnp.concatenate([right[..., half:], far[..., :half]], axis=-1)
    to_left = jnp.concatenate([left[..., :half], far[..., half:]], axis=-1)
    got_left = lax.ppermute(to_right, axis, shift_perm(count, 1))
    got_right = lax.ppermute(to_left, axis, shift_perm(count, -1))
    fwd_right = right[..., :half] + got_left[..., half:]
    fwd_left = left[..., half:] + got_right[..., half:]
    got2_left = lax.ppermute(fwd_right, axis, shift_perm(count, 1))
    got2_right = lax.ppermute(fwd_left, axis, shift_perm(count, -1))
    head = own[..., :half] + got_right[..., :half] + got2_left
    tail = own[..., half:] + got_left[..., :half] + got2_right
    return jnp.concatenate([head, tail], axis=-1)


def scatter_sum_direct(value, axis, count):
    me = lax.axis_index(axis)
    blocks = value.reshape((count, value.shape[0] // count) + value.shape[1:])
    total = lax.dynamic_index_in_dim(blocks, me, axis=0, keepdims=False)
    for s in range(1, count):
        piece = lax.dynamic_index_in_dim(blocks, (me + s) % count, axis=0, keepdims=False)
        sent = lax.ppermute(piece.astype(jnp.bfloat16), axis, shift_perm(count, s))
        total = total + sent.astype(jnp.float32)
    return total


def on_device(records, window_start, channel_segment, segment_row):
    tile_size = records.shape[0]
    block_count = records.shape[1] // NFFT
    sizes = {name: lax.axis_size(name) for name in ("x", "zl", "y", "zh", "core")}
    src_count = sizes["zh"] * sizes["core"]
    x_i, zl_i, y_i = lax.axis_index("x"), lax.axis_index("zl"), lax.axis_index("y")
    zh_i, core_i = lax.axis_index("zh"), lax.axis_index("core")
    group_index = (x_i * sizes["zl"] + zl_i) * sizes["y"] + y_i
    position = zh_i * sizes["core"] + core_i
    segment_total = segment_row.shape[0]

    blocks = records.reshape(tile_size * block_count, NFFT)
    spectrum = jnp.dot(
        blocks, dft_table(NFFT), precision=lax.Precision.HIGHEST, preferred_element_type=jnp.float32
    )
    white = whiten(spectrum).astype(jnp.bfloat16).reshape(tile_size, block_count, NFFT)
    start_row = jnp.zeros((1, block_count, NFFT), jnp.bfloat16).at[0, 0, 0].set(
        window_start[0].astype(jnp.bfloat16)
    )
    extended = jnp.concatenate([white, start_row], axis=0).transpose(1, 0, 2)
    count = sizes["zh"]
    swap = shift_perm(sizes["core"], 1)
    half = NFFT // 2
    partner_own = lax.ppermute(extended, "core", swap)
    from_left = lax.ppermute(extended, "zh", shift_perm(count, 1))
    from_right = lax.ppermute(extended, "zh", shift_perm(count, -1))
    partner_left, partner_right = lax.ppermute((from_left, from_right), "core", swap)
    far_head = lax.ppermute(from_left[..., :half], "zh", shift_perm(count, 1))
    far_tail = lax.ppermute(from_right[..., half:], "zh", shift_perm(count, -1))
    far = jnp.concatenate([far_head, far_tail], axis=-1)
    partner_far = lax.ppermute(far, "core", swap)
    gathered = jnp.stack([extended, from_left, far, from_right])
    partner = jnp.stack([partner_own, partner_left, partner_far, partner_right])
    gathered = jnp.stack([gathered, partner]).reshape(src_count, block_count, tile_size + 1, NFFT)
    starts = gathered[:, 0, tile_size, 0].astype(jnp.int32)
    group_size = src_count * tile_size
    window_total = group_size // 4
    k_per = window_total // src_count

    slot = jnp.arange(src_count, dtype=jnp.int32)
    slot_zh = (zh_i - slot % sizes["zh"]) % sizes["zh"]
    slot_core = (core_i + slot // sizes["zh"]) % sizes["core"]
    slot_position = slot_zh * sizes["core"] + slot_core
    k_idx = position * k_per + jnp.arange(k_per, dtype=jnp.int32)
    window_idx = starts[:, None] + k_idx[None, :]
    tile_first = (slot_position * tile_size)[:, None]
    source_idx = jnp.where(window_idx < tile_first, window_idx, window_idx + tile_size)
    source_pos = source_idx // tile_size
    source_slot = ((source_pos % sizes["core"] - core_i) % sizes["core"]) * sizes["zh"] + (
        zh_i - source_pos // sizes["core"]
    ) % sizes["zh"]
    source_row = (source_slot * (tile_size + 1) + source_idx % tile_size).reshape(-1)
    sources = jnp.stack(
        [
            jnp.take(gathered[:, b].reshape(-1, NFFT), source_row, axis=0).reshape(
                src_count, k_per, NFFT
            )
            for b in range(block_count)
        ],
        axis=1,
    )
    correlation = correlate(gathered, sources, lag_table(NFFT, LAGS), tile_size)
    correlation = correlation.reshape(src_count, k_per, tile_size, LAGS)

    channel_ids = (slot_position[:, None] * tile_size + jnp.arange(tile_size, dtype=jnp.int32)[None, :]).reshape(-1)
    group_segments = jnp.take(channel_segment, group_index * group_size + channel_ids)
    seg_match = group_segments[:, None] == jnp.arange(segment_total, dtype=jnp.int32)[None, :]
    group_rows = jnp.sum(jnp.where(seg_match, segment_row[None, :], 0), axis=1)
    staged_rows = group_rows
    onehot = (
        jnp.arange(segment_total, dtype=jnp.int32)[:, None] == staged_rows[None, :]
    ).astype(jnp.bfloat16)
    onehot = onehot.reshape(segment_total, src_count, tile_size)
    partial = jnp.einsum("rqi,qkim->rkm", onehot, correlation, preferred_element_type=jnp.float32)
    owners = sizes["x"] * sizes["zl"] * sizes["y"]
    pieces = partial.astype(jnp.bfloat16).reshape((owners, partial.shape[0] // owners) + partial.shape[1:])
    arrived = lax.all_to_all(pieces, ("x", "zl", "y"), split_axis=0, concat_axis=0, tiled=True)
    summed = jnp.sum(arrived.astype(jnp.float32), axis=0)
    counts = row_counts(channel_segment, segment_row, group_index)
    return summed / jnp.sqrt(jnp.maximum(counts, 1.0))[:, None, None]


def solution(mesh):
    names = ("x", "zl", "y", "zh", "core")
    rcv_count, src_count = mesh.devices.shape
    zh_count = src_count // 2
    side = round(rcv_count ** (1 / 3))
    fine = Mesh(mesh.devices.reshape(side, side, rcv_count // side // side, zh_count, 2), names)
    rcv, src = ("x", "zl", "y"), ("zh", "core")
    in_specs = (P(rcv + src, None), P(rcv + src), P(), P())
    out_specs = P(rcv, src, None)
    return jax.shard_map(
        on_device, mesh=fine, in_specs=in_specs, out_specs=out_specs, check_vma=False
    )
```

```python
import math

import jax
import jax.numpy as jnp
from jax import lax
from jax.experimental import pallas as pl
from jax.experimental.pallas import tpu as pltpu
from jax.sharding import Mesh, PartitionSpec as P

NFFT = 1024
LAGS = 256
SEG_PER = 4


def dft_table(length):
    fine_count = 32
    coarse_count = length // fine_count
    frequency = jnp.arange(length // 2, dtype=jnp.int32)
    scale = 2.0 * math.pi / length

    def angle_table(steps, stride):
        index = (jnp.arange(steps, dtype=jnp.int32)[:, None] * stride * frequency[None, :]) % length
        angles = index.astype(jnp.float32) * scale
        return jnp.cos(angles), jnp.sin(angles)

    coarse_cos, coarse_sin = angle_table(coarse_count, fine_count)
    fine_cos, fine_sin = angle_table(fine_count, 1)
    cos_part = coarse_cos[:, None] * fine_cos[None] - coarse_sin[:, None] * fine_sin[None]
    sin_part = coarse_sin[:, None] * fine_cos[None] + coarse_cos[:, None] * fine_sin[None]
    return jnp.concatenate([cos_part, -sin_part], axis=-1).reshape(length, length)


def lag_table(length, lag_count):
    frequency = jnp.arange(length // 2, dtype=jnp.int32)
    shifts = jnp.arange(lag_count, dtype=jnp.int32) - lag_count // 2
    angles = (frequency[:, None] * shifts[None, :] % length).astype(jnp.float32) * (
        2.0 * math.pi / length
    )
    return jnp.concatenate([jnp.cos(angles), -jnp.sin(angles)], axis=0).astype(jnp.bfloat16)


def whiten(spectrum):
    half_size = spectrum.shape[-1] // 2
    powers = spectrum[..., :half_size] ** 2 + spectrum[..., half_size:] ** 2
    mean_power = jnp.mean(powers, axis=-1, keepdims=True)
    magnitude = jnp.sqrt(powers + 0.1 * mean_power + 1e-06)
    return spectrum / jnp.concatenate([magnitude, magnitude], axis=-1)


def correlate_kernel(left_ref, src_ref, lag_ref, out_ref, cross_ref):
    block_count, rows, width = left_ref.shape[1], left_ref.shape[2], left_ref.shape[3]
    k_count = src_ref.shape[2]
    half = width // 2
    left = [left_ref[0, b].astype(jnp.float32) for b in range(block_count)]
    source_rows = [src_ref[0, b].astype(jnp.float32) for b in range(block_count)]
    for k in range(k_count):
        real_part = None
        imag_part = None
        for b in range(block_count):
            source = source_rows[b][k:k + 1, :]
            l_re, l_im = left[b][:, :half], left[b][:, half:]
            s_re, s_im = source[:, :half], source[:, half:]
            re_term = l_re * s_re + l_im * s_im
            im_term = l_re * s_im - l_im * s_re
            real_part = re_term if real_part is None else real_part + re_term
            imag_part = im_term if imag_part is None else imag_part + im_term
        cross_ref[k * rows:(k + 1) * rows, :half] = real_part.astype(jnp.bfloat16)
        cross_ref[k * rows:(k + 1) * rows, half:] = imag_part.astype(jnp.bfloat16)
    product = jnp.dot(cross_ref[...], lag_ref[...], preferred_element_type=jnp.float32)
    out_ref[0] = (product / math.sqrt(block_count * half)).astype(out_ref.dtype)


def correlate(left, sources, lag_rows, rows):
    slots, block_count, _, width = left.shape
    k_count = sources.shape[2]
    lag_count = lag_rows.shape[1]
    flops = slots * k_count * rows * (block_count * width * 4 + 2 * width * lag_count)
    return pl.pallas_call(
        correlate_kernel,
        grid=(slots,),
        in_specs=[
            pl.BlockSpec((1, block_count, rows, width), lambda q: (q, 0, 0, 0)),
            pl.BlockSpec((1, block_count, k_count, width), lambda q: (q, 0, 0, 0)),
            pl.BlockSpec((width, lag_count), lambda q: (0, 0)),
        ],
        out_specs=pl.BlockSpec((1, k_count * rows, lag_count), lambda q: (q, 0, 0)),
        out_shape=jax.ShapeDtypeStruct((slots, k_count * rows, lag_count), jnp.bfloat16),
        scratch_shapes=[pltpu.VMEM((k_count * rows, width), jnp.bfloat16)],
        cost_estimate=pl.CostEstimate(
            flops=flops,
            bytes_accessed=2 * (left.size // left.shape[2] * rows + sources.size + lag_rows.size)
            + 2 * slots * k_count * rows * lag_count,
            transcendentals=0,
        ),
    )(left, sources, lag_rows)


def row_counts(channel_segment, segment_row, owner):
    held_rows = owner * SEG_PER + jnp.arange(SEG_PER, dtype=jnp.int32)
    matches = segment_row[None, :] == held_rows[:, None]
    segment_ids = jnp.arange(segment_row.shape[0], dtype=jnp.int32)
    held_segments = jnp.sum(jnp.where(matches, segment_ids[None, :], 0), axis=1)
    members = channel_segment[None, :] == held_segments[:, None]
    return jnp.sum(members.astype(jnp.float32), axis=1)


def shift_perm(count, shift):
    return [(i, (i + shift) % count) for i in range(count)]


def gather_relative(value, axis, count):
    if count != 4:
        parts = [value] + [lax.ppermute(value, axis, shift_perm(count, s)) for s in range(1, count)]
        return jnp.stack(parts)
    half = value.shape[-1] // 2
    from_left = lax.ppermute(value, axis, shift_perm(count, 1))
    from_right = lax.ppermute(value, axis, shift_perm(count, -1))
    far_head = lax.ppermute(from_left[..., :half], axis, shift_perm(count, 1))
    far_tail = lax.ppermute(from_right[..., half:], axis, shift_perm(count, -1))
    far = jnp.concatenate([far_head, far_tail], axis=-1)
    return jnp.stack([value, from_left, far, from_right])


def scatter_sum(value, axis, count):
    me = lax.axis_index(axis)
    blocks = value.reshape((count, value.shape[0] // count) + value.shape[1:])

    def block(offset):
        return lax.dynamic_index_in_dim(blocks, (me + offset) % count, axis=0, keepdims=False)

    if count != 4:
        total = block(0)
        for s in range(1, count):
            total = total + lax.ppermute(block(s), axis, shift_perm(count, s))
        return total
    half = blocks.shape[-1] // 2
    right, left, far, own = block(1), block(-1), block(2), block(0)
    to_right = jnp.concatenate([right[..., half:], far[..., :half]], axis=-1)
    to_left = jnp.concatenate([left[..., :half], far[..., half:]], axis=-1)
    got_left = lax.ppermute(to_right, axis, shift_perm(count, 1))
    got_right = lax.ppermute(to_left, axis, shift_perm(count, -1))
    fwd_right = right[..., :half] + got_left[..., half:]
    fwd_left = left[..., half:] + got_right[..., half:]
    got2_left = lax.ppermute(fwd_right, axis, shift_perm(count, 1))
    got2_right = lax.ppermute(fwd_left, axis, shift_perm(count, -1))
    head = own[..., :half] + got_right[..., :half] + got2_left
    tail = own[..., half:] + got_left[..., :half] + got2_right
    return jnp.concatenate([head, tail], axis=-1)


def scatter_sum_direct(value, axis, count):
    me = lax.axis_index(axis)
    blocks = value.reshape((count, value.shape[0] // count) + value.shape[1:])
    total = lax.dynamic_index_in_dim(blocks, me, axis=0, keepdims=False)
    for s in range(1, count):
        piece = lax.dynamic_index_in_dim(blocks, (me + s) % count, axis=0, keepdims=False)
        sent = lax.ppermute(piece.astype(jnp.bfloat16), axis, shift_perm(count, s))
        total = total + sent.astype(jnp.float32)
    return total


def on_device(records, window_start, channel_segment, segment_row):
    tile_size = records.shape[0]
    block_count = records.shape[1] // NFFT
    sizes = {name: lax.axis_size(name) for name in ("x", "zl", "y", "zh", "core")}
    src_count = sizes["zh"] * sizes["core"]
    x_i, zl_i, y_i = lax.axis_index("x"), lax.axis_index("zl"), lax.axis_index("y")
    zh_i, core_i = lax.axis_index("zh"), lax.axis_index("core")
    group_index = (x_i * sizes["zl"] + zl_i) * sizes["y"] + y_i
    position = zh_i * sizes["core"] + core_i
    segment_total = segment_row.shape[0]

    blocks = records.reshape(tile_size * block_count, NFFT)
    spectrum = jnp.dot(
        blocks, dft_table(NFFT), precision=lax.Precision.HIGHEST, preferred_element_type=jnp.float32
    )
    white = whiten(spectrum).astype(jnp.bfloat16).reshape(tile_size, block_count, NFFT)
    start_row = jnp.zeros((1, block_count, NFFT), jnp.bfloat16).at[0, 0, 0].set(
        window_start[0].astype(jnp.bfloat16)
    )
    extended = jnp.concatenate([white, start_row], axis=0).transpose(1, 0, 2)
    gathered = gather_relative(extended, "zh", sizes["zh"])
    partner = lax.ppermute(gathered, "core", shift_perm(sizes["core"], 1))
    gathered = jnp.stack([gathered, partner]).reshape(src_count, block_count, tile_size + 1, NFFT)
    starts = gathered[:, 0, tile_size, 0].astype(jnp.int32)
    group_size = src_count * tile_size
    window_total = group_size // 4
    k_per = window_total // src_count

    slot = jnp.arange(src_count, dtype=jnp.int32)
    slot_zh = (zh_i - slot % sizes["zh"]) % sizes["zh"]
    slot_core = (core_i + slot // sizes["zh"]) % sizes["core"]
    slot_position = slot_zh * sizes["core"] + slot_core
    k_idx = position * k_per + jnp.arange(k_per, dtype=jnp.int32)
    window_idx = starts[:, None] + k_idx[None, :]
    tile_first = (slot_position * tile_size)[:, None]
    source_idx = jnp.where(window_idx < tile_first, window_idx, window_idx + tile_size)
    source_pos = source_idx // tile_size
    source_slot = ((source_pos % sizes["core"] - core_i) % sizes["core"]) * sizes["zh"] + (
        zh_i - source_pos // sizes["core"]
    ) % sizes["zh"]
    source_row = (source_slot * (tile_size + 1) + source_idx % tile_size).reshape(-1)
    sources = jnp.stack(
        [
            jnp.take(gathered[:, b].reshape(-1, NFFT), source_row, axis=0).reshape(
                src_count, k_per, NFFT
            )
            for b in range(block_count)
        ],
        axis=1,
    )
    lag_rows = lag_table(NFFT, LAGS)

    channel_ids = (slot_position[:, None] * tile_size + jnp.arange(tile_size, dtype=jnp.int32)[None, :]).reshape(-1)
    group_segments = jnp.take(channel_segment, group_index * group_size + channel_ids)
    seg_match = group_segments[:, None] == jnp.arange(segment_total, dtype=jnp.int32)[None, :]
    group_rows = jnp.sum(jnp.where(seg_match, segment_row[None, :], 0), axis=1)
    onehot = (
        jnp.arange(segment_total, dtype=jnp.int32)[:, None] == group_rows[None, :]
    ).astype(jnp.bfloat16)
    onehot = onehot.reshape(segment_total, src_count, tile_size)
    owners = sizes["x"] * sizes["zl"] * sizes["y"]
    k_half = k_per // 2
    stacked = []
    for first in (0, k_half):
        correlation = correlate(gathered, sources[:, :, first:first + k_half], lag_rows, tile_size)
        correlation = correlation.reshape(src_count, k_half, tile_size, LAGS)
        partial = jnp.einsum("rqi,qkim->rkm", onehot, correlation, preferred_element_type=jnp.float32)
        pieces = partial.astype(jnp.bfloat16).reshape((owners, partial.shape[0] // owners) + partial.shape[1:])
        arrived = lax.all_to_all(pieces, ("x", "zl", "y"), split_axis=0, concat_axis=0, tiled=True)
        stacked.append(jnp.sum(arrived.astype(jnp.float32), axis=0))
    summed = jnp.concatenate(stacked, axis=1)
    counts = row_counts(channel_segment, segment_row, group_index)
    return summed / jnp.sqrt(jnp.maximum(counts, 1.0))[:, None, None]


def solution(mesh):
    names = ("x", "zl", "y", "zh", "core")
    rcv_count, src_count = mesh.devices.shape
    zh_count = src_count // 2
    side = round(rcv_count ** (1 / 3))
    fine = Mesh(mesh.devices.reshape(side, side, rcv_count // side // side, zh_count, 2), names)
    rcv, src = ("x", "zl", "y"), ("zh", "core")
    in_specs = (P(rcv + src, None), P(rcv + src), P(), P())
    out_specs = P(rcv, src, None)
    return jax.shard_map(
        on_device, mesh=fine, in_specs=in_specs, out_specs=out_specs, check_vma=False
    )
```

```python
import math

import jax
import jax.numpy as jnp
from jax import lax
from jax.experimental import pallas as pl
from jax.experimental.pallas import tpu as pltpu
from jax.sharding import Mesh, PartitionSpec as P

NFFT = 1024
LAGS = 256
SEG_PER = 4


def dft_table(length):
    fine_count = 32
    coarse_count = length // fine_count
    frequency = jnp.arange(length // 2, dtype=jnp.int32)
    scale = 2.0 * math.pi / length

    def angle_table(steps, stride):
        index = (jnp.arange(steps, dtype=jnp.int32)[:, None] * stride * frequency[None, :]) % length
        angles = index.astype(jnp.float32) * scale
        return jnp.cos(angles), jnp.sin(angles)

    coarse_cos, coarse_sin = angle_table(coarse_count, fine_count)
    fine_cos, fine_sin = angle_table(fine_count, 1)
    cos_part = coarse_cos[:, None] * fine_cos[None] - coarse_sin[:, None] * fine_sin[None]
    sin_part = coarse_sin[:, None] * fine_cos[None] + coarse_cos[:, None] * fine_sin[None]
    return jnp.concatenate([cos_part, -sin_part], axis=-1).reshape(length, length)


def lag_table(length, lag_count):
    frequency = jnp.arange(length // 2, dtype=jnp.int32)
    shifts = jnp.arange(lag_count, dtype=jnp.int32) - lag_count // 2
    angles = (frequency[:, None] * shifts[None, :] % length).astype(jnp.float32) * (
        2.0 * math.pi / length
    )
    return jnp.concatenate([jnp.cos(angles), -jnp.sin(angles)], axis=0).astype(jnp.bfloat16)


def whiten(spectrum):
    half_size = spectrum.shape[-1] // 2
    powers = spectrum[..., :half_size] ** 2 + spectrum[..., half_size:] ** 2
    mean_power = jnp.mean(powers, axis=-1, keepdims=True)
    magnitude = jnp.sqrt(powers + 0.1 * mean_power + 1e-06)
    return spectrum / jnp.concatenate([magnitude, magnitude], axis=-1)


def correlate_kernel(left_ref, src_ref, lag_ref, out_ref, cross_ref):
    block_count, rows, width = left_ref.shape[1], left_ref.shape[2], left_ref.shape[3]
    k_count = src_ref.shape[2]
    half = width // 2
    for slot in range(left_ref.shape[0]):
        left = [left_ref[slot, b].astype(jnp.float32) for b in range(block_count)]
        source_rows = [src_ref[slot, b].astype(jnp.float32) for b in range(block_count)]
        for k in range(k_count):
            real_part = None
            imag_part = None
            for b in range(block_count):
                source = source_rows[b][k:k + 1, :]
                l_re, l_im = left[b][:, :half], left[b][:, half:]
                s_re, s_im = source[:, :half], source[:, half:]
                re_term = l_re * s_re + l_im * s_im
                im_term = l_re * s_im - l_im * s_re
                real_part = re_term if real_part is None else real_part + re_term
                imag_part = im_term if imag_part is None else imag_part + im_term
            cross_ref[k * rows:(k + 1) * rows, :half] = real_part.astype(jnp.bfloat16)
            cross_ref[k * rows:(k + 1) * rows, half:] = imag_part.astype(jnp.bfloat16)
        product = jnp.dot(cross_ref[...], lag_ref[...], preferred_element_type=jnp.float32)
        out_ref[slot] = (product / math.sqrt(block_count * half)).astype(out_ref.dtype)


def correlate(left, sources, lag_rows, rows):
    slots, block_count, _, width = left.shape
    k_count = sources.shape[2]
    lag_count = lag_rows.shape[1]
    flops = slots * k_count * rows * (block_count * width * 4 + 2 * width * lag_count)
    return pl.pallas_call(
        correlate_kernel,
        grid=(slots // 2,),
        in_specs=[
            pl.BlockSpec((2, block_count, rows, width), lambda q: (q, 0, 0, 0)),
            pl.BlockSpec((2, block_count, k_count, width), lambda q: (q, 0, 0, 0)),
            pl.BlockSpec((width, lag_count), lambda q: (0, 0)),
        ],
        out_specs=pl.BlockSpec((2, k_count * rows, lag_count), lambda q: (q, 0, 0)),
        out_shape=jax.ShapeDtypeStruct((slots, k_count * rows, lag_count), jnp.bfloat16),
        scratch_shapes=[pltpu.VMEM((k_count * rows, width), jnp.bfloat16)],
        cost_estimate=pl.CostEstimate(
            flops=flops,
            bytes_accessed=2 * (left.size // left.shape[2] * rows + sources.size + lag_rows.size)
            + 2 * slots * k_count * rows * lag_count,
            transcendentals=0,
        ),
    )(left, sources, lag_rows)


def row_counts(channel_segment, segment_row, owner):
    held_rows = owner * SEG_PER + jnp.arange(SEG_PER, dtype=jnp.int32)
    matches = segment_row[None, :] == held_rows[:, None]
    segment_ids = jnp.arange(segment_row.shape[0], dtype=jnp.int32)
    held_segments = jnp.sum(jnp.where(matches, segment_ids[None, :], 0), axis=1)
    members = channel_segment[None, :] == held_segments[:, None]
    return jnp.sum(members.astype(jnp.float32), axis=1)


def shift_perm(count, shift):
    return [(i, (i + shift) % count) for i in range(count)]


def gather_relative(value, axis, count):
    if count != 4:
        parts = [value] + [lax.ppermute(value, axis, shift_perm(count, s)) for s in range(1, count)]
        return jnp.stack(parts)
    half = value.shape[-1] // 2
    from_left = lax.ppermute(value, axis, shift_perm(count, 1))
    from_right = lax.ppermute(value, axis, shift_perm(count, -1))
    far_head = lax.ppermute(from_left[..., :half], axis, shift_perm(count, 1))
    far_tail = lax.ppermute(from_right[..., half:], axis, shift_perm(count, -1))
    far = jnp.concatenate([far_head, far_tail], axis=-1)
    return jnp.stack([value, from_left, far, from_right])


def scatter_sum(value, axis, count):
    me = lax.axis_index(axis)
    blocks = value.reshape((count, value.shape[0] // count) + value.shape[1:])

    def block(offset):
        return lax.dynamic_index_in_dim(blocks, (me + offset) % count, axis=0, keepdims=False)

    if count != 4:
        total = block(0)
        for s in range(1, count):
            total = total + lax.ppermute(block(s), axis, shift_perm(count, s))
        return total
    half = blocks.shape[-1] // 2
    right, left, far, own = block(1), block(-1), block(2), block(0)
    to_right = jnp.concatenate([right[..., half:], far[..., :half]], axis=-1)
    to_left = jnp.concatenate([left[..., :half], far[..., half:]], axis=-1)
    got_left = lax.ppermute(to_right, axis, shift_perm(count, 1))
    got_right = lax.ppermute(to_left, axis, shift_perm(count, -1))
    fwd_right = right[..., :half] + got_left[..., half:]
    fwd_left = left[..., half:] + got_right[..., half:]
    got2_left = lax.ppermute(fwd_right, axis, shift_perm(count, 1))
    got2_right = lax.ppermute(fwd_left, axis, shift_perm(count, -1))
    head = own[..., :half] + got_right[..., :half] + got2_left
    tail = own[..., half:] + got_left[..., :half] + got2_right
    return jnp.concatenate([head, tail], axis=-1)


def scatter_sum_direct(value, axis, count):
    me = lax.axis_index(axis)
    blocks = value.reshape((count, value.shape[0] // count) + value.shape[1:])
    total = lax.dynamic_index_in_dim(blocks, me, axis=0, keepdims=False)
    for s in range(1, count):
        piece = lax.dynamic_index_in_dim(blocks, (me + s) % count, axis=0, keepdims=False)
        sent = lax.ppermute(piece.astype(jnp.bfloat16), axis, shift_perm(count, s))
        total = total + sent.astype(jnp.float32)
    return total


def on_device(records, window_start, channel_segment, segment_row):
    tile_size = records.shape[0]
    block_count = records.shape[1] // NFFT
    sizes = {name: lax.axis_size(name) for name in ("x", "zl", "y", "zh", "core")}
    src_count = sizes["zh"] * sizes["core"]
    x_i, zl_i, y_i = lax.axis_index("x"), lax.axis_index("zl"), lax.axis_index("y")
    zh_i, core_i = lax.axis_index("zh"), lax.axis_index("core")
    group_index = (x_i * sizes["zl"] + zl_i) * sizes["y"] + y_i
    position = zh_i * sizes["core"] + core_i
    segment_total = segment_row.shape[0]

    blocks = records.reshape(tile_size * block_count, NFFT)
    spectrum = jnp.dot(
        blocks, dft_table(NFFT), precision=lax.Precision.HIGHEST, preferred_element_type=jnp.float32
    )
    white = whiten(spectrum).astype(jnp.bfloat16).reshape(tile_size, block_count, NFFT)
    start_row = jnp.zeros((1, block_count, NFFT), jnp.bfloat16).at[0, 0, 0].set(
        window_start[0].astype(jnp.bfloat16)
    )
    extended = jnp.concatenate([white, start_row], axis=0).transpose(1, 0, 2)
    gathered = gather_relative(extended, "zh", sizes["zh"])
    partner = lax.ppermute(gathered, "core", shift_perm(sizes["core"], 1))
    gathered = jnp.stack([gathered, partner]).reshape(src_count, block_count, tile_size + 1, NFFT)
    starts = gathered[:, 0, tile_size, 0].astype(jnp.int32)
    group_size = src_count * tile_size
    window_total = group_size // 4
    k_per = window_total // src_count

    slot = jnp.arange(src_count, dtype=jnp.int32)
    slot_zh = (zh_i - slot % sizes["zh"]) % sizes["zh"]
    slot_core = (core_i + slot // sizes["zh"]) % sizes["core"]
    slot_position = slot_zh * sizes["core"] + slot_core
    k_idx = position * k_per + jnp.arange(k_per, dtype=jnp.int32)
    window_idx = starts[:, None] + k_idx[None, :]
    tile_first = (slot_position * tile_size)[:, None]
    source_idx = jnp.where(window_idx < tile_first, window_idx, window_idx + tile_size)
    source_pos = source_idx // tile_size
    source_slot = ((source_pos % sizes["core"] - core_i) % sizes["core"]) * sizes["zh"] + (
        zh_i - source_pos // sizes["core"]
    ) % sizes["zh"]
    source_row = (source_slot * (tile_size + 1) + source_idx % tile_size).reshape(-1)
    sources = jnp.stack(
        [
            jnp.take(gathered[:, b].reshape(-1, NFFT), source_row, axis=0).reshape(
                src_count, k_per, NFFT
            )
            for b in range(block_count)
        ],
        axis=1,
    )
    correlation = correlate(gathered, sources, lag_table(NFFT, LAGS), tile_size)
    correlation = correlation.reshape(src_count, k_per, tile_size, LAGS)

    channel_ids = (slot_position[:, None] * tile_size + jnp.arange(tile_size, dtype=jnp.int32)[None, :]).reshape(-1)
    group_segments = jnp.take(channel_segment, group_index * group_size + channel_ids)
    seg_match = group_segments[:, None] == jnp.arange(segment_total, dtype=jnp.int32)[None, :]
    group_rows = jnp.sum(jnp.where(seg_match, segment_row[None, :], 0), axis=1)
    staged_rows = group_rows
    onehot = (
        jnp.arange(segment_total, dtype=jnp.int32)[:, None] == staged_rows[None, :]
    ).astype(jnp.bfloat16)
    onehot = onehot.reshape(segment_total, src_count, tile_size)
    partial = jnp.einsum("rqi,qkim->rkm", onehot, correlation, preferred_element_type=jnp.float32)
    owners = sizes["x"] * sizes["zl"] * sizes["y"]
    pieces = partial.astype(jnp.bfloat16).reshape((owners, partial.shape[0] // owners) + partial.shape[1:])
    arrived = lax.all_to_all(pieces, ("x", "zl", "y"), split_axis=0, concat_axis=0, tiled=True)
    summed = jnp.sum(arrived.astype(jnp.float32), axis=0)
    counts = row_counts(channel_segment, segment_row, group_index)
    return summed / jnp.sqrt(jnp.maximum(counts, 1.0))[:, None, None]


def solution(mesh):
    names = ("x", "zl", "y", "zh", "core")
    rcv_count, src_count = mesh.devices.shape
    zh_count = src_count // 2
    side = round(rcv_count ** (1 / 3))
    fine = Mesh(mesh.devices.reshape(side, side, rcv_count // side // side, zh_count, 2), names)
    rcv, src = ("x", "zl", "y"), ("zh", "core")
    in_specs = (P(rcv + src, None), P(rcv + src), P(), P())
    out_specs = P(rcv, src, None)
    return jax.shard_map(
        on_device, mesh=fine, in_specs=in_specs, out_specs=out_specs, check_vma=False
    )
```

```python
import math

import jax
import jax.numpy as jnp
from jax import lax
from jax.experimental import pallas as pl
from jax.experimental.pallas import tpu as pltpu
from jax.sharding import Mesh, PartitionSpec as P

NFFT = 1024
LAGS = 256
SEG_PER = 4


def dft_table(length):
    fine_count = 32
    coarse_count = length // fine_count
    frequency = jnp.arange(length // 2, dtype=jnp.int32)
    scale = 2.0 * math.pi / length

    def angle_table(steps, stride):
        index = (jnp.arange(steps, dtype=jnp.int32)[:, None] * stride * frequency[None, :]) % length
        angles = index.astype(jnp.float32) * scale
        return jnp.cos(angles), jnp.sin(angles)

    coarse_cos, coarse_sin = angle_table(coarse_count, fine_count)
    fine_cos, fine_sin = angle_table(fine_count, 1)
    cos_part = coarse_cos[:, None] * fine_cos[None] - coarse_sin[:, None] * fine_sin[None]
    sin_part = coarse_sin[:, None] * fine_cos[None] + coarse_cos[:, None] * fine_sin[None]
    return jnp.concatenate([cos_part, -sin_part], axis=-1).reshape(length, length)


def lag_table(length, lag_count):
    frequency = jnp.arange(length // 2, dtype=jnp.int32)
    shifts = jnp.arange(lag_count, dtype=jnp.int32) - lag_count // 2
    angles = (frequency[:, None] * shifts[None, :] % length).astype(jnp.float32) * (
        2.0 * math.pi / length
    )
    return jnp.concatenate([jnp.cos(angles), -jnp.sin(angles)], axis=0).astype(jnp.bfloat16)


def whiten(spectrum):
    half_size = spectrum.shape[-1] // 2
    powers = spectrum[..., :half_size] ** 2 + spectrum[..., half_size:] ** 2
    mean_power = jnp.mean(powers, axis=-1, keepdims=True)
    magnitude = jnp.sqrt(powers + 0.1 * mean_power + 1e-06)
    return spectrum / jnp.concatenate([magnitude, magnitude], axis=-1)


def correlate_kernel(left_ref, src_ref, lag_ref, out_ref, cross_ref):
    block_count, rows, width = left_ref.shape[1], left_ref.shape[2], left_ref.shape[3]
    k_count = src_ref.shape[2]
    half = width // 2
    for slot in range(left_ref.shape[0]):
        left = [left_ref[slot, b].astype(jnp.float32) for b in range(block_count)]
        source_rows = [src_ref[slot, b].astype(jnp.float32) for b in range(block_count)]
        for k in range(k_count):
            real_part = None
            imag_part = None
            for b in range(block_count):
                source = source_rows[b][k:k + 1, :]
                l_re, l_im = left[b][:, :half], left[b][:, half:]
                s_re, s_im = source[:, :half], source[:, half:]
                re_term = l_re * s_re + l_im * s_im
                im_term = l_re * s_im - l_im * s_re
                real_part = re_term if real_part is None else real_part + re_term
                imag_part = im_term if imag_part is None else imag_part + im_term
            cross_ref[k * rows:(k + 1) * rows, :half] = real_part.astype(jnp.bfloat16)
            cross_ref[k * rows:(k + 1) * rows, half:] = imag_part.astype(jnp.bfloat16)
        product = jnp.dot(cross_ref[...], lag_ref[...], preferred_element_type=jnp.float32)
        out_ref[slot] = (product / math.sqrt(block_count * half)).astype(out_ref.dtype)


def correlate(left, sources, lag_rows, rows):
    slots, block_count, _, width = left.shape
    k_count = sources.shape[2]
    lag_count = lag_rows.shape[1]
    flops = slots * k_count * rows * (block_count * width * 4 + 2 * width * lag_count)
    return pl.pallas_call(
        correlate_kernel,
        grid=(slots // 4,),
        in_specs=[
            pl.BlockSpec((4, block_count, rows, width), lambda q: (q, 0, 0, 0)),
            pl.BlockSpec((4, block_count, k_count, width), lambda q: (q, 0, 0, 0)),
            pl.BlockSpec((width, lag_count), lambda q: (0, 0)),
        ],
        out_specs=pl.BlockSpec((4, k_count * rows, lag_count), lambda q: (q, 0, 0)),
        out_shape=jax.ShapeDtypeStruct((slots, k_count * rows, lag_count), jnp.bfloat16),
        scratch_shapes=[pltpu.VMEM((k_count * rows, width), jnp.bfloat16)],
        cost_estimate=pl.CostEstimate(
            flops=flops,
            bytes_accessed=2 * (left.size // left.shape[2] * rows + sources.size + lag_rows.size)
            + 2 * slots * k_count * rows * lag_count,
            transcendentals=0,
        ),
    )(left, sources, lag_rows)


def row_counts(channel_segment, segment_row, owner):
    held_rows = owner * SEG_PER + jnp.arange(SEG_PER, dtype=jnp.int32)
    matches = segment_row[None, :] == held_rows[:, None]
    segment_ids = jnp.arange(segment_row.shape[0], dtype=jnp.int32)
    held_segments = jnp.sum(jnp.where(matches, segment_ids[None, :], 0), axis=1)
    members = channel_segment[None, :] == held_segments[:, None]
    return jnp.sum(members.astype(jnp.float32), axis=1)


def shift_perm(count, shift):
    return [(i, (i + shift) % count) for i in range(count)]


def gather_relative(value, axis, count):
    if count != 4:
        parts = [value] + [lax.ppermute(value, axis, shift_perm(count, s)) for s in range(1, count)]
        return jnp.stack(parts)
    half = value.shape[-1] // 2
    from_left = lax.ppermute(value, axis, shift_perm(count, 1))
    from_right = lax.ppermute(value, axis, shift_perm(count, -1))
    far_head = lax.ppermute(from_left[..., :half], axis, shift_perm(count, 1))
    far_tail = lax.ppermute(from_right[..., half:], axis, shift_perm(count, -1))
    far = jnp.concatenate([far_head, far_tail], axis=-1)
    return jnp.stack([value, from_left, far, from_right])


def scatter_sum(value, axis, count):
    me = lax.axis_index(axis)
    blocks = value.reshape((count, value.shape[0] // count) + value.shape[1:])

    def block(offset):
        return lax.dynamic_index_in_dim(blocks, (me + offset) % count, axis=0, keepdims=False)

    if count != 4:
        total = block(0)
        for s in range(1, count):
            total = total + lax.ppermute(block(s), axis, shift_perm(count, s))
        return total
    half = blocks.shape[-1] // 2
    right, left, far, own = block(1), block(-1), block(2), block(0)
    to_right = jnp.concatenate([right[..., half:], far[..., :half]], axis=-1)
    to_left = jnp.concatenate([left[..., :half], far[..., half:]], axis=-1)
    got_left = lax.ppermute(to_right, axis, shift_perm(count, 1))
    got_right = lax.ppermute(to_left, axis, shift_perm(count, -1))
    fwd_right = right[..., :half] + got_left[..., half:]
    fwd_left = left[..., half:] + got_right[..., half:]
    got2_left = lax.ppermute(fwd_right, axis, shift_perm(count, 1))
    got2_right = lax.ppermute(fwd_left, axis, shift_perm(count, -1))
    head = own[..., :half] + got_right[..., :half] + got2_left
    tail = own[..., half:] + got_left[..., :half] + got2_right
    return jnp.concatenate([head, tail], axis=-1)


def scatter_sum_direct(value, axis, count):
    me = lax.axis_index(axis)
    blocks = value.reshape((count, value.shape[0] // count) + value.shape[1:])
    total = lax.dynamic_index_in_dim(blocks, me, axis=0, keepdims=False)
    for s in range(1, count):
        piece = lax.dynamic_index_in_dim(blocks, (me + s) % count, axis=0, keepdims=False)
        sent = lax.ppermute(piece.astype(jnp.bfloat16), axis, shift_perm(count, s))
        total = total + sent.astype(jnp.float32)
    return total


def on_device(records, window_start, channel_segment, segment_row):
    tile_size = records.shape[0]
    block_count = records.shape[1] // NFFT
    sizes = {name: lax.axis_size(name) for name in ("x", "zl", "y", "zh", "core")}
    src_count = sizes["zh"] * sizes["core"]
    x_i, zl_i, y_i = lax.axis_index("x"), lax.axis_index("zl"), lax.axis_index("y")
    zh_i, core_i = lax.axis_index("zh"), lax.axis_index("core")
    group_index = (x_i * sizes["zl"] + zl_i) * sizes["y"] + y_i
    position = zh_i * sizes["core"] + core_i
    segment_total = segment_row.shape[0]

    blocks = records.reshape(tile_size * block_count, NFFT)
    spectrum = jnp.dot(
        blocks, dft_table(NFFT), precision=lax.Precision.HIGHEST, preferred_element_type=jnp.float32
    )
    white = whiten(spectrum).astype(jnp.bfloat16).reshape(tile_size, block_count, NFFT)
    start_row = jnp.zeros((1, block_count, NFFT), jnp.bfloat16).at[0, 0, 0].set(
        window_start[0].astype(jnp.bfloat16)
    )
    extended = jnp.concatenate([white, start_row], axis=0).transpose(1, 0, 2)
    gathered = gather_relative(extended, "zh", sizes["zh"])
    partner = lax.ppermute(gathered, "core", shift_perm(sizes["core"], 1))
    gathered = jnp.stack([gathered, partner]).reshape(src_count, block_count, tile_size + 1, NFFT)
    starts = gathered[:, 0, tile_size, 0].astype(jnp.int32)
    group_size = src_count * tile_size
    window_total = group_size // 4
    k_per = window_total // src_count

    slot = jnp.arange(src_count, dtype=jnp.int32)
    slot_zh = (zh_i - slot % sizes["zh"]) % sizes["zh"]
    slot_core = (core_i + slot // sizes["zh"]) % sizes["core"]
    slot_position = slot_zh * sizes["core"] + slot_core
    k_idx = position * k_per + jnp.arange(k_per, dtype=jnp.int32)
    window_idx = starts[:, None] + k_idx[None, :]
    tile_first = (slot_position * tile_size)[:, None]
    source_idx = jnp.where(window_idx < tile_first, window_idx, window_idx + tile_size)
    source_pos = source_idx // tile_size
    source_slot = ((source_pos % sizes["core"] - core_i) % sizes["core"]) * sizes["zh"] + (
        zh_i - source_pos // sizes["core"]
    ) % sizes["zh"]
    source_row = (source_slot * (tile_size + 1) + source_idx % tile_size).reshape(-1)
    sources = jnp.stack(
        [
            jnp.take(gathered[:, b].reshape(-1, NFFT), source_row, axis=0).reshape(
                src_count, k_per, NFFT
            )
            for b in range(block_count)
        ],
        axis=1,
    )
    correlation = correlate(gathered, sources, lag_table(NFFT, LAGS), tile_size)
    correlation = correlation.reshape(src_count, k_per, tile_size, LAGS)

    channel_ids = (slot_position[:, None] * tile_size + jnp.arange(tile_size, dtype=jnp.int32)[None, :]).reshape(-1)
    group_segments = jnp.take(channel_segment, group_index * group_size + channel_ids)
    seg_match = group_segments[:, None] == jnp.arange(segment_total, dtype=jnp.int32)[None, :]
    group_rows = jnp.sum(jnp.where(seg_match, segment_row[None, :], 0), axis=1)
    staged_rows = group_rows
    onehot = (
        jnp.arange(segment_total, dtype=jnp.int32)[:, None] == staged_rows[None, :]
    ).astype(jnp.bfloat16)
    onehot = onehot.reshape(segment_total, src_count, tile_size)
    partial = jnp.einsum("rqi,qkim->rkm", onehot, correlation, preferred_element_type=jnp.float32)
    owners = sizes["x"] * sizes["zl"] * sizes["y"]
    pieces = partial.astype(jnp.bfloat16).reshape((owners, partial.shape[0] // owners) + partial.shape[1:])
    arrived = lax.all_to_all(pieces, ("x", "zl", "y"), split_axis=0, concat_axis=0, tiled=True)
    summed = jnp.sum(arrived.astype(jnp.float32), axis=0)
    counts = row_counts(channel_segment, segment_row, group_index)
    return summed / jnp.sqrt(jnp.maximum(counts, 1.0))[:, None, None]


def solution(mesh):
    names = ("x", "zl", "y", "zh", "core")
    rcv_count, src_count = mesh.devices.shape
    zh_count = src_count // 2
    side = round(rcv_count ** (1 / 3))
    fine = Mesh(mesh.devices.reshape(side, side, rcv_count // side // side, zh_count, 2), names)
    rcv, src = ("x", "zl", "y"), ("zh", "core")
    in_specs = (P(rcv + src, None), P(rcv + src), P(), P())
    out_specs = P(rcv, src, None)
    return jax.shard_map(
        on_device, mesh=fine, in_specs=in_specs, out_specs=out_specs, check_vma=False
    )
```

```python
import math

import jax
import jax.numpy as jnp
from jax import lax
from jax.experimental import pallas as pl
from jax.experimental.pallas import tpu as pltpu
from jax.sharding import Mesh, PartitionSpec as P

NFFT = 1024
LAGS = 256
SEG_PER = 4


def dft_table(length):
    fine_count = 32
    coarse_count = length // fine_count
    frequency = jnp.arange(length // 2, dtype=jnp.int32)
    scale = 2.0 * math.pi / length

    def angle_table(steps, stride):
        index = (jnp.arange(steps, dtype=jnp.int32)[:, None] * stride * frequency[None, :]) % length
        angles = index.astype(jnp.float32) * scale
        return jnp.cos(angles), jnp.sin(angles)

    coarse_cos, coarse_sin = angle_table(coarse_count, fine_count)
    fine_cos, fine_sin = angle_table(fine_count, 1)
    cos_part = coarse_cos[:, None] * fine_cos[None] - coarse_sin[:, None] * fine_sin[None]
    sin_part = coarse_sin[:, None] * fine_cos[None] + coarse_cos[:, None] * fine_sin[None]
    return jnp.concatenate([cos_part, -sin_part], axis=-1).reshape(length, length)


def lag_table(length, lag_count):
    frequency = jnp.arange(length // 2, dtype=jnp.int32)
    shifts = jnp.arange(lag_count, dtype=jnp.int32) - lag_count // 2
    angles = (frequency[:, None] * shifts[None, :] % length).astype(jnp.float32) * (
        2.0 * math.pi / length
    )
    return jnp.concatenate([jnp.cos(angles), -jnp.sin(angles)], axis=0).astype(jnp.bfloat16)


def whiten(spectrum):
    half_size = spectrum.shape[-1] // 2
    powers = spectrum[..., :half_size] ** 2 + spectrum[..., half_size:] ** 2
    mean_power = jnp.mean(powers, axis=-1, keepdims=True)
    magnitude = jnp.sqrt(powers + 0.1 * mean_power + 1e-06)
    return spectrum / jnp.concatenate([magnitude, magnitude], axis=-1)


def correlate_kernel(left_ref, src_ref, lag_ref, onehot_ref, out_ref, cross_ref, acc_ref):
    block_count, rows, width = left_ref.shape[1], left_ref.shape[2], left_ref.shape[3]
    k_count = src_ref.shape[2]
    half = width // 2

    @pl.when(pl.program_id(0) == 0)
    def _():
        acc_ref[...] = jnp.zeros_like(acc_ref)

    for slot in range(left_ref.shape[0]):
        left = [left_ref[slot, b].astype(jnp.float32) for b in range(block_count)]
        source_rows = [src_ref[slot, b].astype(jnp.float32) for b in range(block_count)]
        for k in range(k_count):
            real_part = None
            imag_part = None
            for b in range(block_count):
                source = source_rows[b][k:k + 1, :]
                l_re, l_im = left[b][:, :half], left[b][:, half:]
                s_re, s_im = source[:, :half], source[:, half:]
                re_term = l_re * s_re + l_im * s_im
                im_term = l_re * s_im - l_im * s_re
                real_part = re_term if real_part is None else real_part + re_term
                imag_part = im_term if imag_part is None else imag_part + im_term
            cross_ref[k * rows:(k + 1) * rows, :half] = real_part.astype(jnp.bfloat16)
            cross_ref[k * rows:(k + 1) * rows, half:] = imag_part.astype(jnp.bfloat16)
        product = jnp.dot(cross_ref[...], lag_ref[...], preferred_element_type=jnp.float32)
        correlation = (product / math.sqrt(block_count * half)).astype(jnp.bfloat16)
        lag_count = correlation.shape[-1]
        members = onehot_ref[slot]
        for k in range(k_count):
            stacked = jnp.dot(
                members, correlation[k * rows:(k + 1) * rows], preferred_element_type=jnp.float32
            )
            acc_ref[:, k * lag_count:(k + 1) * lag_count] += stacked

    @pl.when(pl.program_id(0) == pl.num_programs(0) - 1)
    def _():
        out_ref[...] = acc_ref[...].astype(out_ref.dtype)


def correlate(left, sources, lag_rows, onehot, rows):
    slots, block_count, _, width = left.shape
    k_count = sources.shape[2]
    lag_count = lag_rows.shape[1]
    row_total = onehot.shape[1]
    step = 4
    flops = slots * k_count * rows * (block_count * width * 4 + 2 * width * lag_count + 2 * row_total * lag_count)
    return pl.pallas_call(
        correlate_kernel,
        grid=(slots // step,),
        in_specs=[
            pl.BlockSpec((step, block_count, rows, width), lambda q: (q, 0, 0, 0)),
            pl.BlockSpec((step, block_count, k_count, width), lambda q: (q, 0, 0, 0)),
            pl.BlockSpec((width, lag_count), lambda q: (0, 0)),
            pl.BlockSpec((step, row_total, rows), lambda q: (q, 0, 0)),
        ],
        out_specs=pl.BlockSpec((row_total, k_count * lag_count), lambda q: (0, 0)),
        out_shape=jax.ShapeDtypeStruct((row_total, k_count * lag_count), jnp.bfloat16),
        scratch_shapes=[
            pltpu.VMEM((k_count * rows, width), jnp.bfloat16),
            pltpu.VMEM((row_total, k_count * lag_count), jnp.float32),
        ],
        cost_estimate=pl.CostEstimate(
            flops=flops,
            bytes_accessed=2 * (left.size // left.shape[2] * rows + sources.size + lag_rows.size + onehot.size)
            + 2 * row_total * k_count * lag_count,
            transcendentals=0,
        ),
    )(left, sources, lag_rows, onehot)


def row_counts(channel_segment, segment_row, owner):
    held_rows = owner * SEG_PER + jnp.arange(SEG_PER, dtype=jnp.int32)
    matches = segment_row[None, :] == held_rows[:, None]
    segment_ids = jnp.arange(segment_row.shape[0], dtype=jnp.int32)
    held_segments = jnp.sum(jnp.where(matches, segment_ids[None, :], 0), axis=1)
    members = channel_segment[None, :] == held_segments[:, None]
    return jnp.sum(members.astype(jnp.float32), axis=1)


def shift_perm(count, shift):
    return [(i, (i + shift) % count) for i in range(count)]


def gather_relative(value, axis, count):
    if count != 4:
        parts = [value] + [lax.ppermute(value, axis, shift_perm(count, s)) for s in range(1, count)]
        return jnp.stack(parts)
    half = value.shape[-1] // 2
    from_left = lax.ppermute(value, axis, shift_perm(count, 1))
    from_right = lax.ppermute(value, axis, shift_perm(count, -1))
    far_head = lax.ppermute(from_left[..., :half], axis, shift_perm(count, 1))
    far_tail = lax.ppermute(from_right[..., half:], axis, shift_perm(count, -1))
    far = jnp.concatenate([far_head, far_tail], axis=-1)
    return jnp.stack([value, from_left, far, from_right])


def scatter_sum(value, axis, count):
    me = lax.axis_index(axis)
    blocks = value.reshape((count, value.shape[0] // count) + value.shape[1:])

    def block(offset):
        return lax.dynamic_index_in_dim(blocks, (me + offset) % count, axis=0, keepdims=False)

    if count != 4:
        total = block(0)
        for s in range(1, count):
            total = total + lax.ppermute(block(s), axis, shift_perm(count, s))
        return total
    half = blocks.shape[-1] // 2
    right, left, far, own = block(1), block(-1), block(2), block(0)
    to_right = jnp.concatenate([right[..., half:], far[..., :half]], axis=-1)
    to_left = jnp.concatenate([left[..., :half], far[..., half:]], axis=-1)
    got_left = lax.ppermute(to_right, axis, shift_perm(count, 1))
    got_right = lax.ppermute(to_left, axis, shift_perm(count, -1))
    fwd_right = right[..., :half] + got_left[..., half:]
    fwd_left = left[..., half:] + got_right[..., half:]
    got2_left = lax.ppermute(fwd_right, axis, shift_perm(count, 1))
    got2_right = lax.ppermute(fwd_left, axis, shift_perm(count, -1))
    head = own[..., :half] + got_right[..., :half] + got2_left
    tail = own[..., half:] + got_left[..., :half] + got2_right
    return jnp.concatenate([head, tail], axis=-1)


def scatter_sum_direct(value, axis, count):
    me = lax.axis_index(axis)
    blocks = value.reshape((count, value.shape[0] // count) + value.shape[1:])
    total = lax.dynamic_index_in_dim(blocks, me, axis=0, keepdims=False)
    for s in range(1, count):
        piece = lax.dynamic_index_in_dim(blocks, (me + s) % count, axis=0, keepdims=False)
        sent = lax.ppermute(piece.astype(jnp.bfloat16), axis, shift_perm(count, s))
        total = total + sent.astype(jnp.float32)
    return total


def on_device(records, window_start, channel_segment, segment_row):
    tile_size = records.shape[0]
    block_count = records.shape[1] // NFFT
    sizes = {name: lax.axis_size(name) for name in ("x", "zl", "y", "zh", "core")}
    src_count = sizes["zh"] * sizes["core"]
    x_i, zl_i, y_i = lax.axis_index("x"), lax.axis_index("zl"), lax.axis_index("y")
    zh_i, core_i = lax.axis_index("zh"), lax.axis_index("core")
    group_index = (x_i * sizes["zl"] + zl_i) * sizes["y"] + y_i
    position = zh_i * sizes["core"] + core_i
    segment_total = segment_row.shape[0]

    blocks = records.reshape(tile_size * block_count, NFFT)
    spectrum = jnp.dot(
        blocks, dft_table(NFFT), precision=lax.Precision.HIGHEST, preferred_element_type=jnp.float32
    )
    white = whiten(spectrum).astype(jnp.bfloat16).reshape(tile_size, block_count, NFFT)
    start_row = jnp.zeros((1, block_count, NFFT), jnp.bfloat16).at[0, 0, 0].set(
        window_start[0].astype(jnp.bfloat16)
    )
    extended = jnp.concatenate([white, start_row], axis=0).transpose(1, 0, 2)
    gathered = gather_relative(extended, "zh", sizes["zh"])
    partner = lax.ppermute(gathered, "core", shift_perm(sizes["core"], 1))
    gathered = jnp.stack([gathered, partner]).reshape(src_count, block_count, tile_size + 1, NFFT)
    starts = gathered[:, 0, tile_size, 0].astype(jnp.int32)
    group_size = src_count * tile_size
    window_total = group_size // 4
    k_per = window_total // src_count

    slot = jnp.arange(src_count, dtype=jnp.int32)
    slot_zh = (zh_i - slot % sizes["zh"]) % sizes["zh"]
    slot_core = (core_i + slot // sizes["zh"]) % sizes["core"]
    slot_position = slot_zh * sizes["core"] + slot_core
    k_idx = position * k_per + jnp.arange(k_per, dtype=jnp.int32)
    window_idx = starts[:, None] + k_idx[None, :]
    tile_first = (slot_position * tile_size)[:, None]
    source_idx = jnp.where(window_idx < tile_first, window_idx, window_idx + tile_size)
    source_pos = source_idx // tile_size
    source_slot = ((source_pos % sizes["core"] - core_i) % sizes["core"]) * sizes["zh"] + (
        zh_i - source_pos // sizes["core"]
    ) % sizes["zh"]
    source_row = (source_slot * (tile_size + 1) + source_idx % tile_size).reshape(-1)
    sources = jnp.stack(
        [
            jnp.take(gathered[:, b].reshape(-1, NFFT), source_row, axis=0).reshape(
                src_count, k_per, NFFT
            )
            for b in range(block_count)
        ],
        axis=1,
    )
    channel_ids = (slot_position[:, None] * tile_size + jnp.arange(tile_size, dtype=jnp.int32)[None, :]).reshape(-1)
    group_segments = jnp.take(channel_segment, group_index * group_size + channel_ids)
    seg_match = group_segments[:, None] == jnp.arange(segment_total, dtype=jnp.int32)[None, :]
    group_rows = jnp.sum(jnp.where(seg_match, segment_row[None, :], 0), axis=1).reshape(src_count, tile_size)
    onehot = (
        jnp.arange(segment_total, dtype=jnp.int32)[None, :, None] == group_rows[:, None, :]
    ).astype(jnp.bfloat16)
    stacked = correlate(gathered, sources, lag_table(NFFT, LAGS), onehot, tile_size)
    owners = sizes["x"] * sizes["zl"] * sizes["y"]
    pieces = stacked.reshape(owners, segment_total // owners, k_per, LAGS)
    arrived = lax.all_to_all(pieces, ("x", "zl", "y"), split_axis=0, concat_axis=0, tiled=True)
    summed = jnp.sum(arrived.astype(jnp.float32), axis=0)
    counts = row_counts(channel_segment, segment_row, group_index)
    return summed / jnp.sqrt(jnp.maximum(counts, 1.0))[:, None, None]


def solution(mesh):
    names = ("x", "zl", "y", "zh", "core")
    rcv_count, src_count = mesh.devices.shape
    zh_count = src_count // 2
    side = round(rcv_count ** (1 / 3))
    fine = Mesh(mesh.devices.reshape(side, side, rcv_count // side // side, zh_count, 2), names)
    rcv, src = ("x", "zl", "y"), ("zh", "core")
    in_specs = (P(rcv + src, None), P(rcv + src), P(), P())
    out_specs = P(rcv, src, None)
    return jax.shard_map(
        on_device, mesh=fine, in_specs=in_specs, out_specs=out_specs, check_vma=False
    )
```

```python
import math

import jax
import jax.numpy as jnp
from jax import lax
from jax.experimental import pallas as pl
from jax.experimental.pallas import tpu as pltpu
from jax.sharding import Mesh, PartitionSpec as P

NFFT = 1024
LAGS = 256
SEG_PER = 4


def dft_table(length):
    fine_count = 32
    coarse_count = length // fine_count
    frequency = jnp.arange(length // 2, dtype=jnp.int32)
    scale = 2.0 * math.pi / length

    def angle_table(steps, stride):
        index = (jnp.arange(steps, dtype=jnp.int32)[:, None] * stride * frequency[None, :]) % length
        angles = index.astype(jnp.float32) * scale
        return jnp.cos(angles), jnp.sin(angles)

    coarse_cos, coarse_sin = angle_table(coarse_count, fine_count)
    fine_cos, fine_sin = angle_table(fine_count, 1)
    cos_part = coarse_cos[:, None] * fine_cos[None] - coarse_sin[:, None] * fine_sin[None]
    sin_part = coarse_sin[:, None] * fine_cos[None] + coarse_cos[:, None] * fine_sin[None]
    return jnp.concatenate([cos_part, -sin_part], axis=-1).reshape(length, length)


def lag_table(length, lag_count):
    frequency = jnp.arange(length // 2, dtype=jnp.int32)
    shifts = jnp.arange(lag_count, dtype=jnp.int32) - lag_count // 2
    angles = (frequency[:, None] * shifts[None, :] % length).astype(jnp.float32) * (
        2.0 * math.pi / length
    )
    return jnp.concatenate([jnp.cos(angles), -jnp.sin(angles)], axis=0).astype(jnp.bfloat16)


def whiten(spectrum):
    half_size = spectrum.shape[-1] // 2
    powers = spectrum[..., :half_size] ** 2 + spectrum[..., half_size:] ** 2
    mean_power = jnp.mean(powers, axis=-1, keepdims=True)
    magnitude = jnp.sqrt(powers + 0.1 * mean_power + 1e-06)
    return spectrum / jnp.concatenate([magnitude, magnitude], axis=-1)


def correlate_kernel(left_ref, src_ref, lag_ref, out_ref, cross_ref):
    block_count, rows, width = left_ref.shape[1], left_ref.shape[2], left_ref.shape[3]
    k_count = src_ref.shape[2]
    half = width // 2
    for slot in range(left_ref.shape[0]):
        left = [left_ref[slot, b].astype(jnp.float32) for b in range(block_count)]
        source_rows = [src_ref[slot, b].astype(jnp.float32) for b in range(block_count)]
        for k in range(k_count):
            real_part = None
            imag_part = None
            for b in range(block_count):
                source = source_rows[b][k:k + 1, :]
                l_re, l_im = left[b][:, :half], left[b][:, half:]
                s_re, s_im = source[:, :half], source[:, half:]
                re_term = l_re * s_re + l_im * s_im
                im_term = l_re * s_im - l_im * s_re
                real_part = re_term if real_part is None else real_part + re_term
                imag_part = im_term if imag_part is None else imag_part + im_term
            cross_ref[k * rows:(k + 1) * rows, :half] = real_part.astype(jnp.bfloat16)
            cross_ref[k * rows:(k + 1) * rows, half:] = imag_part.astype(jnp.bfloat16)
        product = jnp.dot(cross_ref[...], lag_ref[...], preferred_element_type=jnp.float32)
        out_ref[slot] = (product / math.sqrt(block_count * half)).astype(out_ref.dtype)


def correlate(left, sources, lag_rows, rows):
    slots, block_count, _, width = left.shape
    k_count = sources.shape[2]
    lag_count = lag_rows.shape[1]
    flops = slots * k_count * rows * (block_count * width * 4 + 2 * width * lag_count)
    return pl.pallas_call(
        correlate_kernel,
        grid=(slots // 4,),
        in_specs=[
            pl.BlockSpec((4, block_count, rows, width), lambda q: (q, 0, 0, 0)),
            pl.BlockSpec((4, block_count, k_count, width), lambda q: (q, 0, 0, 0)),
            pl.BlockSpec((width, lag_count), lambda q: (0, 0)),
        ],
        out_specs=pl.BlockSpec((4, k_count * rows, lag_count), lambda q: (q, 0, 0)),
        out_shape=jax.ShapeDtypeStruct((slots, k_count * rows, lag_count), jnp.bfloat16),
        scratch_shapes=[pltpu.VMEM((k_count * rows, width), jnp.bfloat16)],
        cost_estimate=pl.CostEstimate(
            flops=flops,
            bytes_accessed=2 * (left.size // left.shape[2] * rows + sources.size + lag_rows.size)
            + 2 * slots * k_count * rows * lag_count,
            transcendentals=0,
        ),
    )(left, sources, lag_rows)


def row_counts(channel_segment, segment_row, owner):
    held_rows = owner * SEG_PER + jnp.arange(SEG_PER, dtype=jnp.int32)
    matches = segment_row[None, :] == held_rows[:, None]
    segment_ids = jnp.arange(segment_row.shape[0], dtype=jnp.int32)
    held_segments = jnp.sum(jnp.where(matches, segment_ids[None, :], 0), axis=1)
    members = channel_segment[None, :] == held_segments[:, None]
    return jnp.sum(members.astype(jnp.float32), axis=1)


def shift_perm(count, shift):
    return [(i, (i + shift) % count) for i in range(count)]


def gather_relative(value, axis, count):
    if count != 4:
        parts = [value] + [lax.ppermute(value, axis, shift_perm(count, s)) for s in range(1, count)]
        return jnp.stack(parts)
    half = value.shape[-1] // 2
    from_left = lax.ppermute(value, axis, shift_perm(count, 1))
    from_right = lax.ppermute(value, axis, shift_perm(count, -1))
    far_head = lax.ppermute(from_left[..., :half], axis, shift_perm(count, 1))
    far_tail = lax.ppermute(from_right[..., half:], axis, shift_perm(count, -1))
    far = jnp.concatenate([far_head, far_tail], axis=-1)
    return jnp.stack([value, from_left, far, from_right])


def scatter_sum(value, axis, count):
    me = lax.axis_index(axis)
    blocks = value.reshape((count, value.shape[0] // count) + value.shape[1:])

    def block(offset):
        return lax.dynamic_index_in_dim(blocks, (me + offset) % count, axis=0, keepdims=False)

    if count != 4:
        total = block(0)
        for s in range(1, count):
            total = total + lax.ppermute(block(s), axis, shift_perm(count, s))
        return total
    half = blocks.shape[-1] // 2
    right, left, far, own = block(1), block(-1), block(2), block(0)
    to_right = jnp.concatenate([right[..., half:], far[..., :half]], axis=-1)
    to_left = jnp.concatenate([left[..., :half], far[..., half:]], axis=-1)
    got_left = lax.ppermute(to_right, axis, shift_perm(count, 1))
    got_right = lax.ppermute(to_left, axis, shift_perm(count, -1))
    fwd_right = right[..., :half] + got_left[..., half:]
    fwd_left = left[..., half:] + got_right[..., half:]
    got2_left = lax.ppermute(fwd_right, axis, shift_perm(count, 1))
    got2_right = lax.ppermute(fwd_left, axis, shift_perm(count, -1))
    head = own[..., :half] + got_right[..., :half] + got2_left
    tail = own[..., half:] + got_left[..., :half] + got2_right
    return jnp.concatenate([head, tail], axis=-1)


def scatter_sum_direct(value, axis, count):
    me = lax.axis_index(axis)
    blocks = value.reshape((count, value.shape[0] // count) + value.shape[1:])
    total = lax.dynamic_index_in_dim(blocks, me, axis=0, keepdims=False)
    for s in range(1, count):
        piece = lax.dynamic_index_in_dim(blocks, (me + s) % count, axis=0, keepdims=False)
        sent = lax.ppermute(piece.astype(jnp.bfloat16), axis, shift_perm(count, s))
        total = total + sent.astype(jnp.float32)
    return total


def on_device(records, window_start, channel_segment, segment_row):
    tile_size = records.shape[0]
    block_count = records.shape[1] // NFFT
    sizes = {name: lax.axis_size(name) for name in ("x", "zl", "y", "zh", "core")}
    src_count = sizes["zh"] * sizes["core"]
    x_i, zl_i, y_i = lax.axis_index("x"), lax.axis_index("zl"), lax.axis_index("y")
    zh_i, core_i = lax.axis_index("zh"), lax.axis_index("core")
    group_index = (x_i * sizes["zl"] + zl_i) * sizes["y"] + y_i
    position = zh_i * sizes["core"] + core_i
    segment_total = segment_row.shape[0]

    blocks = records.reshape(tile_size * block_count, NFFT)
    spectrum = jnp.dot(
        blocks, dft_table(NFFT), precision=lax.Precision.HIGH, preferred_element_type=jnp.float32
    )
    white = whiten(spectrum).astype(jnp.bfloat16).reshape(tile_size, block_count, NFFT)
    start_row = jnp.zeros((1, block_count, NFFT), jnp.bfloat16).at[0, 0, 0].set(
        window_start[0].astype(jnp.bfloat16)
    )
    extended = jnp.concatenate([white, start_row], axis=0).transpose(1, 0, 2)
    gathered = gather_relative(extended, "zh", sizes["zh"])
    partner = lax.ppermute(gathered, "core", shift_perm(sizes["core"], 1))
    gathered = jnp.stack([gathered, partner]).reshape(src_count, block_count, tile_size + 1, NFFT)
    starts = gathered[:, 0, tile_size, 0].astype(jnp.int32)
    group_size = src_count * tile_size
    window_total = group_size // 4
    k_per = window_total // src_count

    slot = jnp.arange(src_count, dtype=jnp.int32)
    slot_zh = (zh_i - slot % sizes["zh"]) % sizes["zh"]
    slot_core = (core_i + slot // sizes["zh"]) % sizes["core"]
    slot_position = slot_zh * sizes["core"] + slot_core
    k_idx = position * k_per + jnp.arange(k_per, dtype=jnp.int32)
    window_idx = starts[:, None] + k_idx[None, :]
    tile_first = (slot_position * tile_size)[:, None]
    source_idx = jnp.where(window_idx < tile_first, window_idx, window_idx + tile_size)
    source_pos = source_idx // tile_size
    source_slot = ((source_pos % sizes["core"] - core_i) % sizes["core"]) * sizes["zh"] + (
        zh_i - source_pos // sizes["core"]
    ) % sizes["zh"]
    source_row = (source_slot * (tile_size + 1) + source_idx % tile_size).reshape(-1)
    sources = jnp.stack(
        [
            jnp.take(gathered[:, b].reshape(-1, NFFT), source_row, axis=0).reshape(
                src_count, k_per, NFFT
            )
            for b in range(block_count)
        ],
        axis=1,
    )
    correlation = correlate(gathered, sources, lag_table(NFFT, LAGS), tile_size)
    correlation = correlation.reshape(src_count, k_per, tile_size, LAGS)

    channel_ids = (slot_position[:, None] * tile_size + jnp.arange(tile_size, dtype=jnp.int32)[None, :]).reshape(-1)
    group_segments = jnp.take(channel_segment, group_index * group_size + channel_ids)
    seg_match = group_segments[:, None] == jnp.arange(segment_total, dtype=jnp.int32)[None, :]
    group_rows = jnp.sum(jnp.where(seg_match, segment_row[None, :], 0), axis=1)
    staged_rows = group_rows
    onehot = (
        jnp.arange(segment_total, dtype=jnp.int32)[:, None] == staged_rows[None, :]
    ).astype(jnp.bfloat16)
    onehot = onehot.reshape(segment_total, src_count, tile_size)
    partial = jnp.einsum("rqi,qkim->rkm", onehot, correlation, preferred_element_type=jnp.float32)
    owners = sizes["x"] * sizes["zl"] * sizes["y"]
    pieces = partial.astype(jnp.bfloat16).reshape((owners, partial.shape[0] // owners) + partial.shape[1:])
    arrived = lax.all_to_all(pieces, ("x", "zl", "y"), split_axis=0, concat_axis=0, tiled=True)
    summed = jnp.sum(arrived.astype(jnp.float32), axis=0)
    counts = row_counts(channel_segment, segment_row, group_index)
    return summed / jnp.sqrt(jnp.maximum(counts, 1.0))[:, None, None]


def solution(mesh):
    names = ("x", "zl", "y", "zh", "core")
    rcv_count, src_count = mesh.devices.shape
    zh_count = src_count // 2
    side = round(rcv_count ** (1 / 3))
    fine = Mesh(mesh.devices.reshape(side, side, rcv_count // side // side, zh_count, 2), names)
    rcv, src = ("x", "zl", "y"), ("zh", "core")
    in_specs = (P(rcv + src, None), P(rcv + src), P(), P())
    out_specs = P(rcv, src, None)
    return jax.shard_map(
        on_device, mesh=fine, in_specs=in_specs, out_specs=out_specs, check_vma=False
    )
```

```python
import math

import jax
import jax.numpy as jnp
from jax import lax
from jax.experimental import pallas as pl
from jax.experimental.pallas import tpu as pltpu
from jax.sharding import Mesh, PartitionSpec as P

NFFT = 1024
LAGS = 256
SEG_PER = 4


def dft_table(length):
    fine_count = 32
    coarse_count = length // fine_count
    frequency = jnp.arange(length // 2, dtype=jnp.int32)
    scale = 2.0 * math.pi / length

    def angle_table(steps, stride):
        index = (jnp.arange(steps, dtype=jnp.int32)[:, None] * stride * frequency[None, :]) % length
        angles = index.astype(jnp.float32) * scale
        return jnp.cos(angles), jnp.sin(angles)

    coarse_cos, coarse_sin = angle_table(coarse_count, fine_count)
    fine_cos, fine_sin = angle_table(fine_count, 1)
    cos_part = coarse_cos[:, None] * fine_cos[None] - coarse_sin[:, None] * fine_sin[None]
    sin_part = coarse_sin[:, None] * fine_cos[None] + coarse_cos[:, None] * fine_sin[None]
    return jnp.concatenate([cos_part, -sin_part], axis=-1).reshape(length, length)


def lag_table(length, lag_count):
    frequency = jnp.arange(length // 2, dtype=jnp.int32)
    shifts = jnp.arange(lag_count, dtype=jnp.int32) - lag_count // 2
    angles = (frequency[:, None] * shifts[None, :] % length).astype(jnp.float32) * (
        2.0 * math.pi / length
    )
    return jnp.concatenate([jnp.cos(angles), -jnp.sin(angles)], axis=0).astype(jnp.bfloat16)


def whiten(spectrum):
    half_size = spectrum.shape[-1] // 2
    powers = spectrum[..., :half_size] ** 2 + spectrum[..., half_size:] ** 2
    mean_power = jnp.mean(powers, axis=-1, keepdims=True)
    magnitude = jnp.sqrt(powers + 0.1 * mean_power + 1e-06)
    return spectrum / jnp.concatenate([magnitude, magnitude], axis=-1)


def correlate_kernel(left_ref, src_ref, lag_ref, out_ref, cross_ref):
    block_count, rows, width = left_ref.shape[1], left_ref.shape[2], left_ref.shape[3]
    k_count = src_ref.shape[2]
    half = width // 2
    for slot in range(left_ref.shape[0]):
        left = [left_ref[slot, b].astype(jnp.float32) for b in range(block_count)]
        source_rows = [src_ref[slot, b].astype(jnp.float32) for b in range(block_count)]
        for k in range(k_count):
            real_part = None
            imag_part = None
            for b in range(block_count):
                source = source_rows[b][k:k + 1, :]
                l_re, l_im = left[b][:, :half], left[b][:, half:]
                s_re, s_im = source[:, :half], source[:, half:]
                re_term = l_re * s_re + l_im * s_im
                im_term = l_re * s_im - l_im * s_re
                real_part = re_term if real_part is None else real_part + re_term
                imag_part = im_term if imag_part is None else imag_part + im_term
            cross_ref[k * rows:(k + 1) * rows, :half] = real_part.astype(jnp.bfloat16)
            cross_ref[k * rows:(k + 1) * rows, half:] = imag_part.astype(jnp.bfloat16)
        product = jnp.dot(cross_ref[...], lag_ref[...], preferred_element_type=jnp.float32)
        out_ref[slot] = (product / math.sqrt(block_count * half)).astype(out_ref.dtype)


def correlate(left, sources, lag_rows, rows):
    slots, block_count, _, width = left.shape
    k_count = sources.shape[2]
    lag_count = lag_rows.shape[1]
    flops = slots * k_count * rows * (block_count * width * 4 + 2 * width * lag_count)
    return pl.pallas_call(
        correlate_kernel,
        grid=(slots // 4,),
        in_specs=[
            pl.BlockSpec((4, block_count, rows, width), lambda q: (q, 0, 0, 0)),
            pl.BlockSpec((4, block_count, k_count, width), lambda q: (q, 0, 0, 0)),
            pl.BlockSpec((width, lag_count), lambda q: (0, 0)),
        ],
        out_specs=pl.BlockSpec((4, k_count * rows, lag_count), lambda q: (q, 0, 0)),
        out_shape=jax.ShapeDtypeStruct((slots, k_count * rows, lag_count), jnp.bfloat16),
        scratch_shapes=[pltpu.VMEM((k_count * rows, width), jnp.bfloat16)],
        cost_estimate=pl.CostEstimate(
            flops=flops,
            bytes_accessed=2 * (left.size // left.shape[2] * rows + sources.size + lag_rows.size)
            + 2 * slots * k_count * rows * lag_count,
            transcendentals=0,
        ),
    )(left, sources, lag_rows)


def row_counts(channel_segment, segment_row, owner):
    held_rows = owner * SEG_PER + jnp.arange(SEG_PER, dtype=jnp.int32)
    matches = segment_row[None, :] == held_rows[:, None]
    segment_ids = jnp.arange(segment_row.shape[0], dtype=jnp.int32)
    held_segments = jnp.sum(jnp.where(matches, segment_ids[None, :], 0), axis=1)
    members = channel_segment[None, :] == held_segments[:, None]
    return jnp.sum(members.astype(jnp.float32), axis=1)


def shift_perm(count, shift):
    return [(i, (i + shift) % count) for i in range(count)]


def gather_relative(value, axis, count):
    if count != 4:
        parts = [value] + [lax.ppermute(value, axis, shift_perm(count, s)) for s in range(1, count)]
        return jnp.stack(parts)
    half = value.shape[-1] // 2
    from_left = lax.ppermute(value, axis, shift_perm(count, 1))
    from_right = lax.ppermute(value, axis, shift_perm(count, -1))
    far_head = lax.ppermute(from_left[..., :half], axis, shift_perm(count, 1))
    far_tail = lax.ppermute(from_right[..., half:], axis, shift_perm(count, -1))
    far = jnp.concatenate([far_head, far_tail], axis=-1)
    return jnp.stack([value, from_left, far, from_right])


def scatter_sum(value, axis, count):
    me = lax.axis_index(axis)
    blocks = value.reshape((count, value.shape[0] // count) + value.shape[1:])

    def block(offset):
        return lax.dynamic_index_in_dim(blocks, (me + offset) % count, axis=0, keepdims=False)

    if count != 4:
        total = block(0)
        for s in range(1, count):
            total = total + lax.ppermute(block(s), axis, shift_perm(count, s))
        return total
    half = blocks.shape[-1] // 2
    right, left, far, own = block(1), block(-1), block(2), block(0)
    to_right = jnp.concatenate([right[..., half:], far[..., :half]], axis=-1)
    to_left = jnp.concatenate([left[..., :half], far[..., half:]], axis=-1)
    got_left = lax.ppermute(to_right, axis, shift_perm(count, 1))
    got_right = lax.ppermute(to_left, axis, shift_perm(count, -1))
    fwd_right = right[..., :half] + got_left[..., half:]
    fwd_left = left[..., half:] + got_right[..., half:]
    got2_left = lax.ppermute(fwd_right, axis, shift_perm(count, 1))
    got2_right = lax.ppermute(fwd_left, axis, shift_perm(count, -1))
    head = own[..., :half] + got_right[..., :half] + got2_left
    tail = own[..., half:] + got_left[..., :half] + got2_right
    return jnp.concatenate([head, tail], axis=-1)


def scatter_sum_direct(value, axis, count):
    me = lax.axis_index(axis)
    blocks = value.reshape((count, value.shape[0] // count) + value.shape[1:])
    total = lax.dynamic_index_in_dim(blocks, me, axis=0, keepdims=False)
    for s in range(1, count):
        piece = lax.dynamic_index_in_dim(blocks, (me + s) % count, axis=0, keepdims=False)
        sent = lax.ppermute(piece.astype(jnp.bfloat16), axis, shift_perm(count, s))
        total = total + sent.astype(jnp.float32)
    return total


def on_device(records, window_start, channel_segment, segment_row):
    tile_size = records.shape[0]
    block_count = records.shape[1] // NFFT
    sizes = {name: lax.axis_size(name) for name in ("x", "zl", "y", "zh", "core")}
    src_count = sizes["zh"] * sizes["core"]
    x_i, zl_i, y_i = lax.axis_index("x"), lax.axis_index("zl"), lax.axis_index("y")
    zh_i, core_i = lax.axis_index("zh"), lax.axis_index("core")
    group_index = (x_i * sizes["zl"] + zl_i) * sizes["y"] + y_i
    position = zh_i * sizes["core"] + core_i
    segment_total = segment_row.shape[0]

    blocks = records.reshape(tile_size, block_count, NFFT)
    spectrum = jnp.einsum(
        "cbn,nf->cbf", blocks, dft_table(NFFT), precision=lax.Precision.HIGH,
        preferred_element_type=jnp.float32,
    )
    white = whiten(spectrum).astype(jnp.bfloat16)
    start_row = jnp.zeros((1, block_count, NFFT), jnp.bfloat16).at[0, 0, 0].set(
        window_start[0].astype(jnp.bfloat16)
    )
    extended = jnp.concatenate([white, start_row], axis=0).transpose(1, 0, 2)
    gathered = gather_relative(extended, "zh", sizes["zh"])
    partner = lax.ppermute(gathered, "core", shift_perm(sizes["core"], 1))
    gathered = jnp.stack([gathered, partner]).reshape(src_count, block_count, tile_size + 1, NFFT)
    starts = gathered[:, 0, tile_size, 0].astype(jnp.int32)
    group_size = src_count * tile_size
    window_total = group_size // 4
    k_per = window_total // src_count

    slot = jnp.arange(src_count, dtype=jnp.int32)
    slot_zh = (zh_i - slot % sizes["zh"]) % sizes["zh"]
    slot_core = (core_i + slot // sizes["zh"]) % sizes["core"]
    slot_position = slot_zh * sizes["core"] + slot_core
    k_idx = position * k_per + jnp.arange(k_per, dtype=jnp.int32)
    window_idx = starts[:, None] + k_idx[None, :]
    tile_first = (slot_position * tile_size)[:, None]
    source_idx = jnp.where(window_idx < tile_first, window_idx, window_idx + tile_size)
    source_pos = source_idx // tile_size
    source_slot = ((source_pos % sizes["core"] - core_i) % sizes["core"]) * sizes["zh"] + (
        zh_i - source_pos // sizes["core"]
    ) % sizes["zh"]
    source_row = (source_slot * (tile_size + 1) + source_idx % tile_size).reshape(-1)
    sources = jnp.stack(
        [
            jnp.take(gathered[:, b].reshape(-1, NFFT), source_row, axis=0).reshape(
                src_count, k_per, NFFT
            )
            for b in range(block_count)
        ],
        axis=1,
    )
    correlation = correlate(gathered, sources, lag_table(NFFT, LAGS), tile_size)
    correlation = correlation.reshape(src_count, k_per, tile_size, LAGS)

    channel_ids = (slot_position[:, None] * tile_size + jnp.arange(tile_size, dtype=jnp.int32)[None, :]).reshape(-1)
    group_segments = jnp.take(channel_segment, group_index * group_size + channel_ids)
    seg_match = group_segments[:, None] == jnp.arange(segment_total, dtype=jnp.int32)[None, :]
    group_rows = jnp.sum(jnp.where(seg_match, segment_row[None, :], 0), axis=1)
    staged_rows = group_rows
    onehot = (
        jnp.arange(segment_total, dtype=jnp.int32)[:, None] == staged_rows[None, :]
    ).astype(jnp.bfloat16)
    onehot = onehot.reshape(segment_total, src_count, tile_size)
    partial = jnp.einsum("rqi,qkim->rkm", onehot, correlation, preferred_element_type=jnp.float32)
    owners = sizes["x"] * sizes["zl"] * sizes["y"]
    pieces = partial.astype(jnp.bfloat16).reshape((owners, partial.shape[0] // owners) + partial.shape[1:])
    arrived = lax.all_to_all(pieces, ("x", "zl", "y"), split_axis=0, concat_axis=0, tiled=True)
    summed = jnp.sum(arrived.astype(jnp.float32), axis=0)
    counts = row_counts(channel_segment, segment_row, group_index)
    return summed / jnp.sqrt(jnp.maximum(counts, 1.0))[:, None, None]


def solution(mesh):
    names = ("x", "zl", "y", "zh", "core")
    rcv_count, src_count = mesh.devices.shape
    zh_count = src_count // 2
    side = round(rcv_count ** (1 / 3))
    fine = Mesh(mesh.devices.reshape(side, side, rcv_count // side // side, zh_count, 2), names)
    rcv, src = ("x", "zl", "y"), ("zh", "core")
    in_specs = (P(rcv + src, None), P(rcv + src), P(), P())
    out_specs = P(rcv, src, None)
    return jax.shard_map(
        on_device, mesh=fine, in_specs=in_specs, out_specs=out_specs, check_vma=False
    )
```

```python
import math

import jax
import jax.numpy as jnp
from jax import lax
from jax.experimental import pallas as pl
from jax.experimental.pallas import tpu as pltpu
from jax.sharding import Mesh, PartitionSpec as P

NFFT = 1024
LAGS = 256
SEG_PER = 4


def dft_table(length):
    fine_count = 32
    coarse_count = length // fine_count
    frequency = jnp.arange(length // 2, dtype=jnp.int32)
    scale = 2.0 * math.pi / length

    def angle_table(steps, stride):
        index = (jnp.arange(steps, dtype=jnp.int32)[:, None] * stride * frequency[None, :]) % length
        angles = index.astype(jnp.float32) * scale
        return jnp.cos(angles), jnp.sin(angles)

    coarse_cos, coarse_sin = angle_table(coarse_count, fine_count)
    fine_cos, fine_sin = angle_table(fine_count, 1)
    cos_part = coarse_cos[:, None] * fine_cos[None] - coarse_sin[:, None] * fine_sin[None]
    sin_part = coarse_sin[:, None] * fine_cos[None] + coarse_cos[:, None] * fine_sin[None]
    return jnp.concatenate([cos_part, -sin_part], axis=-1).reshape(length, length)


def lag_table(length, lag_count):
    frequency = jnp.arange(length // 2, dtype=jnp.int32)
    shifts = jnp.arange(lag_count, dtype=jnp.int32) - lag_count // 2
    angles = (frequency[:, None] * shifts[None, :] % length).astype(jnp.float32) * (
        2.0 * math.pi / length
    )
    return jnp.concatenate([jnp.cos(angles), -jnp.sin(angles)], axis=0).astype(jnp.bfloat16)


def whiten(spectrum):
    half_size = spectrum.shape[-1] // 2
    powers = spectrum[..., :half_size] ** 2 + spectrum[..., half_size:] ** 2
    mean_power = jnp.mean(powers, axis=-1, keepdims=True)
    magnitude = jnp.sqrt(powers + 0.1 * mean_power + 1e-06)
    return spectrum / jnp.concatenate([magnitude, magnitude], axis=-1)


def correlate_kernel(left_ref, src_ref, lag_ref, out_ref, cross_ref):
    block_count, rows, width = left_ref.shape[1], left_ref.shape[2], left_ref.shape[3]
    k_count = src_ref.shape[2]
    half = width // 2
    for slot in range(left_ref.shape[0]):
        left = [left_ref[slot, b].astype(jnp.float32) for b in range(block_count)]
        source_rows = [src_ref[slot, b].astype(jnp.float32) for b in range(block_count)]
        for k in range(k_count):
            real_part = None
            imag_part = None
            for b in range(block_count):
                source = source_rows[b][k:k + 1, :]
                l_re, l_im = left[b][:, :half], left[b][:, half:]
                s_re, s_im = source[:, :half], source[:, half:]
                re_term = l_re * s_re + l_im * s_im
                im_term = l_re * s_im - l_im * s_re
                real_part = re_term if real_part is None else real_part + re_term
                imag_part = im_term if imag_part is None else imag_part + im_term
            cross_ref[k * rows:(k + 1) * rows, :half] = real_part.astype(jnp.bfloat16)
            cross_ref[k * rows:(k + 1) * rows, half:] = imag_part.astype(jnp.bfloat16)
        product = jnp.dot(cross_ref[...], lag_ref[...], preferred_element_type=jnp.float32)
        out_ref[slot] = (product / math.sqrt(block_count * half)).astype(out_ref.dtype)


def correlate(left, sources, lag_rows, rows):
    slots, block_count, _, width = left.shape
    k_count = sources.shape[2]
    lag_count = lag_rows.shape[1]
    flops = slots * k_count * rows * (block_count * width * 4 + 2 * width * lag_count)
    return pl.pallas_call(
        correlate_kernel,
        grid=(slots // 8,),
        in_specs=[
            pl.BlockSpec((8, block_count, rows, width), lambda q: (q, 0, 0, 0)),
            pl.BlockSpec((8, block_count, k_count, width), lambda q: (q, 0, 0, 0)),
            pl.BlockSpec((width, lag_count), lambda q: (0, 0)),
        ],
        out_specs=pl.BlockSpec((8, k_count * rows, lag_count), lambda q: (q, 0, 0)),
        out_shape=jax.ShapeDtypeStruct((slots, k_count * rows, lag_count), jnp.bfloat16),
        scratch_shapes=[pltpu.VMEM((k_count * rows, width), jnp.bfloat16)],
        cost_estimate=pl.CostEstimate(
            flops=flops,
            bytes_accessed=2 * (left.size // left.shape[2] * rows + sources.size + lag_rows.size)
            + 2 * slots * k_count * rows * lag_count,
            transcendentals=0,
        ),
    )(left, sources, lag_rows)


def row_counts(channel_segment, segment_row, owner):
    held_rows = owner * SEG_PER + jnp.arange(SEG_PER, dtype=jnp.int32)
    matches = segment_row[None, :] == held_rows[:, None]
    segment_ids = jnp.arange(segment_row.shape[0], dtype=jnp.int32)
    held_segments = jnp.sum(jnp.where(matches, segment_ids[None, :], 0), axis=1)
    members = channel_segment[None, :] == held_segments[:, None]
    return jnp.sum(members.astype(jnp.float32), axis=1)


def shift_perm(count, shift):
    return [(i, (i + shift) % count) for i in range(count)]


def gather_relative(value, axis, count):
    if count != 4:
        parts = [value] + [lax.ppermute(value, axis, shift_perm(count, s)) for s in range(1, count)]
        return jnp.stack(parts)
    half = value.shape[-1] // 2
    from_left = lax.ppermute(value, axis, shift_perm(count, 1))
    from_right = lax.ppermute(value, axis, shift_perm(count, -1))
    far_head = lax.ppermute(from_left[..., :half], axis, shift_perm(count, 1))
    far_tail = lax.ppermute(from_right[..., half:], axis, shift_perm(count, -1))
    far = jnp.concatenate([far_head, far_tail], axis=-1)
    return jnp.stack([value, from_left, far, from_right])


def scatter_sum(value, axis, count):
    me = lax.axis_index(axis)
    blocks = value.reshape((count, value.shape[0] // count) + value.shape[1:])

    def block(offset):
        return lax.dynamic_index_in_dim(blocks, (me + offset) % count, axis=0, keepdims=False)

    if count != 4:
        total = block(0)
        for s in range(1, count):
            total = total + lax.ppermute(block(s), axis, shift_perm(count, s))
        return total
    half = blocks.shape[-1] // 2
    right, left, far, own = block(1), block(-1), block(2), block(0)
    to_right = jnp.concatenate([right[..., half:], far[..., :half]], axis=-1)
    to_left = jnp.concatenate([left[..., :half], far[..., half:]], axis=-1)
    got_left = lax.ppermute(to_right, axis, shift_perm(count, 1))
    got_right = lax.ppermute(to_left, axis, shift_perm(count, -1))
    fwd_right = right[..., :half] + got_left[..., half:]
    fwd_left = left[..., half:] + got_right[..., half:]
    got2_left = lax.ppermute(fwd_right, axis, shift_perm(count, 1))
    got2_right = lax.ppermute(fwd_left, axis, shift_perm(count, -1))
    head = own[..., :half] + got_right[..., :half] + got2_left
    tail = own[..., half:] + got_left[..., :half] + got2_right
    return jnp.concatenate([head, tail], axis=-1)


def scatter_sum_direct(value, axis, count):
    me = lax.axis_index(axis)
    blocks = value.reshape((count, value.shape[0] // count) + value.shape[1:])
    total = lax.dynamic_index_in_dim(blocks, me, axis=0, keepdims=False)
    for s in range(1, count):
        piece = lax.dynamic_index_in_dim(blocks, (me + s) % count, axis=0, keepdims=False)
        sent = lax.ppermute(piece.astype(jnp.bfloat16), axis, shift_perm(count, s))
        total = total + sent.astype(jnp.float32)
    return total


def on_device(records, window_start, channel_segment, segment_row):
    tile_size = records.shape[0]
    block_count = records.shape[1] // NFFT
    sizes = {name: lax.axis_size(name) for name in ("x", "zl", "y", "zh", "core")}
    src_count = sizes["zh"] * sizes["core"]
    x_i, zl_i, y_i = lax.axis_index("x"), lax.axis_index("zl"), lax.axis_index("y")
    zh_i, core_i = lax.axis_index("zh"), lax.axis_index("core")
    group_index = (x_i * sizes["zl"] + zl_i) * sizes["y"] + y_i
    position = zh_i * sizes["core"] + core_i
    segment_total = segment_row.shape[0]

    blocks = records.reshape(tile_size * block_count, NFFT)
    spectrum = jnp.dot(
        blocks, dft_table(NFFT), precision=lax.Precision.HIGH, preferred_element_type=jnp.float32
    )
    white = whiten(spectrum).astype(jnp.bfloat16).reshape(tile_size, block_count, NFFT)
    start_row = jnp.zeros((1, block_count, NFFT), jnp.bfloat16).at[0, 0, 0].set(
        window_start[0].astype(jnp.bfloat16)
    )
    extended = jnp.concatenate([white, start_row], axis=0).transpose(1, 0, 2)
    gathered = gather_relative(extended, "zh", sizes["zh"])
    partner = lax.ppermute(gathered, "core", shift_perm(sizes["core"], 1))
    gathered = jnp.stack([gathered, partner]).reshape(src_count, block_count, tile_size + 1, NFFT)
    starts = gathered[:, 0, tile_size, 0].astype(jnp.int32)
    group_size = src_count * tile_size
    window_total = group_size // 4
    k_per = window_total // src_count

    slot = jnp.arange(src_count, dtype=jnp.int32)
    slot_zh = (zh_i - slot % sizes["zh"]) % sizes["zh"]
    slot_core = (core_i + slot // sizes["zh"]) % sizes["core"]
    slot_position = slot_zh * sizes["core"] + slot_core
    k_idx = position * k_per + jnp.arange(k_per, dtype=jnp.int32)
    window_idx = starts[:, None] + k_idx[None, :]
    tile_first = (slot_position * tile_size)[:, None]
    source_idx = jnp.where(window_idx < tile_first, window_idx, window_idx + tile_size)
    source_pos = source_idx // tile_size
    source_slot = ((source_pos % sizes["core"] - core_i) % sizes["core"]) * sizes["zh"] + (
        zh_i - source_pos // sizes["core"]
    ) % sizes["zh"]
    source_row = (source_slot * (tile_size + 1) + source_idx % tile_size).reshape(-1)
    sources = jnp.stack(
        [
            jnp.take(gathered[:, b].reshape(-1, NFFT), source_row, axis=0).reshape(
                src_count, k_per, NFFT
            )
            for b in range(block_count)
        ],
        axis=1,
    )
    correlation = correlate(gathered, sources, lag_table(NFFT, LAGS), tile_size)
    correlation = correlation.reshape(src_count, k_per, tile_size, LAGS)

    channel_ids = (slot_position[:, None] * tile_size + jnp.arange(tile_size, dtype=jnp.int32)[None, :]).reshape(-1)
    group_segments = jnp.take(channel_segment, group_index * group_size + channel_ids)
    seg_match = group_segments[:, None] == jnp.arange(segment_total, dtype=jnp.int32)[None, :]
    group_rows = jnp.sum(jnp.where(seg_match, segment_row[None, :], 0), axis=1)
    staged_rows = group_rows
    onehot = (
        jnp.arange(segment_total, dtype=jnp.int32)[:, None] == staged_rows[None, :]
    ).astype(jnp.bfloat16)
    onehot = onehot.reshape(segment_total, src_count, tile_size)
    partial = jnp.einsum("rqi,qkim->rkm", onehot, correlation, preferred_element_type=jnp.float32)
    owners = sizes["x"] * sizes["zl"] * sizes["y"]
    pieces = partial.astype(jnp.bfloat16).reshape((owners, partial.shape[0] // owners) + partial.shape[1:])
    arrived = lax.all_to_all(pieces, ("x", "zl", "y"), split_axis=0, concat_axis=0, tiled=True)
    summed = jnp.sum(arrived.astype(jnp.float32), axis=0)
    counts = row_counts(channel_segment, segment_row, group_index)
    return summed / jnp.sqrt(jnp.maximum(counts, 1.0))[:, None, None]


def solution(mesh):
    names = ("x", "zl", "y", "zh", "core")
    rcv_count, src_count = mesh.devices.shape
    zh_count = src_count // 2
    side = round(rcv_count ** (1 / 3))
    fine = Mesh(mesh.devices.reshape(side, side, rcv_count // side // side, zh_count, 2), names)
    rcv, src = ("x", "zl", "y"), ("zh", "core")
    in_specs = (P(rcv + src, None), P(rcv + src), P(), P())
    out_specs = P(rcv, src, None)
    return jax.shard_map(
        on_device, mesh=fine, in_specs=in_specs, out_specs=out_specs, check_vma=False
    )
```

```python
import math

import jax
import ml_dtypes
import numpy as np
import jax.numpy as jnp
from jax import lax
from jax.experimental import pallas as pl
from jax.experimental.pallas import tpu as pltpu
from jax.sharding import Mesh, PartitionSpec as P

NFFT = 1024
LAGS = 256
SEG_PER = 4


def dft_table(length):
    fine_count = 32
    coarse_count = length // fine_count
    frequency = jnp.arange(length // 2, dtype=jnp.int32)
    scale = 2.0 * math.pi / length

    def angle_table(steps, stride):
        index = (jnp.arange(steps, dtype=jnp.int32)[:, None] * stride * frequency[None, :]) % length
        angles = index.astype(jnp.float32) * scale
        return jnp.cos(angles), jnp.sin(angles)

    coarse_cos, coarse_sin = angle_table(coarse_count, fine_count)
    fine_cos, fine_sin = angle_table(fine_count, 1)
    cos_part = coarse_cos[:, None] * fine_cos[None] - coarse_sin[:, None] * fine_sin[None]
    sin_part = coarse_sin[:, None] * fine_cos[None] + coarse_cos[:, None] * fine_sin[None]
    return jnp.concatenate([cos_part, -sin_part], axis=-1).reshape(length, length)


def lag_table(length, lag_count):
    frequency = np.arange(length // 2, dtype=np.int64)
    shifts = np.arange(lag_count, dtype=np.int64) - lag_count // 2
    angles = (frequency[:, None] * shifts[None, :] % length).astype(np.float32) * np.float32(
        2.0 * math.pi / length
    )
    table = np.concatenate([np.cos(angles), -np.sin(angles)], axis=0).astype(ml_dtypes.bfloat16)
    return jnp.asarray(table)


def whiten(spectrum):
    half_size = spectrum.shape[-1] // 2
    powers = spectrum[..., :half_size] ** 2 + spectrum[..., half_size:] ** 2
    mean_power = jnp.mean(powers, axis=-1, keepdims=True)
    magnitude = jnp.sqrt(powers + 0.1 * mean_power + 1e-06)
    return spectrum / jnp.concatenate([magnitude, magnitude], axis=-1)


def correlate_kernel(left_ref, src_ref, lag_ref, out_ref, cross_ref):
    block_count, rows, width = left_ref.shape[1], left_ref.shape[2], left_ref.shape[3]
    k_count = src_ref.shape[2]
    half = width // 2
    for slot in range(left_ref.shape[0]):
        left = [left_ref[slot, b].astype(jnp.float32) for b in range(block_count)]
        source_rows = [src_ref[slot, b].astype(jnp.float32) for b in range(block_count)]
        for k in range(k_count):
            real_part = None
            imag_part = None
            for b in range(block_count):
                source = source_rows[b][k:k + 1, :]
                l_re, l_im = left[b][:, :half], left[b][:, half:]
                s_re, s_im = source[:, :half], source[:, half:]
                re_term = l_re * s_re + l_im * s_im
                im_term = l_re * s_im - l_im * s_re
                real_part = re_term if real_part is None else real_part + re_term
                imag_part = im_term if imag_part is None else imag_part + im_term
            cross_ref[k * rows:(k + 1) * rows, :half] = real_part.astype(jnp.bfloat16)
            cross_ref[k * rows:(k + 1) * rows, half:] = imag_part.astype(jnp.bfloat16)
        product = jnp.dot(cross_ref[...], lag_ref[...], preferred_element_type=jnp.float32)
        out_ref[slot] = (product / math.sqrt(block_count * half)).astype(out_ref.dtype)


def correlate(left, sources, lag_rows, rows):
    slots, block_count, _, width = left.shape
    k_count = sources.shape[2]
    lag_count = lag_rows.shape[1]
    flops = slots * k_count * rows * (block_count * width * 4 + 2 * width * lag_count)
    return pl.pallas_call(
        correlate_kernel,
        grid=(slots // 4,),
        in_specs=[
            pl.BlockSpec((4, block_count, rows, width), lambda q: (q, 0, 0, 0)),
            pl.BlockSpec((4, block_count, k_count, width), lambda q: (q, 0, 0, 0)),
            pl.BlockSpec((width, lag_count), lambda q: (0, 0)),
        ],
        out_specs=pl.BlockSpec((4, k_count * rows, lag_count), lambda q: (q, 0, 0)),
        out_shape=jax.ShapeDtypeStruct((slots, k_count * rows, lag_count), jnp.bfloat16),
        scratch_shapes=[pltpu.VMEM((k_count * rows, width), jnp.bfloat16)],
        cost_estimate=pl.CostEstimate(
            flops=flops,
            bytes_accessed=2 * (left.size // left.shape[2] * rows + sources.size + lag_rows.size)
            + 2 * slots * k_count * rows * lag_count,
            transcendentals=0,
        ),
    )(left, sources, lag_rows)


def row_counts(channel_segment, segment_row, owner):
    held_rows = owner * SEG_PER + jnp.arange(SEG_PER, dtype=jnp.int32)
    matches = segment_row[None, :] == held_rows[:, None]
    segment_ids = jnp.arange(segment_row.shape[0], dtype=jnp.int32)
    held_segments = jnp.sum(jnp.where(matches, segment_ids[None, :], 0), axis=1)
    members = channel_segment[None, :] == held_segments[:, None]
    return jnp.sum(members.astype(jnp.float32), axis=1)


def shift_perm(count, shift):
    return [(i, (i + shift) % count) for i in range(count)]


def gather_relative(value, axis, count):
    if count != 4:
        parts = [value] + [lax.ppermute(value, axis, shift_perm(count, s)) for s in range(1, count)]
        return jnp.stack(parts)
    half = value.shape[-1] // 2
    from_left = lax.ppermute(value, axis, shift_perm(count, 1))
    from_right = lax.ppermute(value, axis, shift_perm(count, -1))
    far_head = lax.ppermute(from_left[..., :half], axis, shift_perm(count, 1))
    far_tail = lax.ppermute(from_right[..., half:], axis, shift_perm(count, -1))
    far = jnp.concatenate([far_head, far_tail], axis=-1)
    return jnp.stack([value, from_left, far, from_right])


def scatter_sum(value, axis, count):
    me = lax.axis_index(axis)
    blocks = value.reshape((count, value.shape[0] // count) + value.shape[1:])

    def block(offset):
        return lax.dynamic_index_in_dim(blocks, (me + offset) % count, axis=0, keepdims=False)

    if count != 4:
        total = block(0)
        for s in range(1, count):
            total = total + lax.ppermute(block(s), axis, shift_perm(count, s))
        return total
    half = blocks.shape[-1] // 2
    right, left, far, own = block(1), block(-1), block(2), block(0)
    to_right = jnp.concatenate([right[..., half:], far[..., :half]], axis=-1)
    to_left = jnp.concatenate([left[..., :half], far[..., half:]], axis=-1)
    got_left = lax.ppermute(to_right, axis, shift_perm(count, 1))
    got_right = lax.ppermute(to_left, axis, shift_perm(count, -1))
    fwd_right = right[..., :half] + got_left[..., half:]
    fwd_left = left[..., half:] + got_right[..., half:]
    got2_left = lax.ppermute(fwd_right, axis, shift_perm(count, 1))
    got2_right = lax.ppermute(fwd_left, axis, shift_perm(count, -1))
    head = own[..., :half] + got_right[..., :half] + got2_left
    tail = own[..., half:] + got_left[..., :half] + got2_right
    return jnp.concatenate([head, tail], axis=-1)


def scatter_sum_direct(value, axis, count):
    me = lax.axis_index(axis)
    blocks = value.reshape((count, value.shape[0] // count) + value.shape[1:])
    total = lax.dynamic_index_in_dim(blocks, me, axis=0, keepdims=False)
    for s in range(1, count):
        piece = lax.dynamic_index_in_dim(blocks, (me + s) % count, axis=0, keepdims=False)
        sent = lax.ppermute(piece.astype(jnp.bfloat16), axis, shift_perm(count, s))
        total = total + sent.astype(jnp.float32)
    return total


def on_device(records, window_start, channel_segment, segment_row):
    tile_size = records.shape[0]
    block_count = records.shape[1] // NFFT
    sizes = {name: lax.axis_size(name) for name in ("x", "zl", "y", "zh", "core")}
    src_count = sizes["zh"] * sizes["core"]
    x_i, zl_i, y_i = lax.axis_index("x"), lax.axis_index("zl"), lax.axis_index("y")
    zh_i, core_i = lax.axis_index("zh"), lax.axis_index("core")
    group_index = (x_i * sizes["zl"] + zl_i) * sizes["y"] + y_i
    position = zh_i * sizes["core"] + core_i
    segment_total = segment_row.shape[0]

    blocks = records.reshape(tile_size * block_count, NFFT)
    spectrum = jnp.dot(
        blocks, dft_table(NFFT), precision=lax.Precision.HIGH, preferred_element_type=jnp.float32
    )
    white = whiten(spectrum).astype(jnp.bfloat16).reshape(tile_size, block_count, NFFT)
    start_row = jnp.zeros((1, block_count, NFFT), jnp.bfloat16).at[0, 0, 0].set(
        window_start[0].astype(jnp.bfloat16)
    )
    extended = jnp.concatenate([white, start_row], axis=0).transpose(1, 0, 2)
    gathered = gather_relative(extended, "zh", sizes["zh"])
    partner = lax.ppermute(gathered, "core", shift_perm(sizes["core"], 1))
    gathered = jnp.stack([gathered, partner]).reshape(src_count, block_count, tile_size + 1, NFFT)
    starts = gathered[:, 0, tile_size, 0].astype(jnp.int32)
    group_size = src_count * tile_size
    window_total = group_size // 4
    k_per = window_total // src_count

    slot = jnp.arange(src_count, dtype=jnp.int32)
    slot_zh = (zh_i - slot % sizes["zh"]) % sizes["zh"]
    slot_core = (core_i + slot // sizes["zh"]) % sizes["core"]
    slot_position = slot_zh * sizes["core"] + slot_core
    k_idx = position * k_per + jnp.arange(k_per, dtype=jnp.int32)
    window_idx = starts[:, None] + k_idx[None, :]
    tile_first = (slot_position * tile_size)[:, None]
    source_idx = jnp.where(window_idx < tile_first, window_idx, window_idx + tile_size)
    source_pos = source_idx // tile_size
    source_slot = ((source_pos % sizes["core"] - core_i) % sizes["core"]) * sizes["zh"] + (
        zh_i - source_pos // sizes["core"]
    ) % sizes["zh"]
    source_row = (source_slot * (tile_size + 1) + source_idx % tile_size).reshape(-1)
    sources = jnp.stack(
        [
            jnp.take(gathered[:, b].reshape(-1, NFFT), source_row, axis=0).reshape(
                src_count, k_per, NFFT
            )
            for b in range(block_count)
        ],
        axis=1,
    )
    correlation = correlate(gathered, sources, lag_table(NFFT, LAGS), tile_size)
    correlation = correlation.reshape(src_count, k_per, tile_size, LAGS)

    channel_ids = (slot_position[:, None] * tile_size + jnp.arange(tile_size, dtype=jnp.int32)[None, :]).reshape(-1)
    group_segments = jnp.take(channel_segment, group_index * group_size + channel_ids)
    seg_match = group_segments[:, None] == jnp.arange(segment_total, dtype=jnp.int32)[None, :]
    group_rows = jnp.sum(jnp.where(seg_match, segment_row[None, :], 0), axis=1)
    staged_rows = group_rows
    onehot = (
        jnp.arange(segment_total, dtype=jnp.int32)[:, None] == staged_rows[None, :]
    ).astype(jnp.bfloat16)
    onehot = onehot.reshape(segment_total, src_count, tile_size)
    partial = jnp.einsum("rqi,qkim->rkm", onehot, correlation, preferred_element_type=jnp.float32)
    owners = sizes["x"] * sizes["zl"] * sizes["y"]
    pieces = partial.astype(jnp.bfloat16).reshape((owners, partial.shape[0] // owners) + partial.shape[1:])
    arrived = lax.all_to_all(pieces, ("x", "zl", "y"), split_axis=0, concat_axis=0, tiled=True)
    summed = jnp.sum(arrived.astype(jnp.float32), axis=0)
    counts = row_counts(channel_segment, segment_row, group_index)
    return summed / jnp.sqrt(jnp.maximum(counts, 1.0))[:, None, None]


def solution(mesh):
    names = ("x", "zl", "y", "zh", "core")
    rcv_count, src_count = mesh.devices.shape
    zh_count = src_count // 2
    side = round(rcv_count ** (1 / 3))
    fine = Mesh(mesh.devices.reshape(side, side, rcv_count // side // side, zh_count, 2), names)
    rcv, src = ("x", "zl", "y"), ("zh", "core")
    in_specs = (P(rcv + src, None), P(rcv + src), P(), P())
    out_specs = P(rcv, src, None)
    return jax.shard_map(
        on_device, mesh=fine, in_specs=in_specs, out_specs=out_specs, check_vma=False
    )
```
